32 devices in a mesh: req: 2 (over x), tile: 16 (over z, y, core).
Axes of the slice: x: 2, y: 2, z: 4, core: 2. Of those that a mesh axis runs over, the one named last changes fastest.
Arguments:
- queries: bfloat16 [32, 512, 384], P(('req', 'tile')), parts along dimension 0, may hold values from -12 to 12
- keys: bfloat16 [32, 512, 384], P(('req', 'tile')), parts along dimension 0, may hold values from -5 to 5
- values: bfloat16 [32, 512, 384], P(('req', 'tile')), parts along dimension 0, may hold values from -6 to 6
- text_keys: bfloat16 [512, 1536], P(('req', 'tile')), parts along dimension 0, may hold values from -6 to 6
- text_values: bfloat16 [512, 1536], P(('req', 'tile')), parts along dimension 0, may hold values from -6 to 6
- text_mask: int32 [512], P(('req', 'tile')), parts along dimension 0, may hold values 0 or 1
Outputs:
- attended: bfloat16 [32, 512, 384], P(('req', 'tile')), parts along dimension 0
The draws below stay inside these ranges and needn't reach their ends.
There are 2 independent parts, one for each index of `req`. The reference program is written for one: setup_inputs(seed, part) draws one part's arguments, and reference() takes and returns one part's arrays. A program takes and returns all parts, laid end to end along the dimension named above; each array names one. Nothing has to cross between parts.
All inputs are finite; a program needn't handle non-finite values. No bound on the sum of `text_mask` on one device may be relied on, other than what follows from the above.
Results may differ from the reference program's by a relative error of at most 0.004.
Values may be sent and summed in bfloat16 or wider, within the bound.
No kernel may reach another device: no remote copies, remote signals or barrier semaphores. Data moves between devices by JAX's collectives and lax.ppermute only.
A program may use at most 192 MiB of HBM per device.

```python
import math
import jax
import jax.numpy as jnp
from jax import lax

TS = 8
HEADS = 12
HEAD_DIM = 128
HEAD_GROUPS = 4
TEXT = 256
TT = 512
HEADS_DEV = 3
WIDTH_DEV = 384
TILES = 4
GW = 4
GH = 1
GF = 1
VALID_FRAMES = 6


def draw_queries(key, part):
    full_shape = (TILES * HEAD_GROUPS, TT, HEADS_DEV * HEAD_DIM)
    base_key = jax.random.fold_in(key, 3)
    drawn = jnp.clip(2.8 * jax.random.normal(base_key, full_shape, jnp.float32), -12.0, 12.0)
    return drawn.astype(jnp.bfloat16)


def draw_keys(key, part):
    full_shape = (TILES * HEAD_GROUPS, TT, HEADS_DEV * HEAD_DIM)
    base_key = jax.random.fold_in(key, 5)
    drawn = jnp.clip(jax.random.normal(base_key, full_shape, jnp.float32), -5.0, 5.0)
    return drawn.astype(jnp.bfloat16)


def set_ends(values, key, least, largest):
    shape = values.shape
    index_at = [jax.random.randint(jax.random.fold_in(key, axis), (), 0, shape[axis]) for axis in range(len(shape))]
    values = values.at[tuple(index_at)].set(least)
    longest = shape.index(max(shape))
    index_at[longest] = (index_at[longest] + 1) % shape[longest]
    return values.at[tuple(index_at)].set(largest)


def block_scale(rng, dims, split, low, top_value):
    factor_of = 1.0
    for dim, blocks in split:
        draws = jax.random.uniform(jax.random.fold_in(jax.random.fold_in(rng, 6), dim), (blocks,), jnp.float32, low / len(split), top_value / len(split))
        factor_of = factor_of * jnp.repeat(jnp.exp(draws), dims[dim] // blocks).reshape((-1,) + (1,) * (len(dims) - 1 - dim))
    return factor_of


def bell_draw(key, shape, deviation, bound, pieces=(), kind=jnp.bfloat16):
    entries = jax.random.normal(key, shape, jnp.float32) * deviation
    if len(pieces) > 0:
        entries = block_scale(key, shape, pieces, -0.22, 0.18) * entries
    return jnp.clip(entries, min=-bound, max=bound).astype(kind)


def setup_inputs(seed: int = 0, part: int = 0) -> dict:
    splits = jax.random.split(jax.random.key(seed), 7)
    part_splits = jax.random.split(jax.random.fold_in(splits[6], part), 7)
    return {
        "queries": draw_queries(jax.random.fold_in(jax.random.fold_in(splits[6], part), 71), part),
        "keys": draw_keys(jax.random.fold_in(jax.random.fold_in(splits[6], part), 71), part),
        "values": bell_draw(part_splits[2], (TILES * HEAD_GROUPS, TT, WIDTH_DEV), 1.0, 6.0, ((0, 16),)),
        "text_keys": bell_draw(part_splits[3], (TEXT, HEADS * HEAD_DIM), 1.0, 6.0, ((0, 16),)),
        "text_values": bell_draw(part_splits[4], (TEXT, HEADS * HEAD_DIM), 1.0, 6.0, ((0, 16),)),
        "text_mask": set_ends((jax.random.randint(part_splits[5], (TEXT,), 0, 4) < 3).astype(jnp.int32), jax.random.fold_in(part_splits[5], 1), 0, 1),
    }


MASKED = -1e+30

def reference(queries, keys, values, text_keys, text_values, text_mask):
    lane_width = HEADS_DEV * HEAD_DIM
    score_scale = 1.0 / math.sqrt(HEAD_DIM)
    grid_keys = keys.reshape(GF, GH, GW, HEAD_GROUPS, TT, lane_width)
    grid_values = values.reshape(GF, GH, GW, HEAD_GROUPS, TT, lane_width)
    pad_spec = ((1, 1), (1, 1), (1, 1), (0, 0), (0, 0), (0, 0))
    padded_keys = jnp.pad(grid_keys, pad_spec)
    padded_values = jnp.pad(grid_values, pad_spec)
    frame_local = jnp.arange(TT, dtype=jnp.int32) // (TS * TS)
    text_keep = text_mask > 0

    def one_block(block_id):
        tile_id = block_id // HEAD_GROUPS
        head_group = block_id % HEAD_GROUPS
        w_pos = tile_id % GW
        h_pos = tile_id // GW % GH
        f_pos = tile_id // (GW * GH)
        zero_index = jnp.zeros((), jnp.int32)
        corner = (f_pos.astype(jnp.int32), h_pos.astype(jnp.int32), w_pos.astype(jnp.int32), head_group.astype(jnp.int32), zero_index, zero_index)
        near_keys = lax.dynamic_slice(padded_keys, corner, (3, 3, 3, 1, TT, lane_width)).reshape(27 * TT, lane_width)
        near_values = lax.dynamic_slice(padded_values, corner, (3, 3, 3, 1, TT, lane_width)).reshape(27 * TT, lane_width)
        offsets = jnp.arange(3, dtype=jnp.int32) - 1
        f_near = f_pos + offsets
        h_near = h_pos + offsets
        w_near = w_pos + offsets
        f_inside = (f_near >= 0) & (f_near < GF)
        h_inside = (h_near >= 0) & (h_near < GH)
        w_inside = (w_near >= 0) & (w_near < GW)
        frame_ok = f_near[:, None] * TS + frame_local[None, :] < VALID_FRAMES
        key_keep = f_inside[:, None, None, None] & h_inside[None, :, None, None] & w_inside[None, None, :, None] & frame_ok[:, None, None, :]
        key_keep = jnp.concatenate([key_keep.reshape(-1), text_keep], axis=0)
        text_cols = lax.dynamic_slice_in_dim(text_keys, (head_group * lane_width).astype(jnp.int32), lane_width, 1)
        text_vals = lax.dynamic_slice_in_dim(text_values, (head_group * lane_width).astype(jnp.int32), lane_width, 1)
        all_keys = jnp.concatenate([near_keys, text_cols], axis=0).astype(jnp.float32).reshape(-1, HEADS_DEV, HEAD_DIM)
        all_values = jnp.concatenate([near_values, text_vals], axis=0).astype(jnp.float32).reshape(-1, HEADS_DEV, HEAD_DIM)
        query_rows = queries[block_id].astype(jnp.float32).reshape(TT, HEADS_DEV, HEAD_DIM)
        scores = jnp.einsum('qhd,khd->hqk', query_rows, all_keys) * score_scale
        scores = jnp.where(key_keep[None, None, :], scores, MASKED)
        row_top = lax.optimization_barrier(jnp.max(scores, axis=-1, keepdims=True))
        exp_terms = jnp.where(key_keep[None, None, :], jnp.exp(scores - row_top), 0.0)
        row_total = lax.optimization_barrier(jnp.sum(exp_terms, axis=-1))
        rounded = lax.optimization_barrier(exp_terms.astype(jnp.bfloat16))
        weights = rounded.astype(jnp.float32)
        summed = jnp.einsum('hqk,khd->qhd', weights, all_values)
        result = summed / jnp.transpose(row_total)[:, :, None]
        return result.reshape(TT, lane_width).astype(jnp.bfloat16)
    return lax.map(one_block, jnp.arange(TILES * HEAD_GROUPS, dtype=jnp.int32))
```

```python
import math

import jax
import jax.numpy as jnp
from jax import lax
from jax.sharding import PartitionSpec as P

TS = 8
HEAD_DIM = 128
HEAD_GROUPS = 4


MASKED = -1e30


def passed_along(value, axis, steps):
    count = lax.axis_size(axis)
    first, last = (max(0, -steps), min(count, count - steps))
    return lax.ppermute(value, axis, [(source, source + steps) for source in range(first, last)])


def shortened(value):
    return jax.tree.map(lambda a: a.astype(jnp.bfloat16) if a.dtype == jnp.float32 else a, value)


def fold_block(running, query_heads, key_block, value_block, key_keep):
    row_top, row_total, summed = running
    head_count = query_heads.shape[1]
    key_heads = key_block.reshape(key_block.shape[0], head_count, HEAD_DIM)
    value_heads = value_block.reshape(value_block.shape[0], head_count, HEAD_DIM)
    scores = jnp.einsum("qhd,khd->hqk", query_heads, key_heads, preferred_element_type=jnp.float32)
    scores = scores * (1.0 / math.sqrt(HEAD_DIM))
    scores = jnp.where(key_keep[None, None, :], scores, MASKED)
    new_top = jnp.maximum(row_top, jnp.max(scores, axis=-1))
    scale_down = jnp.exp(row_top - new_top)
    exp_terms = jnp.where(key_keep[None, None, :], jnp.exp(scores - new_top[:, :, None]), 0.0)
    row_total = row_total * scale_down + jnp.sum(exp_terms, axis=-1)
    weights = exp_terms.astype(jnp.bfloat16)
    summed = summed * scale_down[:, :, None] + jnp.einsum(
        "hqk,khd->hqd", weights, value_heads, preferred_element_type=jnp.float32
    )
    return (new_top, row_total, summed)


def text_pieces(text_keys, text_values, text_mask, group_count, lane_width):
    count = lax.axis_size("tile")
    rows = text_keys.shape[0]
    flags = jnp.broadcast_to(text_mask.astype(jnp.bfloat16)[:, None], (rows, 128))
    per_group = jnp.stack(
        [
            jnp.concatenate(
                [
                    text_keys[:, g * lane_width : (g + 1) * lane_width],
                    text_values[:, g * lane_width : (g + 1) * lane_width],
                    flags,
                ],
                axis=1,
            )
            for g in range(group_count)
        ]
    )
    outgoing = jnp.tile(per_group, (count // group_count, 1, 1)).reshape(count * rows, 2 * lane_width + 128)
    got = lax.all_to_all(outgoing, "tile", 0, 0, tiled=True)
    return got[:, :lane_width], got[:, lane_width : 2 * lane_width], got[:, 2 * lane_width] > 0.5


def shards(queries, keys, values, text_keys, text_values, text_mask):
    tokens = queries.shape[1]
    lane_width = queries.shape[2]
    head_count = lane_width // HEAD_DIM
    query_heads = queries[0].reshape(tokens, head_count, HEAD_DIM)
    group_count = HEAD_GROUPS
    tiles_all = lax.axis_size("tile") // group_count
    grid_w = min(4, tiles_all)
    grid_h = min(4, tiles_all // grid_w)
    grid_f = tiles_all // (grid_w * grid_h)
    frames_valid = grid_f * TS - TS // 4
    my_index = lax.axis_index("tile")
    tile_id = my_index // group_count
    head_group = my_index % group_count
    w_pos = tile_id % grid_w
    h_pos = tile_id // grid_w % grid_h
    f_pos = tile_id // (grid_w * grid_h)
    key_rows = tokens
    if grid_f == 1:
        key_rows = min(tokens, frames_valid * TS * TS)
    own_pair = jnp.stack([keys[0, :key_rows], values[0, :key_rows]])
    local_frame = jnp.arange(key_rows, dtype=jnp.int32) // (TS * TS)

    def keep_mask(off_frame, off_height, off_width):
        inside = (
            (f_pos + off_frame >= 0)
            & (f_pos + off_frame < grid_f)
            & (h_pos + off_height >= 0)
            & (h_pos + off_height < grid_h)
            & (w_pos + off_width >= 0)
            & (w_pos + off_width < grid_w)
        )
        return inside & ((f_pos + off_frame) * TS + local_frame < frames_valid)

    running = (
        jnp.full((head_count, tokens), MASKED, jnp.float32),
        jnp.zeros((head_count, tokens), jnp.float32),
        jnp.zeros((head_count, tokens, HEAD_DIM), jnp.float32),
    )
    piece_keys, piece_values, text_keep = text_pieces(text_keys, text_values, text_mask, group_count, lane_width)
    running = fold_block(running, query_heads, piece_keys, piece_values, text_keep)
    running = fold_block(running, query_heads, own_pair[0], own_pair[1], keep_mask(0, 0, 0))
    width_set = {0: own_pair}
    for off_width in (-1, 1):
        width_set[off_width] = passed_along(own_pair, "tile", -off_width * group_count)
    width_offsets = sorted(width_set)
    row_stack = jnp.stack([width_set[spot] for spot in width_offsets])
    height_set = {0: row_stack}
    if grid_h > 1:
        for off_height in (-1, 1):
            height_set[off_height] = passed_along(
                shortened(row_stack), "tile", -off_height * grid_w * group_count
            ).astype(row_stack.dtype)
    height_offsets = sorted(height_set)
    slab_stack = jnp.stack([height_set[spot] for spot in height_offsets])

    def fold_slab(state_now, slab_pairs, off_frame):
        for h_slot, off_height in enumerate(height_offsets):
            for w_slot, off_width in enumerate(width_offsets):
                if off_frame == 0 and off_height == 0 and (off_width == 0):
                    continue
                state_now = fold_block(
                    state_now,
                    query_heads,
                    slab_pairs[h_slot, w_slot, 0],
                    slab_pairs[h_slot, w_slot, 1],
                    keep_mask(off_frame, off_height, off_width),
                )
        return state_now

    running = fold_slab(running, slab_stack, 0)
    if grid_f > 1:
        for off_frame in (-1, 1):
            got_slab = passed_along(
                shortened(slab_stack), "tile", -off_frame * grid_h * grid_w * group_count
            ).astype(slab_stack.dtype)
            running = fold_slab(running, got_slab, off_frame)
    row_top, row_total, summed = running
    result = summed / row_total[:, :, None]
    result = jnp.transpose(result, (1, 0, 2)).reshape(tokens, lane_width)
    return result.astype(jnp.bfloat16)[None]


def solution(mesh):
    return jax.shard_map(
        shards,
        mesh=mesh,
        in_specs=(
            P(("req", "tile"), None, None),
            P(("req", "tile"), None, None),
            P(("req", "tile"), None, None),
            P(("req", "tile"), None),
            P(("req", "tile"), None),
            P(("req", "tile")),
        ),
        out_specs=P(("req", "tile"), None, None),
        check_vma=False,
    )
```

```python
import functools
import math

import jax
import jax.numpy as jnp
from jax import lax
from jax.experimental import pallas as pl
from jax.experimental.pallas import tpu as pltpu
from jax.sharding import PartitionSpec as P

TS = 8
HEAD_DIM = 128
HEAD_GROUPS = 4


MASKED = -1e30


def passed_along(value, axis, steps):
    count = lax.axis_size(axis)
    first, last = (max(0, -steps), min(count, count - steps))
    return lax.ppermute(value, axis, [(source, source + steps) for source in range(first, last)])


def shortened(value):
    return jax.tree.map(lambda a: a.astype(jnp.bfloat16) if a.dtype == jnp.float32 else a, value)


def fold_block(running, query_heads, key_block, value_block, key_keep):
    row_top, row_total, summed = running
    head_count = query_heads.shape[1]
    key_heads = key_block.reshape(key_block.shape[0], head_count, HEAD_DIM)
    value_heads = value_block.reshape(value_block.shape[0], head_count, HEAD_DIM)
    scores = jnp.einsum("qhd,khd->hqk", query_heads, key_heads, preferred_element_type=jnp.float32)
    scores = scores * (1.0 / math.sqrt(HEAD_DIM))
    scores = jnp.where(key_keep[None, None, :], scores, MASKED)
    new_top = jnp.maximum(row_top, jnp.max(scores, axis=-1))
    scale_down = jnp.exp(row_top - new_top)
    exp_terms = jnp.where(key_keep[None, None, :], jnp.exp(scores - new_top[:, :, None]), 0.0)
    row_total = row_total * scale_down + jnp.sum(exp_terms, axis=-1)
    weights = exp_terms.astype(jnp.bfloat16)
    summed = summed * scale_down[:, :, None] + jnp.einsum(
        "hqk,khd->hqd", weights, value_heads, preferred_element_type=jnp.float32
    )
    return (new_top, row_total, summed)


def window_kernel(block_count, q_ref, *refs):
    key_refs = refs[:block_count]
    value_refs = refs[block_count : 2 * block_count]
    keep_refs = refs[2 * block_count : 3 * block_count]
    out_ref = refs[3 * block_count]
    query = q_ref[...]
    scores = []
    for b in range(block_count):
        s = lax.dot_general(
            query, key_refs[b][...], (((1,), (1,)), ((), ())), preferred_element_type=jnp.float32
        )
        s = s * (1.0 / math.sqrt(HEAD_DIM))
        scores.append(jnp.where(keep_refs[b][...] > 0.5, s, MASKED))
    top = scores[0].max(axis=1, keepdims=True)
    for s in scores[1:]:
        top = jnp.maximum(top, s.max(axis=1, keepdims=True))
    total = jnp.zeros_like(top)
    summed = jnp.zeros(out_ref.shape, jnp.float32)
    for b in range(block_count):
        terms = jnp.where(keep_refs[b][...] > 0.5, jnp.exp(scores[b] - top), 0.0)
        total = total + terms.sum(axis=1, keepdims=True)
        summed = summed + jnp.dot(
            terms.astype(jnp.bfloat16), value_refs[b][...], preferred_element_type=jnp.float32
        )
    out_ref[...] = (summed / total).astype(out_ref.dtype)


def window_attention(query_rows, blocks):
    tokens, lane_width = query_rows.shape
    head_count = lane_width // HEAD_DIM
    q_chunk = 256 if tokens % 256 == 0 else tokens
    chunks = tokens // q_chunk
    key_specs, value_specs, keep_specs, key_args, value_args, keep_args = [], [], [], [], [], []
    key_total = 0
    for source, key_at, value_at, keep in blocks:
        rows = keep.shape[1]
        key_total += rows
        if source.ndim == 3:
            key_specs.append(pl.BlockSpec((pl.Squeezed(), rows, HEAD_DIM), lambda h, i, s=key_at: (s, 0, h)))
            value_specs.append(pl.BlockSpec((pl.Squeezed(), rows, HEAD_DIM), lambda h, i, s=value_at: (s, 0, h)))
        else:
            key_specs.append(pl.BlockSpec((rows, HEAD_DIM), lambda h, i, s=key_at: (0, s + h)))
            value_specs.append(pl.BlockSpec((rows, HEAD_DIM), lambda h, i, s=value_at: (0, s + h)))
        keep_specs.append(pl.BlockSpec((1, rows), lambda h, i: (0, 0)))
        key_args.append(source)
        value_args.append(source)
        keep_args.append(keep)
    flops = 4 * tokens * key_total * lane_width
    moved = 2 * (2 * tokens * lane_width + 2 * key_total * lane_width)
    return pl.pallas_call(
        functools.partial(window_kernel, len(blocks)),
        out_shape=jax.ShapeDtypeStruct((tokens, lane_width), jnp.bfloat16),
        grid=(head_count, chunks),
        in_specs=[pl.BlockSpec((q_chunk, HEAD_DIM), lambda h, i: (i, h))] + key_specs + value_specs + keep_specs,
        out_specs=pl.BlockSpec((q_chunk, HEAD_DIM), lambda h, i: (i, h)),
        cost_estimate=pl.CostEstimate(
            flops=flops, transcendentals=tokens * key_total * head_count, bytes_accessed=moved
        ),
    )(query_rows, *key_args, *value_args, *keep_args)


def text_pieces(text_keys, text_values, text_mask, group_count, lane_width):
    count = lax.axis_size("tile")
    rows = text_keys.shape[0]
    flags = jnp.broadcast_to(text_mask.astype(jnp.bfloat16)[:, None], (rows, 128))
    per_group = jnp.stack(
        [
            jnp.concatenate(
                [
                    text_keys[:, g * lane_width : (g + 1) * lane_width],
                    text_values[:, g * lane_width : (g + 1) * lane_width],
                    flags,
                ],
                axis=1,
            )
            for g in range(group_count)
        ]
    )
    outgoing = jnp.tile(per_group, (count // group_count, 1, 1)).reshape(count * rows, 2 * lane_width + 128)
    got = lax.all_to_all(outgoing, "tile", 0, 0, tiled=True)
    return got, got[:, 2 * lane_width] > 0.5


def shards(queries, keys, values, text_keys, text_values, text_mask):
    tokens = queries.shape[1]
    lane_width = queries.shape[2]
    head_count = lane_width // HEAD_DIM
    query_heads = queries[0].reshape(tokens, head_count, HEAD_DIM)
    group_count = HEAD_GROUPS
    tiles_all = lax.axis_size("tile") // group_count
    grid_w = min(4, tiles_all)
    grid_h = min(4, tiles_all // grid_w)
    grid_f = tiles_all // (grid_w * grid_h)
    frames_valid = grid_f * TS - TS // 4
    my_index = lax.axis_index("tile")
    tile_id = my_index // group_count
    head_group = my_index % group_count
    w_pos = tile_id % grid_w
    h_pos = tile_id // grid_w % grid_h
    f_pos = tile_id // (grid_w * grid_h)
    key_rows = tokens
    if grid_f == 1:
        key_rows = min(tokens, frames_valid * TS * TS)
    own_pair = jnp.stack([keys[0, :key_rows], values[0, :key_rows]])
    local_frame = jnp.arange(key_rows, dtype=jnp.int32) // (TS * TS)

    def keep_mask(off_frame, off_height, off_width):
        inside = (
            (f_pos + off_frame >= 0)
            & (f_pos + off_frame < grid_f)
            & (h_pos + off_height >= 0)
            & (h_pos + off_height < grid_h)
            & (w_pos + off_width >= 0)
            & (w_pos + off_width < grid_w)
        )
        return inside & ((f_pos + off_frame) * TS + local_frame < frames_valid)

    running = (
        jnp.full((head_count, tokens), MASKED, jnp.float32),
        jnp.zeros((head_count, tokens), jnp.float32),
        jnp.zeros((head_count, tokens, HEAD_DIM), jnp.float32),
    )
    text_got, text_keep = text_pieces(text_keys, text_values, text_mask, group_count, lane_width)
    width_set = {0: own_pair}
    for off_width in (-1, 1):
        width_set[off_width] = passed_along(own_pair, "tile", -off_width * group_count)
    if grid_h == 1 and grid_f == 1:
        as_row = lambda keep: keep.astype(jnp.float32)[None, :]
        blocks = [(text_got, 0, head_count, as_row(text_keep))]
        for off_width in (-1, 0, 1):
            blocks.append((width_set[off_width], 0, 1, as_row(keep_mask(0, 0, off_width))))
        return window_attention(queries[0], blocks)[None]
    piece_keys = text_got[:, :lane_width]
    piece_values = text_got[:, lane_width : 2 * lane_width]
    running = fold_block(running, query_heads, piece_keys, piece_values, text_keep)
    running = fold_block(running, query_heads, own_pair[0], own_pair[1], keep_mask(0, 0, 0))
    width_offsets = sorted(width_set)
    row_stack = jnp.stack([width_set[spot] for spot in width_offsets])
    height_set = {0: row_stack}
    if grid_h > 1:
        for off_height in (-1, 1):
            height_set[off_height] = passed_along(
                shortened(row_stack), "tile", -off_height * grid_w * group_count
            ).astype(row_stack.dtype)
    height_offsets = sorted(height_set)
    slab_stack = jnp.stack([height_set[spot] for spot in height_offsets])

    def fold_slab(state_now, slab_pairs, off_frame):
        for h_slot, off_height in enumerate(height_offsets):
            for w_slot, off_width in enumerate(width_offsets):
                if off_frame == 0 and off_height == 0 and (off_width == 0):
                    continue
                state_now = fold_block(
                    state_now,
                    query_heads,
                    slab_pairs[h_slot, w_slot, 0],
                    slab_pairs[h_slot, w_slot, 1],
                    keep_mask(off_frame, off_height, off_width),
                )
        return state_now

    running = fold_slab(running, slab_stack, 0)
    if grid_f > 1:
        for off_frame in (-1, 1):
            got_slab = passed_along(
                shortened(slab_stack), "tile", -off_frame * grid_h * grid_w * group_count
            ).astype(slab_stack.dtype)
            running = fold_slab(running, got_slab, off_frame)
    row_top, row_total, summed = running
    result = summed / row_total[:, :, None]
    result = jnp.transpose(result, (1, 0, 2)).reshape(tokens, lane_width)
    return result.astype(jnp.bfloat16)[None]


def solution(mesh):
    return jax.shard_map(
        shards,
        mesh=mesh,
        in_specs=(
            P(("req", "tile"), None, None),
            P(("req", "tile"), None, None),
            P(("req", "tile"), None, None),
            P(("req", "tile"), None),
            P(("req", "tile"), None),
            P(("req", "tile")),
        ),
        out_specs=P(("req", "tile"), None, None),
        check_vma=False,
    )
```

```python
import functools
import math

import jax
import jax.numpy as jnp
from jax import lax
from jax.experimental import pallas as pl
from jax.experimental.pallas import tpu as pltpu
from jax.sharding import PartitionSpec as P

TS = 8
HEAD_DIM = 128
HEAD_GROUPS = 4


MASKED = -1e30


def passed_along(value, axis, steps):
    count = lax.axis_size(axis)
    first, last = (max(0, -steps), min(count, count - steps))
    return lax.ppermute(value, axis, [(source, source + steps) for source in range(first, last)])


def shortened(value):
    return jax.tree.map(lambda a: a.astype(jnp.bfloat16) if a.dtype == jnp.float32 else a, value)


def fold_block(running, query_heads, key_block, value_block, key_keep):
    row_top, row_total, summed = running
    head_count = query_heads.shape[1]
    key_heads = key_block.reshape(key_block.shape[0], head_count, HEAD_DIM)
    value_heads = value_block.reshape(value_block.shape[0], head_count, HEAD_DIM)
    scores = jnp.einsum("qhd,khd->hqk", query_heads, key_heads, preferred_element_type=jnp.float32)
    scores = scores * (1.0 / math.sqrt(HEAD_DIM))
    scores = jnp.where(key_keep[None, None, :], scores, MASKED)
    new_top = jnp.maximum(row_top, jnp.max(scores, axis=-1))
    scale_down = jnp.exp(row_top - new_top)
    exp_terms = jnp.where(key_keep[None, None, :], jnp.exp(scores - new_top[:, :, None]), 0.0)
    row_total = row_total * scale_down + jnp.sum(exp_terms, axis=-1)
    weights = exp_terms.astype(jnp.bfloat16)
    summed = summed * scale_down[:, :, None] + jnp.einsum(
        "hqk,khd->hqd", weights, value_heads, preferred_element_type=jnp.float32
    )
    return (new_top, row_total, summed)


def window_kernel(block_count, carry_in, finish, q_ref, *refs):
    key_refs = refs[:block_count]
    value_refs = refs[block_count : 2 * block_count]
    keep_refs = refs[2 * block_count : 3 * block_count]
    rest = refs[3 * block_count :]
    query = q_ref[...]
    scores = []
    for b in range(block_count):
        s = lax.dot_general(
            query, key_refs[b][...], (((1,), (1,)), ((), ())), preferred_element_type=jnp.float32
        )
        s = s * (1.0 / math.sqrt(HEAD_DIM))
        scores.append(jnp.where(keep_refs[b][...] > 0.5, s, MASKED))
    top = scores[0].max(axis=1, keepdims=True)
    for s in scores[1:]:
        top = jnp.maximum(top, s.max(axis=1, keepdims=True))
    if carry_in:
        top_in, total_in, summed_in = rest[0][...], rest[1][...], rest[2][...]
        rest = rest[3:]
        top = jnp.maximum(top, top_in)
        scale_down = jnp.exp(top_in - top)
        total = total_in * scale_down
        summed = summed_in * scale_down
    else:
        total = jnp.zeros_like(top)
        summed = None
    for b in range(block_count):
        terms = jnp.exp(scores[b] - top)
        total = total + terms.sum(axis=1, keepdims=True)
        part = jnp.dot(terms.astype(jnp.bfloat16), value_refs[b][...], preferred_element_type=jnp.float32)
        summed = part if summed is None else summed + part
    if finish:
        rest[0][...] = (summed / total).astype(rest[0].dtype)
    else:
        rest[0][...] = top
        rest[1][...] = total
        rest[2][...] = summed


def window_attention(query_rows, blocks, carry=None, finish=True):
    tokens, lane_width = query_rows.shape
    head_count = lane_width // HEAD_DIM
    q_chunk = 256 if tokens % 256 == 0 else tokens
    chunks = tokens // q_chunk
    key_specs, value_specs, keep_specs, key_args, value_args, keep_args = [], [], [], [], [], []
    key_total = 0
    for source, key_at, value_at, keep in blocks:
        rows = keep.shape[1]
        key_total += rows
        if source.ndim == 3:
            key_specs.append(pl.BlockSpec((pl.Squeezed(), rows, HEAD_DIM), lambda h, i, s=key_at: (s, 0, h)))
            value_specs.append(pl.BlockSpec((pl.Squeezed(), rows, HEAD_DIM), lambda h, i, s=value_at: (s, 0, h)))
        else:
            key_specs.append(pl.BlockSpec((rows, HEAD_DIM), lambda h, i, s=key_at: (0, s + h)))
            value_specs.append(pl.BlockSpec((rows, HEAD_DIM), lambda h, i, s=value_at: (0, s + h)))
        keep_specs.append(pl.BlockSpec((1, rows), lambda h, i: (0, 0)))
        key_args.append(source)
        value_args.append(source)
        keep_args.append(keep)
    stat_spec = pl.BlockSpec((pl.Squeezed(), q_chunk, 1), lambda h, i: (h, i, 0))
    lane_spec = pl.BlockSpec((q_chunk, HEAD_DIM), lambda h, i: (i, h))
    stat_shape = jax.ShapeDtypeStruct((head_count, tokens, 1), jnp.float32)
    carry_specs = [] if carry is None else [stat_spec, stat_spec, lane_spec]
    if finish:
        out_shape = jax.ShapeDtypeStruct((tokens, lane_width), jnp.bfloat16)
        out_specs = lane_spec
    else:
        out_shape = (stat_shape, stat_shape, jax.ShapeDtypeStruct((tokens, lane_width), jnp.float32))
        out_specs = (stat_spec, stat_spec, lane_spec)
    flops = 4 * tokens * key_total * lane_width
    moved = 2 * (2 * tokens * lane_width + 2 * key_total * lane_width) + 4 * 6 * tokens * lane_width
    return pl.pallas_call(
        functools.partial(window_kernel, len(blocks), carry is not None, finish),
        out_shape=out_shape,
        grid=(head_count, chunks),
        in_specs=[lane_spec] + key_specs + value_specs + keep_specs + carry_specs,
        out_specs=out_specs,
        cost_estimate=pl.CostEstimate(
            flops=flops, transcendentals=tokens * key_total * head_count, bytes_accessed=moved
        ),
    )(query_rows, *key_args, *value_args, *keep_args, *(() if carry is None else carry))


def text_pieces(text_keys, text_values, text_mask, group_count, lane_width):
    count = lax.axis_size("tile")
    rows = text_keys.shape[0]
    flags = jnp.broadcast_to(text_mask.astype(jnp.bfloat16)[:, None], (rows, 128))
    per_group = jnp.stack(
        [
            jnp.concatenate(
                [
                    text_keys[:, g * lane_width : (g + 1) * lane_width],
                    text_values[:, g * lane_width : (g + 1) * lane_width],
                    flags,
                ],
                axis=1,
            )
            for g in range(group_count)
        ]
    )
    outgoing = jnp.tile(per_group, (count // group_count, 1, 1)).reshape(count * rows, 2 * lane_width + 128)
    got = lax.all_to_all(outgoing, "tile", 0, 0, tiled=True)
    return got, got[:, 2 * lane_width] > 0.5


def shards(queries, keys, values, text_keys, text_values, text_mask):
    tokens = queries.shape[1]
    lane_width = queries.shape[2]
    head_count = lane_width // HEAD_DIM
    query_heads = queries[0].reshape(tokens, head_count, HEAD_DIM)
    group_count = HEAD_GROUPS
    tiles_all = lax.axis_size("tile") // group_count
    grid_w = min(4, tiles_all)
    grid_h = min(4, tiles_all // grid_w)
    grid_f = tiles_all // (grid_w * grid_h)
    frames_valid = grid_f * TS - TS // 4
    my_index = lax.axis_index("tile")
    tile_id = my_index // group_count
    head_group = my_index % group_count
    w_pos = tile_id % grid_w
    h_pos = tile_id // grid_w % grid_h
    f_pos = tile_id // (grid_w * grid_h)
    key_rows = tokens
    if grid_f == 1:
        key_rows = min(tokens, frames_valid * TS * TS)
    own_pair = jnp.stack([keys[0, :key_rows], values[0, :key_rows]])
    local_frame = jnp.arange(key_rows, dtype=jnp.int32) // (TS * TS)

    def keep_mask(off_frame, off_height, off_width):
        inside = (
            (f_pos + off_frame >= 0)
            & (f_pos + off_frame < grid_f)
            & (h_pos + off_height >= 0)
            & (h_pos + off_height < grid_h)
            & (w_pos + off_width >= 0)
            & (w_pos + off_width < grid_w)
        )
        return inside & ((f_pos + off_frame) * TS + local_frame < frames_valid)

    running = (
        jnp.full((head_count, tokens), MASKED, jnp.float32),
        jnp.zeros((head_count, tokens), jnp.float32),
        jnp.zeros((head_count, tokens, HEAD_DIM), jnp.float32),
    )
    text_got, text_keep = text_pieces(text_keys, text_values, text_mask, group_count, lane_width)
    width_set = {0: own_pair}
    for off_width in (-1, 1):
        width_set[off_width] = passed_along(own_pair, "tile", -off_width * group_count)
    if grid_h == 1 and grid_f == 1:
        as_row = lambda keep: keep.astype(jnp.float32)[None, :]
        carry = window_attention(queries[0], [(own_pair, 0, 1, as_row(keep_mask(0, 0, 0)))], finish=False)
        carry = window_attention(
            queries[0], [(text_got, 0, head_count, as_row(text_keep))], carry=carry, finish=False
        )
        blocks = [(width_set[off_width], 0, 1, as_row(keep_mask(0, 0, off_width))) for off_width in (-1, 1)]
        return window_attention(queries[0], blocks, carry=carry)[None]
    piece_keys = text_got[:, :lane_width]
    piece_values = text_got[:, lane_width : 2 * lane_width]
    running = fold_block(running, query_heads, piece_keys, piece_values, text_keep)
    running = fold_block(running, query_heads, own_pair[0], own_pair[1], keep_mask(0, 0, 0))
    width_offsets = sorted(width_set)
    row_stack = jnp.stack([width_set[spot] for spot in width_offsets])
    height_set = {0: row_stack}
    if grid_h > 1:
        for off_height in (-1, 1):
            height_set[off_height] = passed_along(
                shortened(row_stack), "tile", -off_height * grid_w * group_count
            ).astype(row_stack.dtype)
    height_offsets = sorted(height_set)
    slab_stack = jnp.stack([height_set[spot] for spot in height_offsets])

    def fold_slab(state_now, slab_pairs, off_frame):
        for h_slot, off_height in enumerate(height_offsets):
            for w_slot, off_width in enumerate(width_offsets):
                if off_frame == 0 and off_height == 0 and (off_width == 0):
                    continue
                state_now = fold_block(
                    state_now,
                    query_heads,
                    slab_pairs[h_slot, w_slot, 0],
                    slab_pairs[h_slot, w_slot, 1],
                    keep_mask(off_frame, off_height, off_width),
                )
        return state_now

    running = fold_slab(running, slab_stack, 0)
    if grid_f > 1:
        for off_frame in (-1, 1):
            got_slab = passed_along(
                shortened(slab_stack), "tile", -off_frame * grid_h * grid_w * group_count
            ).astype(slab_stack.dtype)
            running = fold_slab(running, got_slab, off_frame)
    row_top, row_total, summed = running
    result = summed / row_total[:, :, None]
    result = jnp.transpose(result, (1, 0, 2)).reshape(tokens, lane_width)
    return result.astype(jnp.bfloat16)[None]


def solution(mesh):
    return jax.shard_map(
        shards,
        mesh=mesh,
        in_specs=(
            P(("req", "tile"), None, None),
            P(("req", "tile"), None, None),
            P(("req", "tile"), None, None),
            P(("req", "tile"), None),
            P(("req", "tile"), None),
            P(("req", "tile")),
        ),
        out_specs=P(("req", "tile"), None, None),
        check_vma=False,
    )
```

```python
import functools
import math

import jax
import jax.numpy as jnp
from jax import lax
from jax.experimental import pallas as pl
from jax.experimental.pallas import tpu as pltpu
from jax.sharding import PartitionSpec as P

TS = 8
HEAD_DIM = 128
HEAD_GROUPS = 4


MASKED = -1e30


def passed_along(value, axis, steps):
    count = lax.axis_size(axis)
    first, last = (max(0, -steps), min(count, count - steps))
    return lax.ppermute(value, axis, [(source, source + steps) for source in range(first, last)])


def shortened(value):
    return jax.tree.map(lambda a: a.astype(jnp.bfloat16) if a.dtype == jnp.float32 else a, value)


def fold_block(running, query_heads, key_block, value_block, key_keep):
    row_top, row_total, summed = running
    head_count = query_heads.shape[1]
    key_heads = key_block.reshape(key_block.shape[0], head_count, HEAD_DIM)
    value_heads = value_block.reshape(value_block.shape[0], head_count, HEAD_DIM)
    scores = jnp.einsum("qhd,khd->hqk", query_heads, key_heads, preferred_element_type=jnp.float32)
    scores = scores * (1.0 / math.sqrt(HEAD_DIM))
    scores = jnp.where(key_keep[None, None, :], scores, MASKED)
    new_top = jnp.maximum(row_top, jnp.max(scores, axis=-1))
    scale_down = jnp.exp(row_top - new_top)
    exp_terms = jnp.where(key_keep[None, None, :], jnp.exp(scores - new_top[:, :, None]), 0.0)
    row_total = row_total * scale_down + jnp.sum(exp_terms, axis=-1)
    weights = exp_terms.astype(jnp.bfloat16)
    summed = summed * scale_down[:, :, None] + jnp.einsum(
        "hqk,khd->hqd", weights, value_heads, preferred_element_type=jnp.float32
    )
    return (new_top, row_total, summed)


def window_kernel(blocks, carry_in, finish, q_chunk, q_ref, *refs):
    block_count = len(blocks)
    source_refs = refs[:block_count]
    keep_refs = refs[block_count : 2 * block_count]
    rest = refs[2 * block_count :]
    tokens, lane_width = q_ref.shape
    head_count = lane_width // HEAD_DIM
    keeps = [keep_refs[b][...] > 0.5 for b in range(block_count)]
    for h in range(head_count):
        lanes = slice(h * HEAD_DIM, (h + 1) * HEAD_DIM)
        for c in range(tokens // q_chunk):
            rows = slice(c * q_chunk, (c + 1) * q_chunk)
            query = q_ref[rows, lanes]
            scores, value_tiles = [], []
            for b, (pair_form, key_at, value_at) in enumerate(blocks):
                if pair_form:
                    key_tile = source_refs[b][key_at, :, lanes]
                    value_tile = source_refs[b][value_at, :, lanes]
                else:
                    key_tile = source_refs[b][:, (key_at + h) * HEAD_DIM : (key_at + h + 1) * HEAD_DIM]
                    value_tile = source_refs[b][:, (value_at + h) * HEAD_DIM : (value_at + h + 1) * HEAD_DIM]
                s = lax.dot_general(
                    query, key_tile, (((1,), (1,)), ((), ())), preferred_element_type=jnp.float32
                )
                s = s * (1.0 / math.sqrt(HEAD_DIM))
                scores.append(jnp.where(keeps[b], s, MASKED))
                value_tiles.append(value_tile)
            top = scores[0].max(axis=1, keepdims=True)
            for s in scores[1:]:
                top = jnp.maximum(top, s.max(axis=1, keepdims=True))
            if carry_in:
                top_in = rest[0][h, rows, :]
                top = jnp.maximum(top, top_in)
                scale_down = jnp.exp(top_in - top)
                total = rest[1][h, rows, :] * scale_down
                summed = rest[2][rows, lanes] * scale_down
            else:
                total = jnp.zeros_like(top)
                summed = None
            for b in range(block_count):
                terms = jnp.exp(scores[b] - top)
                total = total + terms.sum(axis=1, keepdims=True)
                part = jnp.dot(terms.astype(jnp.bfloat16), value_tiles[b], preferred_element_type=jnp.float32)
                summed = part if summed is None else summed + part
            outs = rest[3:] if carry_in else rest
            if finish:
                outs[0][rows, lanes] = (summed / total).astype(outs[0].dtype)
            else:
                outs[0][h, rows, :] = top
                outs[1][h, rows, :] = total
                outs[2][rows, lanes] = summed


def window_attention(query_rows, blocks, carry=None, finish=True):
    tokens, lane_width = query_rows.shape
    head_count = lane_width // HEAD_DIM
    q_chunk = 256 if tokens % 256 == 0 else tokens
    layout, sources, keeps = [], [], []
    key_total = 0
    for source, key_at, value_at, keep in blocks:
        key_total += keep.shape[1]
        layout.append((source.ndim == 3, key_at, value_at))
        sources.append(source)
        keeps.append(keep)
    stat_shape = jax.ShapeDtypeStruct((head_count, tokens, 1), jnp.float32)
    if finish:
        out_shape = jax.ShapeDtypeStruct((tokens, lane_width), jnp.bfloat16)
        out_specs = pl.BlockSpec(memory_space=pltpu.VMEM)
    else:
        out_shape = (stat_shape, stat_shape, jax.ShapeDtypeStruct((tokens, lane_width), jnp.float32))
        out_specs = tuple(pl.BlockSpec(memory_space=pltpu.VMEM) for _ in range(3))
    carry_args = () if carry is None else tuple(carry)
    operand_count = 1 + 2 * len(blocks) + len(carry_args)
    flops = 4 * tokens * key_total * lane_width
    moved = 2 * (2 * tokens * lane_width + 2 * key_total * lane_width) + 4 * 6 * tokens * lane_width
    return pl.pallas_call(
        functools.partial(window_kernel, tuple(layout), carry is not None, finish, q_chunk),
        out_shape=out_shape,
        in_specs=[pl.BlockSpec(memory_space=pltpu.VMEM)] * operand_count,
        out_specs=out_specs,
        cost_estimate=pl.CostEstimate(
            flops=flops, transcendentals=tokens * key_total * head_count, bytes_accessed=moved
        ),
    )(query_rows, *sources, *keeps, *carry_args)


def text_pieces(text_keys, text_values, text_mask, group_count, lane_width):
    count = lax.axis_size("tile")
    rows = text_keys.shape[0]
    flags = jnp.broadcast_to(text_mask.astype(jnp.bfloat16)[:, None], (rows, 128))
    per_group = jnp.stack(
        [
            jnp.concatenate(
                [
                    text_keys[:, g * lane_width : (g + 1) * lane_width],
                    text_values[:, g * lane_width : (g + 1) * lane_width],
                    flags,
                ],
                axis=1,
            )
            for g in range(group_count)
        ]
    )
    outgoing = jnp.tile(per_group, (count // group_count, 1, 1)).reshape(count * rows, 2 * lane_width + 128)
    got = lax.all_to_all(outgoing, "tile", 0, 0, tiled=True)
    return got, got[:, 2 * lane_width] > 0.5


def shards(queries, keys, values, text_keys, text_values, text_mask):
    tokens = queries.shape[1]
    lane_width = queries.shape[2]
    head_count = lane_width // HEAD_DIM
    query_heads = queries[0].reshape(tokens, head_count, HEAD_DIM)
    group_count = HEAD_GROUPS
    tiles_all = lax.axis_size("tile") // group_count
    grid_w = min(4, tiles_all)
    grid_h = min(4, tiles_all // grid_w)
    grid_f = tiles_all // (grid_w * grid_h)
    frames_valid = grid_f * TS - TS // 4
    my_index = lax.axis_index("tile")
    tile_id = my_index // group_count
    head_group = my_index % group_count
    w_pos = tile_id % grid_w
    h_pos = tile_id // grid_w % grid_h
    f_pos = tile_id // (grid_w * grid_h)
    key_rows = tokens
    if grid_f == 1:
        key_rows = min(tokens, frames_valid * TS * TS)
    own_pair = jnp.stack([keys[0, :key_rows], values[0, :key_rows]])
    local_frame = jnp.arange(key_rows, dtype=jnp.int32) // (TS * TS)

    def keep_mask(off_frame, off_height, off_width):
        inside = (
            (f_pos + off_frame >= 0)
            & (f_pos + off_frame < grid_f)
            & (h_pos + off_height >= 0)
            & (h_pos + off_height < grid_h)
            & (w_pos + off_width >= 0)
            & (w_pos + off_width < grid_w)
        )
        return inside & ((f_pos + off_frame) * TS + local_frame < frames_valid)

    running = (
        jnp.full((head_count, tokens), MASKED, jnp.float32),
        jnp.zeros((head_count, tokens), jnp.float32),
        jnp.zeros((head_count, tokens, HEAD_DIM), jnp.float32),
    )
    text_got, text_keep = text_pieces(text_keys, text_values, text_mask, group_count, lane_width)
    width_set = {0: own_pair}
    for off_width in (-1, 1):
        width_set[off_width] = passed_along(own_pair, "tile", -off_width * group_count)
    if grid_h == 1 and grid_f == 1:
        as_row = lambda keep: keep.astype(jnp.float32)[None, :]
        carry = window_attention(queries[0], [(own_pair, 0, 1, as_row(keep_mask(0, 0, 0)))], finish=False)
        carry = window_attention(
            queries[0], [(text_got, 0, head_count, as_row(text_keep))], carry=carry, finish=False
        )
        blocks = [(width_set[off_width], 0, 1, as_row(keep_mask(0, 0, off_width))) for off_width in (-1, 1)]
        return window_attention(queries[0], blocks, carry=carry)[None]
    piece_keys = text_got[:, :lane_width]
    piece_values = text_got[:, lane_width : 2 * lane_width]
    running = fold_block(running, query_heads, piece_keys, piece_values, text_keep)
    running = fold_block(running, query_heads, own_pair[0], own_pair[1], keep_mask(0, 0, 0))
    width_offsets = sorted(width_set)
    row_stack = jnp.stack([width_set[spot] for spot in width_offsets])
    height_set = {0: row_stack}
    if grid_h > 1:
        for off_height in (-1, 1):
            height_set[off_height] = passed_along(
                shortened(row_stack), "tile", -off_height * grid_w * group_count
            ).astype(row_stack.dtype)
    height_offsets = sorted(height_set)
    slab_stack = jnp.stack([height_set[spot] for spot in height_offsets])

    def fold_slab(state_now, slab_pairs, off_frame):
        for h_slot, off_height in enumerate(height_offsets):
            for w_slot, off_width in enumerate(width_offsets):
                if off_frame == 0 and off_height == 0 and (off_width == 0):
                    continue
                state_now = fold_block(
                    state_now,
                    query_heads,
                    slab_pairs[h_slot, w_slot, 0],
                    slab_pairs[h_slot, w_slot, 1],
                    keep_mask(off_frame, off_height, off_width),
                )
        return state_now

    running = fold_slab(running, slab_stack, 0)
    if grid_f > 1:
        for off_frame in (-1, 1):
            got_slab = passed_along(
                shortened(slab_stack), "tile", -off_frame * grid_h * grid_w * group_count
            ).astype(slab_stack.dtype)
            running = fold_slab(running, got_slab, off_frame)
    row_top, row_total, summed = running
    result = summed / row_total[:, :, None]
    result = jnp.transpose(result, (1, 0, 2)).reshape(tokens, lane_width)
    return result.astype(jnp.bfloat16)[None]


def solution(mesh):
    return jax.shard_map(
        shards,
        mesh=mesh,
        in_specs=(
            P(("req", "tile"), None, None),
            P(("req", "tile"), None, None),
            P(("req", "tile"), None, None),
            P(("req", "tile"), None),
            P(("req", "tile"), None),
            P(("req", "tile")),
        ),
        out_specs=P(("req", "tile"), None, None),
        check_vma=False,
    )
```

```python
import functools
import math

import jax
import jax.numpy as jnp
from jax import lax
from jax.experimental import pallas as pl
from jax.experimental.pallas import tpu as pltpu
from jax.sharding import PartitionSpec as P

TS = 8
HEAD_DIM = 128
HEAD_GROUPS = 4


MASKED = -1e30


def passed_along(value, axis, steps):
    count = lax.axis_size(axis)
    first, last = (max(0, -steps), min(count, count - steps))
    return lax.ppermute(value, axis, [(source, source + steps) for source in range(first, last)])


def shortened(value):
    return jax.tree.map(lambda a: a.astype(jnp.bfloat16) if a.dtype == jnp.float32 else a, value)


def fold_block(running, query_heads, key_block, value_block, key_keep):
    row_top, row_total, summed = running
    head_count = query_heads.shape[1]
    key_heads = key_block.reshape(key_block.shape[0], head_count, HEAD_DIM)
    value_heads = value_block.reshape(value_block.shape[0], head_count, HEAD_DIM)
    scores = jnp.einsum("qhd,khd->hqk", query_heads, key_heads, preferred_element_type=jnp.float32)
    scores = scores * (1.0 / math.sqrt(HEAD_DIM))
    scores = jnp.where(key_keep[None, None, :], scores, MASKED)
    new_top = jnp.maximum(row_top, jnp.max(scores, axis=-1))
    scale_down = jnp.exp(row_top - new_top)
    exp_terms = jnp.where(key_keep[None, None, :], jnp.exp(scores - new_top[:, :, None]), 0.0)
    row_total = row_total * scale_down + jnp.sum(exp_terms, axis=-1)
    weights = exp_terms.astype(jnp.bfloat16)
    summed = summed * scale_down[:, :, None] + jnp.einsum(
        "hqk,khd->hqd", weights, value_heads, preferred_element_type=jnp.float32
    )
    return (new_top, row_total, summed)


def window_kernel(blocks, carry_in, finish, q_chunk, q_ref, *refs):
    block_count = len(blocks)
    source_refs = refs[:block_count]
    keep_refs = refs[block_count : 2 * block_count]
    rest = refs[2 * block_count :]
    tokens, lane_width = q_ref.shape
    head_count = lane_width // HEAD_DIM
    keeps = [keep_refs[b][...] > 0.5 for b in range(block_count)]
    for h in range(head_count):
        lanes = slice(h * HEAD_DIM, (h + 1) * HEAD_DIM)
        for c in range(tokens // q_chunk):
            rows = slice(c * q_chunk, (c + 1) * q_chunk)
            query = q_ref[rows, lanes]
            scores, value_tiles = [], []
            for b, (pair_form, key_at, value_at) in enumerate(blocks):
                if pair_form:
                    key_tile = source_refs[b][key_at, :, lanes]
                    value_tile = source_refs[b][value_at, :, lanes]
                else:
                    key_tile = source_refs[b][:, (key_at + h) * HEAD_DIM : (key_at + h + 1) * HEAD_DIM]
                    value_tile = source_refs[b][:, (value_at + h) * HEAD_DIM : (value_at + h + 1) * HEAD_DIM]
                s = lax.dot_general(
                    query, key_tile, (((1,), (1,)), ((), ())), preferred_element_type=jnp.float32
                )
                s = s * (1.0 / math.sqrt(HEAD_DIM))
                scores.append(jnp.where(keeps[b], s, MASKED))
                value_tiles.append(value_tile)
            top = scores[0].max(axis=1, keepdims=True)
            for s in scores[1:]:
                top = jnp.maximum(top, s.max(axis=1, keepdims=True))
            if carry_in:
                top_in = rest[0][h, rows, :]
                top = jnp.maximum(top, top_in)
                scale_down = jnp.exp(top_in - top)
                total = rest[1][h, rows, :] * scale_down
                summed = rest[2][rows, lanes] * scale_down
            else:
                total = jnp.zeros_like(top)
                summed = None
            for b in range(block_count):
                terms = jnp.exp(scores[b] - top)
                total = total + terms.sum(axis=1, keepdims=True)
                part = jnp.dot(terms.astype(jnp.bfloat16), value_tiles[b], preferred_element_type=jnp.float32)
                summed = part if summed is None else summed + part
            outs = rest[3:] if carry_in else rest
            if finish:
                outs[0][rows, lanes] = (summed / total).astype(outs[0].dtype)
            else:
                outs[0][h, rows, :] = top
                outs[1][h, rows, :] = total
                outs[2][rows, lanes] = summed


def window_attention(query_rows, blocks, carry=None, finish=True):
    tokens, lane_width = query_rows.shape
    head_count = lane_width // HEAD_DIM
    q_chunk = 512 if tokens % 512 == 0 else tokens
    layout, sources, keeps = [], [], []
    key_total = 0
    for source, key_at, value_at, keep in blocks:
        key_total += keep.shape[1]
        layout.append((source.ndim == 3, key_at, value_at))
        sources.append(source)
        keeps.append(keep)
    stat_shape = jax.ShapeDtypeStruct((head_count, tokens, 1), jnp.float32)
    if finish:
        out_shape = jax.ShapeDtypeStruct((tokens, lane_width), jnp.bfloat16)
        out_specs = pl.BlockSpec(memory_space=pltpu.VMEM)
    else:
        out_shape = (stat_shape, stat_shape, jax.ShapeDtypeStruct((tokens, lane_width), jnp.float32))
        out_specs = tuple(pl.BlockSpec(memory_space=pltpu.VMEM) for _ in range(3))
    carry_args = () if carry is None else tuple(carry)
    operand_count = 1 + 2 * len(blocks) + len(carry_args)
    flops = 4 * tokens * key_total * lane_width
    moved = 2 * (2 * tokens * lane_width + 2 * key_total * lane_width) + 4 * 6 * tokens * lane_width
    return pl.pallas_call(
        functools.partial(window_kernel, tuple(layout), carry is not None, finish, q_chunk),
        out_shape=out_shape,
        in_specs=[pl.BlockSpec(memory_space=pltpu.VMEM)] * operand_count,
        out_specs=out_specs,
        cost_estimate=pl.CostEstimate(
            flops=flops, transcendentals=tokens * key_total * head_count, bytes_accessed=moved
        ),
    )(query_rows, *sources, *keeps, *carry_args)


def text_pieces(text_keys, text_values, text_mask, group_count, lane_width):
    count = lax.axis_size("tile")
    rows = text_keys.shape[0]
    flags = jnp.broadcast_to(text_mask.astype(jnp.bfloat16)[:, None], (rows, 128))
    per_group = jnp.stack(
        [
            jnp.concatenate(
                [
                    text_keys[:, g * lane_width : (g + 1) * lane_width],
                    text_values[:, g * lane_width : (g + 1) * lane_width],
                    flags,
                ],
                axis=1,
            )
            for g in range(group_count)
        ]
    )
    outgoing = jnp.tile(per_group, (count // group_count, 1, 1)).reshape(count * rows, 2 * lane_width + 128)
    got = lax.all_to_all(outgoing, "tile", 0, 0, tiled=True)
    return got, got[:, 2 * lane_width] > 0.5


def shards(queries, keys, values, text_keys, text_values, text_mask):
    tokens = queries.shape[1]
    lane_width = queries.shape[2]
    head_count = lane_width // HEAD_DIM
    query_heads = queries[0].reshape(tokens, head_count, HEAD_DIM)
    group_count = HEAD_GROUPS
    tiles_all = lax.axis_size("tile") // group_count
    grid_w = min(4, tiles_all)
    grid_h = min(4, tiles_all // grid_w)
    grid_f = tiles_all // (grid_w * grid_h)
    frames_valid = grid_f * TS - TS // 4
    my_index = lax.axis_index("tile")
    tile_id = my_index // group_count
    head_group = my_index % group_count
    w_pos = tile_id % grid_w
    h_pos = tile_id // grid_w % grid_h
    f_pos = tile_id // (grid_w * grid_h)
    key_rows = tokens
    if grid_f == 1:
        key_rows = min(tokens, frames_valid * TS * TS)
    own_pair = jnp.stack([keys[0, :key_rows], values[0, :key_rows]])
    local_frame = jnp.arange(key_rows, dtype=jnp.int32) // (TS * TS)

    def keep_mask(off_frame, off_height, off_width):
        inside = (
            (f_pos + off_frame >= 0)
            & (f_pos + off_frame < grid_f)
            & (h_pos + off_height >= 0)
            & (h_pos + off_height < grid_h)
            & (w_pos + off_width >= 0)
            & (w_pos + off_width < grid_w)
        )
        return inside & ((f_pos + off_frame) * TS + local_frame < frames_valid)

    running = (
        jnp.full((head_count, tokens), MASKED, jnp.float32),
        jnp.zeros((head_count, tokens), jnp.float32),
        jnp.zeros((head_count, tokens, HEAD_DIM), jnp.float32),
    )
    text_got, text_keep = text_pieces(text_keys, text_values, text_mask, group_count, lane_width)
    width_set = {0: own_pair}
    for off_width in (-1, 1):
        width_set[off_width] = passed_along(own_pair, "tile", -off_width * group_count)
    if grid_h == 1 and grid_f == 1:
        as_row = lambda keep: keep.astype(jnp.float32)[None, :]
        carry = window_attention(queries[0], [(own_pair, 0, 1, as_row(keep_mask(0, 0, 0)))], finish=False)
        carry = window_attention(
            queries[0], [(text_got, 0, head_count, as_row(text_keep))], carry=carry, finish=False
        )
        blocks = [(width_set[off_width], 0, 1, as_row(keep_mask(0, 0, off_width))) for off_width in (-1, 1)]
        return window_attention(queries[0], blocks, carry=carry)[None]
    piece_keys = text_got[:, :lane_width]
    piece_values = text_got[:, lane_width : 2 * lane_width]
    running = fold_block(running, query_heads, piece_keys, piece_values, text_keep)
    running = fold_block(running, query_heads, own_pair[0], own_pair[1], keep_mask(0, 0, 0))
    width_offsets = sorted(width_set)
    row_stack = jnp.stack([width_set[spot] for spot in width_offsets])
    height_set = {0: row_stack}
    if grid_h > 1:
        for off_height in (-1, 1):
            height_set[off_height] = passed_along(
                shortened(row_stack), "tile", -off_height * grid_w * group_count
            ).astype(row_stack.dtype)
    height_offsets = sorted(height_set)
    slab_stack = jnp.stack([height_set[spot] for spot in height_offsets])

    def fold_slab(state_now, slab_pairs, off_frame):
        for h_slot, off_height in enumerate(height_offsets):
            for w_slot, off_width in enumerate(width_offsets):
                if off_frame == 0 and off_height == 0 and (off_width == 0):
                    continue
                state_now = fold_block(
                    state_now,
                    query_heads,
                    slab_pairs[h_slot, w_slot, 0],
                    slab_pairs[h_slot, w_slot, 1],
                    keep_mask(off_frame, off_height, off_width),
                )
        return state_now

    running = fold_slab(running, slab_stack, 0)
    if grid_f > 1:
        for off_frame in (-1, 1):
            got_slab = passed_along(
                shortened(slab_stack), "tile", -off_frame * grid_h * grid_w * group_count
            ).astype(slab_stack.dtype)
            running = fold_slab(running, got_slab, off_frame)
    row_top, row_total, summed = running
    result = summed / row_total[:, :, None]
    result = jnp.transpose(result, (1, 0, 2)).reshape(tokens, lane_width)
    return result.astype(jnp.bfloat16)[None]


def solution(mesh):
    return jax.shard_map(
        shards,
        mesh=mesh,
        in_specs=(
            P(("req", "tile"), None, None),
            P(("req", "tile"), None, None),
            P(("req", "tile"), None, None),
            P(("req", "tile"), None),
            P(("req", "tile"), None),
            P(("req", "tile")),
        ),
        out_specs=P(("req", "tile"), None, None),
        check_vma=False,
    )
```

```python
import functools
import math

import jax
import jax.numpy as jnp
from jax import lax
from jax.experimental import pallas as pl
from jax.experimental.pallas import tpu as pltpu
from jax.sharding import PartitionSpec as P

TS = 8
HEAD_DIM = 128
HEAD_GROUPS = 4


MASKED = -1e30


def passed_along(value, axis, steps):
    count = lax.axis_size(axis)
    first, last = (max(0, -steps), min(count, count - steps))
    return lax.ppermute(value, axis, [(source, source + steps) for source in range(first, last)])


def shortened(value):
    return jax.tree.map(lambda a: a.astype(jnp.bfloat16) if a.dtype == jnp.float32 else a, value)


def fold_block(running, query_heads, key_block, value_block, key_keep):
    row_top, row_total, summed = running
    head_count = query_heads.shape[1]
    key_heads = key_block.reshape(key_block.shape[0], head_count, HEAD_DIM)
    value_heads = value_block.reshape(value_block.shape[0], head_count, HEAD_DIM)
    scores = jnp.einsum("qhd,khd->hqk", query_heads, key_heads, preferred_element_type=jnp.float32)
    scores = scores * (1.0 / math.sqrt(HEAD_DIM))
    scores = jnp.where(key_keep[None, None, :], scores, MASKED)
    new_top = jnp.maximum(row_top, jnp.max(scores, axis=-1))
    scale_down = jnp.exp(row_top - new_top)
    exp_terms = jnp.where(key_keep[None, None, :], jnp.exp(scores - new_top[:, :, None]), 0.0)
    row_total = row_total * scale_down + jnp.sum(exp_terms, axis=-1)
    weights = exp_terms.astype(jnp.bfloat16)
    summed = summed * scale_down[:, :, None] + jnp.einsum(
        "hqk,khd->hqd", weights, value_heads, preferred_element_type=jnp.float32
    )
    return (new_top, row_total, summed)


def window_kernel(blocks, carry_in, finish, q_chunk, q_ref, *refs):
    block_count = len(blocks)
    source_refs = refs[:block_count]
    keep_refs = refs[block_count : 2 * block_count]
    rest = refs[2 * block_count :]
    tokens, lane_width = q_ref.shape
    head_count = lane_width // HEAD_DIM
    keeps = [keep_refs[b][...] > 0.5 for b in range(block_count)]
    for h in range(head_count):
        lanes = slice(h * HEAD_DIM, (h + 1) * HEAD_DIM)
        for c in range(tokens // q_chunk):
            rows = slice(c * q_chunk, (c + 1) * q_chunk)
            query = q_ref[rows, lanes]
            scores, value_tiles = [], []
            for b, (pair_form, key_at, value_at) in enumerate(blocks):
                if pair_form:
                    key_tile = source_refs[b][key_at, :, lanes]
                    value_tile = source_refs[b][value_at, :, lanes]
                else:
                    key_tile = source_refs[b][:, (key_at + h) * HEAD_DIM : (key_at + h + 1) * HEAD_DIM]
                    value_tile = source_refs[b][:, (value_at + h) * HEAD_DIM : (value_at + h + 1) * HEAD_DIM]
                s = lax.dot_general(
                    query, key_tile, (((1,), (1,)), ((), ())), preferred_element_type=jnp.float32
                )
                s = s * (1.0 / math.sqrt(HEAD_DIM))
                scores.append(jnp.where(keeps[b], s, MASKED))
                value_tiles.append(value_tile)
            top = scores[0].max(axis=1, keepdims=True)
            for s in scores[1:]:
                top = jnp.maximum(top, s.max(axis=1, keepdims=True))
            if carry_in:
                top_in = rest[0][h, rows, :]
                top = jnp.maximum(top, top_in)
                scale_down = jnp.exp(top_in - top)
                total = rest[1][h, rows, :] * scale_down
                summed = rest[2][rows, lanes] * scale_down
            else:
                total = jnp.zeros_like(top)
                summed = None
            for b in range(block_count):
                terms = jnp.exp(scores[b] - top)
                total = total + terms.sum(axis=1, keepdims=True)
                part = jnp.dot(terms.astype(jnp.bfloat16), value_tiles[b], preferred_element_type=jnp.float32)
                summed = part if summed is None else summed + part
            outs = rest[3:] if carry_in else rest
            if finish:
                outs[0][rows, lanes] = (summed / total).astype(outs[0].dtype)
            else:
                outs[0][h, rows, :] = top
                outs[1][h, rows, :] = total
                outs[2][rows, lanes] = summed


def window_attention(query_rows, blocks, carry=None, finish=True):
    tokens, lane_width = query_rows.shape
    head_count = lane_width // HEAD_DIM
    q_chunk = 512 if tokens % 512 == 0 else tokens
    layout, sources, keeps = [], [], []
    key_total = 0
    for source, key_at, value_at, keep in blocks:
        key_total += keep.shape[1]
        layout.append((source.ndim == 3, key_at, value_at))
        sources.append(source)
        keeps.append(keep)
    stat_shape = jax.ShapeDtypeStruct((head_count, tokens, 1), jnp.float32)
    if finish:
        out_shape = jax.ShapeDtypeStruct((tokens, lane_width), jnp.bfloat16)
        out_specs = pl.BlockSpec(memory_space=pltpu.VMEM)
    else:
        out_shape = (stat_shape, stat_shape, jax.ShapeDtypeStruct((tokens, lane_width), jnp.float32))
        out_specs = tuple(pl.BlockSpec(memory_space=pltpu.VMEM) for _ in range(3))
    carry_args = () if carry is None else tuple(carry)
    operand_count = 1 + 2 * len(blocks) + len(carry_args)
    flops = 4 * tokens * key_total * lane_width
    moved = 2 * (2 * tokens * lane_width + 2 * key_total * lane_width) + 4 * 6 * tokens * lane_width
    return pl.pallas_call(
        functools.partial(window_kernel, tuple(layout), carry is not None, finish, q_chunk),
        out_shape=out_shape,
        in_specs=[pl.BlockSpec(memory_space=pltpu.VMEM)] * operand_count,
        out_specs=out_specs,
        cost_estimate=pl.CostEstimate(
            flops=flops, transcendentals=tokens * key_total * head_count, bytes_accessed=moved
        ),
    )(query_rows, *sources, *keeps, *carry_args)


def text_pieces(text_keys, text_values, text_mask, group_count, lane_width):
    count = lax.axis_size("tile")
    rows = text_keys.shape[0]
    flags = jnp.broadcast_to(text_mask.astype(jnp.bfloat16)[:, None], (rows, 128))
    per_group = jnp.stack(
        [
            jnp.concatenate(
                [
                    text_keys[:, g * lane_width : (g + 1) * lane_width],
                    text_values[:, g * lane_width : (g + 1) * lane_width],
                    flags,
                ],
                axis=1,
            )
            for g in range(group_count)
        ]
    )
    outgoing = jnp.tile(per_group, (count // group_count, 1, 1)).reshape(count * rows, 2 * lane_width + 128)
    got = lax.all_to_all(outgoing, "tile", 0, 0, tiled=True)
    return got, got[:, 2 * lane_width] > 0.5


def shards(queries, keys, values, text_keys, text_values, text_mask):
    tokens = queries.shape[1]
    lane_width = queries.shape[2]
    head_count = lane_width // HEAD_DIM
    query_heads = queries[0].reshape(tokens, head_count, HEAD_DIM)
    group_count = HEAD_GROUPS
    tiles_all = lax.axis_size("tile") // group_count
    grid_w = min(4, tiles_all)
    grid_h = min(4, tiles_all // grid_w)
    grid_f = tiles_all // (grid_w * grid_h)
    frames_valid = grid_f * TS - TS // 4
    my_index = lax.axis_index("tile")
    tile_id = my_index // group_count
    head_group = my_index % group_count
    w_pos = tile_id % grid_w
    h_pos = tile_id // grid_w % grid_h
    f_pos = tile_id // (grid_w * grid_h)
    key_rows = tokens
    if grid_f == 1:
        key_rows = min(tokens, frames_valid * TS * TS)
    own_pair = jnp.stack([keys[0, :key_rows], values[0, :key_rows]])
    local_frame = jnp.arange(key_rows, dtype=jnp.int32) // (TS * TS)

    def keep_mask(off_frame, off_height, off_width):
        inside = (
            (f_pos + off_frame >= 0)
            & (f_pos + off_frame < grid_f)
            & (h_pos + off_height >= 0)
            & (h_pos + off_height < grid_h)
            & (w_pos + off_width >= 0)
            & (w_pos + off_width < grid_w)
        )
        return inside & ((f_pos + off_frame) * TS + local_frame < frames_valid)

    running = (
        jnp.full((head_count, tokens), MASKED, jnp.float32),
        jnp.zeros((head_count, tokens), jnp.float32),
        jnp.zeros((head_count, tokens, HEAD_DIM), jnp.float32),
    )
    text_got, text_keep = text_pieces(text_keys, text_values, text_mask, group_count, lane_width)
    width_set = {0: own_pair}
    for off_width in (-1, 1):
        width_set[off_width] = passed_along(own_pair, "tile", -off_width * group_count)
    if grid_h == 1 and grid_f == 1:
        as_row = lambda keep: keep.astype(jnp.float32)[None, :]
        carry = window_attention(queries[0], [(own_pair, 0, 1, as_row(keep_mask(0, 0, 0)))], finish=False)
        carry = window_attention(
            queries[0], [(text_got, 0, head_count, as_row(text_keep))], carry=carry, finish=False
        )
        for off_width in (-1,):
            blocks = [(width_set[off_width], 0, 1, as_row(keep_mask(0, 0, off_width)))]
            carry = window_attention(queries[0], blocks, carry=carry, finish=False)
        blocks = [(width_set[1], 0, 1, as_row(keep_mask(0, 0, 1)))]
        return window_attention(queries[0], blocks, carry=carry)[None]
    piece_keys = text_got[:, :lane_width]
    piece_values = text_got[:, lane_width : 2 * lane_width]
    running = fold_block(running, query_heads, piece_keys, piece_values, text_keep)
    running = fold_block(running, query_heads, own_pair[0], own_pair[1], keep_mask(0, 0, 0))
    width_offsets = sorted(width_set)
    row_stack = jnp.stack([width_set[spot] for spot in width_offsets])
    height_set = {0: row_stack}
    if grid_h > 1:
        for off_height in (-1, 1):
            height_set[off_height] = passed_along(
                shortened(row_stack), "tile", -off_height * grid_w * group_count
            ).astype(row_stack.dtype)
    height_offsets = sorted(height_set)
    slab_stack = jnp.stack([height_set[spot] for spot in height_offsets])

    def fold_slab(state_now, slab_pairs, off_frame):
        for h_slot, off_height in enumerate(height_offsets):
            for w_slot, off_width in enumerate(width_offsets):
                if off_frame == 0 and off_height == 0 and (off_width == 0):
                    continue
                state_now = fold_block(
                    state_now,
                    query_heads,
                    slab_pairs[h_slot, w_slot, 0],
                    slab_pairs[h_slot, w_slot, 1],
                    keep_mask(off_frame, off_height, off_width),
                )
        return state_now

    running = fold_slab(running, slab_stack, 0)
    if grid_f > 1:
        for off_frame in (-1, 1):
            got_slab = passed_along(
                shortened(slab_stack), "tile", -off_frame * grid_h * grid_w * group_count
            ).astype(slab_stack.dtype)
            running = fold_slab(running, got_slab, off_frame)
    row_top, row_total, summed = running
    result = summed / row_total[:, :, None]
    result = jnp.transpose(result, (1, 0, 2)).reshape(tokens, lane_width)
    return result.astype(jnp.bfloat16)[None]


def solution(mesh):
    return jax.shard_map(
        shards,
        mesh=mesh,
        in_specs=(
            P(("req", "tile"), None, None),
            P(("req", "tile"), None, None),
            P(("req", "tile"), None, None),
            P(("req", "tile"), None),
            P(("req", "tile"), None),
            P(("req", "tile")),
        ),
        out_specs=P(("req", "tile"), None, None),
        check_vma=False,
    )
```

```python
import functools
import math

import jax
import jax.numpy as jnp
from jax import lax
from jax.experimental import pallas as pl
from jax.experimental.pallas import tpu as pltpu
from jax.sharding import PartitionSpec as P

TS = 8
HEAD_DIM = 128
HEAD_GROUPS = 4


MASKED = -1e30


def passed_along(value, axis, steps):
    count = lax.axis_size(axis)
    first, last = (max(0, -steps), min(count, count - steps))
    return lax.ppermute(value, axis, [(source, source + steps) for source in range(first, last)])


def shortened(value):
    return jax.tree.map(lambda a: a.astype(jnp.bfloat16) if a.dtype == jnp.float32 else a, value)


def fold_block(running, query_heads, key_block, value_block, key_keep):
    row_top, row_total, summed = running
    head_count = query_heads.shape[1]
    key_heads = key_block.reshape(key_block.shape[0], head_count, HEAD_DIM)
    value_heads = value_block.reshape(value_block.shape[0], head_count, HEAD_DIM)
    scores = jnp.einsum("qhd,khd->hqk", query_heads, key_heads, preferred_element_type=jnp.float32)
    scores = scores * (1.0 / math.sqrt(HEAD_DIM))
    scores = jnp.where(key_keep[None, None, :], scores, MASKED)
    new_top = jnp.maximum(row_top, jnp.max(scores, axis=-1))
    scale_down = jnp.exp(row_top - new_top)
    exp_terms = jnp.where(key_keep[None, None, :], jnp.exp(scores - new_top[:, :, None]), 0.0)
    row_total = row_total * scale_down + jnp.sum(exp_terms, axis=-1)
    weights = exp_terms.astype(jnp.bfloat16)
    summed = summed * scale_down[:, :, None] + jnp.einsum(
        "hqk,khd->hqd", weights, value_heads, preferred_element_type=jnp.float32
    )
    return (new_top, row_total, summed)


def window_kernel(blocks, carry_in, finish, q_chunk, q_ref, *refs):
    block_count = len(blocks)
    source_refs = refs[:block_count]
    keep_refs = refs[block_count : 2 * block_count]
    rest = refs[2 * block_count :]
    tokens, lane_width = q_ref.shape
    head_count = lane_width // HEAD_DIM
    keeps = [keep_refs[b][...] > 0.5 for b in range(block_count)]
    for h in range(head_count):
        lanes = slice(h * HEAD_DIM, (h + 1) * HEAD_DIM)
        for c in range(tokens // q_chunk):
            rows = slice(c * q_chunk, (c + 1) * q_chunk)
            query = q_ref[rows, lanes]
            scores, value_tiles = [], []
            for b, (pair_form, key_at, value_at) in enumerate(blocks):
                if pair_form:
                    key_tile = source_refs[b][key_at, :, lanes]
                    value_tile = source_refs[b][value_at, :, lanes]
                else:
                    key_tile = source_refs[b][:, (key_at + h) * HEAD_DIM : (key_at + h + 1) * HEAD_DIM]
                    value_tile = source_refs[b][:, (value_at + h) * HEAD_DIM : (value_at + h + 1) * HEAD_DIM]
                s = lax.dot_general(
                    query, key_tile, (((1,), (1,)), ((), ())), preferred_element_type=jnp.float32
                )
                s = s * (1.0 / math.sqrt(HEAD_DIM))
                scores.append(jnp.where(keeps[b], s, MASKED))
                value_tiles.append(value_tile)
            top = scores[0].max(axis=1, keepdims=True)
            for s in scores[1:]:
                top = jnp.maximum(top, s.max(axis=1, keepdims=True))
            if carry_in:
                top_in = rest[0][rows, h : h + 1]
                top = jnp.maximum(top, top_in)
                scale_down = jnp.exp(top_in - top)
                total = rest[0][rows, head_count + h : head_count + h + 1] * scale_down
                summed = rest[1][rows, lanes] * scale_down
            else:
                total = jnp.zeros_like(top)
                summed = None
            for b in range(block_count):
                terms = jnp.exp(scores[b] - top)
                total = total + terms.sum(axis=1, keepdims=True)
                part = jnp.dot(terms.astype(jnp.bfloat16), value_tiles[b], preferred_element_type=jnp.float32)
                summed = part if summed is None else summed + part
            outs = rest[2:] if carry_in else rest
            if finish:
                outs[0][rows, lanes] = (summed / total).astype(outs[0].dtype)
            else:
                outs[0][rows, h : h + 1] = top
                outs[0][rows, head_count + h : head_count + h + 1] = total
                outs[1][rows, lanes] = summed


def window_attention(query_rows, blocks, carry=None, finish=True):
    tokens, lane_width = query_rows.shape
    head_count = lane_width // HEAD_DIM
    q_chunk = 512 if tokens % 512 == 0 else tokens
    layout, sources, keeps = [], [], []
    key_total = 0
    for source, key_at, value_at, keep in blocks:
        key_total += keep.shape[1]
        layout.append((source.ndim == 3, key_at, value_at))
        sources.append(source)
        keeps.append(keep)
    stat_shape = jax.ShapeDtypeStruct((tokens, 128), jnp.float32)
    if finish:
        out_shape = jax.ShapeDtypeStruct((tokens, lane_width), jnp.bfloat16)
        out_specs = pl.BlockSpec(memory_space=pltpu.VMEM)
    else:
        out_shape = (stat_shape, jax.ShapeDtypeStruct((tokens, lane_width), jnp.float32))
        out_specs = tuple(pl.BlockSpec(memory_space=pltpu.VMEM) for _ in range(2))
    carry_args = () if carry is None else tuple(carry)
    operand_count = 1 + 2 * len(blocks) + len(carry_args)
    flops = 4 * tokens * key_total * lane_width
    moved = 2 * (2 * tokens * lane_width + 2 * key_total * lane_width) + 4 * 2 * tokens * (lane_width + 128)
    return pl.pallas_call(
        functools.partial(window_kernel, tuple(layout), carry is not None, finish, q_chunk),
        out_shape=out_shape,
        in_specs=[pl.BlockSpec(memory_space=pltpu.VMEM)] * operand_count,
        out_specs=out_specs,
        cost_estimate=pl.CostEstimate(
            flops=flops, transcendentals=tokens * key_total * head_count, bytes_accessed=moved
        ),
    )(query_rows, *sources, *keeps, *carry_args)


def text_pieces(text_keys, text_values, text_mask, group_count, lane_width):
    count = lax.axis_size("tile")
    rows = text_keys.shape[0]
    flags = jnp.broadcast_to(text_mask.astype(jnp.bfloat16)[:, None], (rows, 128))
    per_group = jnp.stack(
        [
            jnp.concatenate(
                [
                    text_keys[:, g * lane_width : (g + 1) * lane_width],
                    text_values[:, g * lane_width : (g + 1) * lane_width],
                    flags,
                ],
                axis=1,
            )
            for g in range(group_count)
        ]
    )
    outgoing = jnp.tile(per_group, (count // group_count, 1, 1)).reshape(count * rows, 2 * lane_width + 128)
    got = lax.all_to_all(outgoing, "tile", 0, 0, tiled=True)
    return got, got[:, 2 * lane_width] > 0.5


def shards(queries, keys, values, text_keys, text_values, text_mask):
    tokens = queries.shape[1]
    lane_width = queries.shape[2]
    head_count = lane_width // HEAD_DIM
    query_heads = queries[0].reshape(tokens, head_count, HEAD_DIM)
    group_count = HEAD_GROUPS
    tiles_all = lax.axis_size("tile") // group_count
    grid_w = min(4, tiles_all)
    grid_h = min(4, tiles_all // grid_w)
    grid_f = tiles_all // (grid_w * grid_h)
    frames_valid = grid_f * TS - TS // 4
    my_index = lax.axis_index("tile")
    tile_id = my_index // group_count
    head_group = my_index % group_count
    w_pos = tile_id % grid_w
    h_pos = tile_id // grid_w % grid_h
    f_pos = tile_id // (grid_w * grid_h)
    key_rows = tokens
    if grid_f == 1:
        key_rows = min(tokens, frames_valid * TS * TS)
    own_pair = jnp.stack([keys[0, :key_rows], values[0, :key_rows]])
    local_frame = jnp.arange(key_rows, dtype=jnp.int32) // (TS * TS)

    def keep_mask(off_frame, off_height, off_width):
        inside = (
            (f_pos + off_frame >= 0)
            & (f_pos + off_frame < grid_f)
            & (h_pos + off_height >= 0)
            & (h_pos + off_height < grid_h)
            & (w_pos + off_width >= 0)
            & (w_pos + off_width < grid_w)
        )
        return inside & ((f_pos + off_frame) * TS + local_frame < frames_valid)

    running = (
        jnp.full((head_count, tokens), MASKED, jnp.float32),
        jnp.zeros((head_count, tokens), jnp.float32),
        jnp.zeros((head_count, tokens, HEAD_DIM), jnp.float32),
    )
    text_got, text_keep = text_pieces(text_keys, text_values, text_mask, group_count, lane_width)
    width_set = {0: own_pair}
    for off_width in (-1, 1):
        width_set[off_width] = passed_along(own_pair, "tile", -off_width * group_count)
    if grid_h == 1 and grid_f == 1:
        as_row = lambda keep: keep.astype(jnp.float32)[None, :]
        carry = window_attention(queries[0], [(own_pair, 0, 1, as_row(keep_mask(0, 0, 0)))], finish=False)
        carry = window_attention(
            queries[0], [(text_got, 0, head_count, as_row(text_keep))], carry=carry, finish=False
        )
        blocks = [(width_set[off_width], 0, 1, as_row(keep_mask(0, 0, off_width))) for off_width in (-1, 1)]
        return window_attention(queries[0], blocks, carry=carry)[None]
    piece_keys = text_got[:, :lane_width]
    piece_values = text_got[:, lane_width : 2 * lane_width]
    running = fold_block(running, query_heads, piece_keys, piece_values, text_keep)
    running = fold_block(running, query_heads, own_pair[0], own_pair[1], keep_mask(0, 0, 0))
    width_offsets = sorted(width_set)
    row_stack = jnp.stack([width_set[spot] for spot in width_offsets])
    height_set = {0: row_stack}
    if grid_h > 1:
        for off_height in (-1, 1):
            height_set[off_height] = passed_along(
                shortened(row_stack), "tile", -off_height * grid_w * group_count
            ).astype(row_stack.dtype)
    height_offsets = sorted(height_set)
    slab_stack = jnp.stack([height_set[spot] for spot in height_offsets])

    def fold_slab(state_now, slab_pairs, off_frame):
        for h_slot, off_height in enumerate(height_offsets):
            for w_slot, off_width in enumerate(width_offsets):
                if off_frame == 0 and off_height == 0 and (off_width == 0):
                    continue
                state_now = fold_block(
                    state_now,
                    query_heads,
                    slab_pairs[h_slot, w_slot, 0],
                    slab_pairs[h_slot, w_slot, 1],
                    keep_mask(off_frame, off_height, off_width),
                )
        return state_now

    running = fold_slab(running, slab_stack, 0)
    if grid_f > 1:
        for off_frame in (-1, 1):
            got_slab = passed_along(
                shortened(slab_stack), "tile", -off_frame * grid_h * grid_w * group_count
            ).astype(slab_stack.dtype)
            running = fold_slab(running, got_slab, off_frame)
    row_top, row_total, summed = running
    result = summed / row_total[:, :, None]
    result = jnp.transpose(result, (1, 0, 2)).reshape(tokens, lane_width)
    return result.astype(jnp.bfloat16)[None]


def solution(mesh):
    return jax.shard_map(
        shards,
        mesh=mesh,
        in_specs=(
            P(("req", "tile"), None, None),
            P(("req", "tile"), None, None),
            P(("req", "tile"), None, None),
            P(("req", "tile"), None),
            P(("req", "tile"), None),
            P(("req", "tile")),
        ),
        out_specs=P(("req", "tile"), None, None),
        check_vma=False,
    )
```

```python
import functools
import math

import jax
import jax.numpy as jnp
from jax import lax
from jax.experimental import pallas as pl
from jax.experimental.pallas import tpu as pltpu
from jax.sharding import PartitionSpec as P

TS = 8
HEAD_DIM = 128
HEAD_GROUPS = 4


MASKED = -1e30


def passed_along(value, axis, steps):
    count = lax.axis_size(axis)
    first, last = (max(0, -steps), min(count, count - steps))
    return lax.ppermute(value, axis, [(source, source + steps) for source in range(first, last)])


def shortened(value):
    return jax.tree.map(lambda a: a.astype(jnp.bfloat16) if a.dtype == jnp.float32 else a, value)


def fold_block(running, query_heads, key_block, value_block, key_keep):
    row_top, row_total, summed = running
    head_count = query_heads.shape[1]
    key_heads = key_block.reshape(key_block.shape[0], head_count, HEAD_DIM)
    value_heads = value_block.reshape(value_block.shape[0], head_count, HEAD_DIM)
    scores = jnp.einsum("qhd,khd->hqk", query_heads, key_heads, preferred_element_type=jnp.float32)
    scores = scores * (1.0 / math.sqrt(HEAD_DIM))
    scores = jnp.where(key_keep[None, None, :], scores, MASKED)
    new_top = jnp.maximum(row_top, jnp.max(scores, axis=-1))
    scale_down = jnp.exp(row_top - new_top)
    exp_terms = jnp.where(key_keep[None, None, :], jnp.exp(scores - new_top[:, :, None]), 0.0)
    row_total = row_total * scale_down + jnp.sum(exp_terms, axis=-1)
    weights = exp_terms.astype(jnp.bfloat16)
    summed = summed * scale_down[:, :, None] + jnp.einsum(
        "hqk,khd->hqd", weights, value_heads, preferred_element_type=jnp.float32
    )
    return (new_top, row_total, summed)


def window_kernel(blocks, carry_in, finish, q_ref, *refs):
    block_count = len(blocks)
    source_refs = refs[:block_count]
    keep_refs = refs[block_count : 2 * block_count]
    rest = refs[2 * block_count :]
    lane_width, tokens = q_ref.shape
    head_count = lane_width // HEAD_DIM
    keeps = [
        jnp.concatenate([keep_refs[b][...]] * (tokens // 128), axis=1) > 0.5 for b in range(block_count)
    ]
    for h in range(head_count):
        lanes = slice(h * HEAD_DIM, (h + 1) * HEAD_DIM)
        query_t = q_ref[lanes, :]
        scores, value_tiles = [], []
        for b, (pair_form, key_at, value_at) in enumerate(blocks):
            if pair_form:
                key_tile = source_refs[b][key_at, :, lanes]
                value_tile = source_refs[b][value_at, :, lanes]
            else:
                key_tile = source_refs[b][:, (key_at + h) * HEAD_DIM : (key_at + h + 1) * HEAD_DIM]
                value_tile = source_refs[b][:, (value_at + h) * HEAD_DIM : (value_at + h + 1) * HEAD_DIM]
            s = jnp.dot(key_tile, query_t, preferred_element_type=jnp.float32)
            s = s * (1.0 / math.sqrt(HEAD_DIM))
            scores.append(jnp.where(keeps[b], s, MASKED))
            value_tiles.append(value_tile)
        top = scores[0].max(axis=0, keepdims=True)
        for s in scores[1:]:
            top = jnp.maximum(top, s.max(axis=0, keepdims=True))
        if carry_in:
            top_in = rest[0][h : h + 1, :]
            top = jnp.maximum(top, top_in)
            scale_down = jnp.exp(top_in - top)
            total = rest[0][head_count + h : head_count + h + 1, :] * scale_down
            summed = rest[1][lanes, :] * scale_down
        else:
            total = jnp.zeros_like(top)
            summed = None
        for b in range(block_count):
            terms = jnp.exp(scores[b] - top)
            total = total + terms.sum(axis=0, keepdims=True)
            part = lax.dot_general(
                value_tiles[b],
                terms.astype(jnp.bfloat16),
                (((0,), (0,)), ((), ())),
                preferred_element_type=jnp.float32,
            )
            summed = part if summed is None else summed + part
        outs = rest[2:] if carry_in else rest
        if finish:
            outs[0][:, lanes] = jnp.transpose(summed / total).astype(outs[0].dtype)
        else:
            outs[0][h : h + 1, :] = top
            outs[0][head_count + h : head_count + h + 1, :] = total
            outs[1][lanes, :] = summed


def window_attention(query_t, blocks, carry=None, finish=True):
    lane_width, tokens = query_t.shape
    head_count = lane_width // HEAD_DIM
    layout, sources, keeps = [], [], []
    key_total = 0
    for source, key_at, value_at, keep in blocks:
        key_total += keep.shape[0]
        layout.append((source.ndim == 3, key_at, value_at))
        sources.append(source)
        keeps.append(keep)
    stat_rows = -(-2 * head_count // 8) * 8
    stat_shape = jax.ShapeDtypeStruct((stat_rows, tokens), jnp.float32)
    if finish:
        out_shape = jax.ShapeDtypeStruct((tokens, lane_width), jnp.bfloat16)
        out_specs = pl.BlockSpec(memory_space=pltpu.VMEM)
    else:
        out_shape = (stat_shape, jax.ShapeDtypeStruct((lane_width, tokens), jnp.float32))
        out_specs = tuple(pl.BlockSpec(memory_space=pltpu.VMEM) for _ in range(2))
    carry_args = () if carry is None else tuple(carry)
    operand_count = 1 + 2 * len(blocks) + len(carry_args)
    flops = 4 * tokens * key_total * lane_width
    moved = 2 * (2 * tokens * lane_width + 2 * key_total * lane_width) + 4 * 2 * tokens * (lane_width + 8)
    return pl.pallas_call(
        functools.partial(window_kernel, tuple(layout), carry is not None, finish),
        out_shape=out_shape,
        in_specs=[pl.BlockSpec(memory_space=pltpu.VMEM)] * operand_count,
        out_specs=out_specs,
        cost_estimate=pl.CostEstimate(
            flops=flops, transcendentals=tokens * key_total * head_count, bytes_accessed=moved
        ),
    )(query_t, *sources, *keeps, *carry_args)


def text_pieces(text_keys, text_values, text_mask, group_count, lane_width):
    count = lax.axis_size("tile")
    rows = text_keys.shape[0]
    flags = jnp.broadcast_to(text_mask.astype(jnp.bfloat16)[:, None], (rows, 128))
    per_group = jnp.stack(
        [
            jnp.concatenate(
                [
                    text_keys[:, g * lane_width : (g + 1) * lane_width],
                    text_values[:, g * lane_width : (g + 1) * lane_width],
                    flags,
                ],
                axis=1,
            )
            for g in range(group_count)
        ]
    )
    outgoing = jnp.tile(per_group, (count // group_count, 1, 1)).reshape(count * rows, 2 * lane_width + 128)
    got = lax.all_to_all(outgoing, "tile", 0, 0, tiled=True)
    return got, got[:, 2 * lane_width] > 0.5


def shards(queries, keys, values, text_keys, text_values, text_mask):
    tokens = queries.shape[1]
    lane_width = queries.shape[2]
    head_count = lane_width // HEAD_DIM
    query_heads = queries[0].reshape(tokens, head_count, HEAD_DIM)
    group_count = HEAD_GROUPS
    tiles_all = lax.axis_size("tile") // group_count
    grid_w = min(4, tiles_all)
    grid_h = min(4, tiles_all // grid_w)
    grid_f = tiles_all // (grid_w * grid_h)
    frames_valid = grid_f * TS - TS // 4
    my_index = lax.axis_index("tile")
    tile_id = my_index // group_count
    head_group = my_index % group_count
    w_pos = tile_id % grid_w
    h_pos = tile_id // grid_w % grid_h
    f_pos = tile_id // (grid_w * grid_h)
    key_rows = tokens
    if grid_f == 1:
        key_rows = min(tokens, frames_valid * TS * TS)
    own_pair = jnp.stack([keys[0, :key_rows], values[0, :key_rows]])
    local_frame = jnp.arange(key_rows, dtype=jnp.int32) // (TS * TS)

    def keep_mask(off_frame, off_height, off_width):
        inside = (
            (f_pos + off_frame >= 0)
            & (f_pos + off_frame < grid_f)
            & (h_pos + off_height >= 0)
            & (h_pos + off_height < grid_h)
            & (w_pos + off_width >= 0)
            & (w_pos + off_width < grid_w)
        )
        return inside & ((f_pos + off_frame) * TS + local_frame < frames_valid)

    running = (
        jnp.full((head_count, tokens), MASKED, jnp.float32),
        jnp.zeros((head_count, tokens), jnp.float32),
        jnp.zeros((head_count, tokens, HEAD_DIM), jnp.float32),
    )
    text_got, text_keep = text_pieces(text_keys, text_values, text_mask, group_count, lane_width)
    width_set = {0: own_pair}
    for off_width in (-1, 1):
        width_set[off_width] = passed_along(own_pair, "tile", -off_width * group_count)
    if grid_h == 1 and grid_f == 1:
        as_row = lambda keep: jnp.broadcast_to(keep.astype(jnp.float32)[:, None], (keep.shape[0], 128))
        query_t = jnp.transpose(queries[0])
        carry = window_attention(query_t, [(own_pair, 0, 1, as_row(keep_mask(0, 0, 0)))], finish=False)
        carry = window_attention(
            query_t, [(text_got, 0, head_count, as_row(text_keep))], carry=carry, finish=False
        )
        blocks = [(width_set[off_width], 0, 1, as_row(keep_mask(0, 0, off_width))) for off_width in (-1, 1)]
        return window_attention(query_t, blocks, carry=carry)[None]
    piece_keys = text_got[:, :lane_width]
    piece_values = text_got[:, lane_width : 2 * lane_width]
    running = fold_block(running, query_heads, piece_keys, piece_values, text_keep)
    running = fold_block(running, query_heads, own_pair[0], own_pair[1], keep_mask(0, 0, 0))
    width_offsets = sorted(width_set)
    row_stack = jnp.stack([width_set[spot] for spot in width_offsets])
    height_set = {0: row_stack}
    if grid_h > 1:
        for off_height in (-1, 1):
            height_set[off_height] = passed_along(
                shortened(row_stack), "tile", -off_height * grid_w * group_count
            ).astype(row_stack.dtype)
    height_offsets = sorted(height_set)
    slab_stack = jnp.stack([height_set[spot] for spot in height_offsets])

    def fold_slab(state_now, slab_pairs, off_frame):
        for h_slot, off_height in enumerate(height_offsets):
            for w_slot, off_width in enumerate(width_offsets):
                if off_frame == 0 and off_height == 0 and (off_width == 0):
                    continue
                state_now = fold_block(
                    state_now,
                    query_heads,
                    slab_pairs[h_slot, w_slot, 0],
                    slab_pairs[h_slot, w_slot, 1],
                    keep_mask(off_frame, off_height, off_width),
                )
        return state_now

    running = fold_slab(running, slab_stack, 0)
    if grid_f > 1:
        for off_frame in (-1, 1):
            got_slab = passed_along(
                shortened(slab_stack), "tile", -off_frame * grid_h * grid_w * group_count
            ).astype(slab_stack.dtype)
            running = fold_slab(running, got_slab, off_frame)
    row_top, row_total, summed = running
    result = summed / row_total[:, :, None]
    result = jnp.transpose(result, (1, 0, 2)).reshape(tokens, lane_width)
    return result.astype(jnp.bfloat16)[None]


def solution(mesh):
    return jax.shard_map(
        shards,
        mesh=mesh,
        in_specs=(
            P(("req", "tile"), None, None),
            P(("req", "tile"), None, None),
            P(("req", "tile"), None, None),
            P(("req", "tile"), None),
            P(("req", "tile"), None),
            P(("req", "tile")),
        ),
        out_specs=P(("req", "tile"), None, None),
        check_vma=False,
    )
```

```python
import functools
import math

import jax
import jax.numpy as jnp
from jax import lax
from jax.experimental import pallas as pl
from jax.experimental.pallas import tpu as pltpu
from jax.sharding import PartitionSpec as P

TS = 8
HEAD_DIM = 128
HEAD_GROUPS = 4


MASKED = -1e30


def passed_along(value, axis, steps):
    count = lax.axis_size(axis)
    first, last = (max(0, -steps), min(count, count - steps))
    return lax.ppermute(value, axis, [(source, source + steps) for source in range(first, last)])


def shortened(value):
    return jax.tree.map(lambda a: a.astype(jnp.bfloat16) if a.dtype == jnp.float32 else a, value)


def fold_block(running, query_heads, key_block, value_block, key_keep):
    row_top, row_total, summed = running
    head_count = query_heads.shape[1]
    key_heads = key_block.reshape(key_block.shape[0], head_count, HEAD_DIM)
    value_heads = value_block.reshape(value_block.shape[0], head_count, HEAD_DIM)
    scores = jnp.einsum("qhd,khd->hqk", query_heads, key_heads, preferred_element_type=jnp.float32)
    scores = scores * (1.0 / math.sqrt(HEAD_DIM))
    scores = jnp.where(key_keep[None, None, :], scores, MASKED)
    new_top = jnp.maximum(row_top, jnp.max(scores, axis=-1))
    scale_down = jnp.exp(row_top - new_top)
    exp_terms = jnp.where(key_keep[None, None, :], jnp.exp(scores - new_top[:, :, None]), 0.0)
    row_total = row_total * scale_down + jnp.sum(exp_terms, axis=-1)
    weights = exp_terms.astype(jnp.bfloat16)
    summed = summed * scale_down[:, :, None] + jnp.einsum(
        "hqk,khd->hqd", weights, value_heads, preferred_element_type=jnp.float32
    )
    return (new_top, row_total, summed)


def window_kernel(blocks, carry_in, finish, q_ref, *refs):
    block_count = len(blocks)
    source_refs = refs[:block_count]
    keep_refs = refs[block_count : 2 * block_count]
    rest = refs[2 * block_count :]
    lane_width, tokens = q_ref.shape
    head_count = lane_width // HEAD_DIM
    keeps = [
        jnp.broadcast_to(keep_refs[b][...], (keep_refs[b].shape[0], tokens)) > 0.5 for b in range(block_count)
    ]
    for h in range(head_count):
        lanes = slice(h * HEAD_DIM, (h + 1) * HEAD_DIM)
        query_t = q_ref[lanes, :]
        scores, value_tiles = [], []
        for b, (pair_form, key_at, value_at) in enumerate(blocks):
            if pair_form:
                key_tile = source_refs[b][key_at, :, lanes]
                value_tile = source_refs[b][value_at, :, lanes]
            else:
                key_tile = source_refs[b][:, (key_at + h) * HEAD_DIM : (key_at + h + 1) * HEAD_DIM]
                value_tile = source_refs[b][:, (value_at + h) * HEAD_DIM : (value_at + h + 1) * HEAD_DIM]
            s = jnp.dot(key_tile, query_t, preferred_element_type=jnp.float32)
            s = s * (1.0 / math.sqrt(HEAD_DIM))
            scores.append(jnp.where(keeps[b], s, MASKED))
            value_tiles.append(value_tile)
        top = scores[0].max(axis=0, keepdims=True)
        for s in scores[1:]:
            top = jnp.maximum(top, s.max(axis=0, keepdims=True))
        if carry_in:
            top_in = rest[0][h : h + 1, :]
            top = jnp.maximum(top, top_in)
            scale_down = jnp.exp(top_in - top)
            total = rest[0][head_count + h : head_count + h + 1, :] * scale_down
            summed = rest[1][lanes, :] * scale_down
        else:
            total = jnp.zeros_like(top)
            summed = None
        for b in range(block_count):
            terms = jnp.exp(scores[b] - top)
            total = total + terms.sum(axis=0, keepdims=True)
            part = lax.dot_general(
                value_tiles[b],
                terms.astype(jnp.bfloat16),
                (((0,), (0,)), ((), ())),
                preferred_element_type=jnp.float32,
            )
            summed = part if summed is None else summed + part
        outs = rest[2:] if carry_in else rest
        if finish:
            outs[0][:, lanes] = jnp.transpose(summed / total).astype(outs[0].dtype)
        else:
            outs[0][h : h + 1, :] = top
            outs[0][head_count + h : head_count + h + 1, :] = total
            outs[1][lanes, :] = summed


def window_attention(query_t, blocks, carry=None, finish=True):
    lane_width, tokens = query_t.shape
    head_count = lane_width // HEAD_DIM
    layout, sources, keeps = [], [], []
    key_total = 0
    for source, key_at, value_at, keep in blocks:
        key_total += keep.shape[0]
        layout.append((source.ndim == 3, key_at, value_at))
        sources.append(source)
        keeps.append(keep)
    stat_rows = -(-2 * head_count // 8) * 8
    stat_shape = jax.ShapeDtypeStruct((stat_rows, tokens), jnp.float32)
    if finish:
        out_shape = jax.ShapeDtypeStruct((tokens, lane_width), jnp.bfloat16)
        out_specs = pl.BlockSpec(memory_space=pltpu.VMEM)
    else:
        out_shape = (stat_shape, jax.ShapeDtypeStruct((lane_width, tokens), jnp.float32))
        out_specs = tuple(pl.BlockSpec(memory_space=pltpu.VMEM) for _ in range(2))
    carry_args = () if carry is None else tuple(carry)
    operand_count = 1 + 2 * len(blocks) + len(carry_args)
    flops = 4 * tokens * key_total * lane_width
    moved = 2 * (2 * tokens * lane_width + 2 * key_total * lane_width) + 4 * 2 * tokens * (lane_width + 8)
    return pl.pallas_call(
        functools.partial(window_kernel, tuple(layout), carry is not None, finish),
        out_shape=out_shape,
        in_specs=[pl.BlockSpec(memory_space=pltpu.VMEM)] * operand_count,
        out_specs=out_specs,
        cost_estimate=pl.CostEstimate(
            flops=flops, transcendentals=tokens * key_total * head_count, bytes_accessed=moved
        ),
    )(query_t, *sources, *keeps, *carry_args)


def text_pieces(text_keys, text_values, text_mask, group_count, lane_width):
    count = lax.axis_size("tile")
    rows = text_keys.shape[0]
    flags = jnp.broadcast_to(text_mask.astype(jnp.bfloat16)[:, None], (rows, 128))
    per_group = jnp.stack(
        [
            jnp.concatenate(
                [
                    text_keys[:, g * lane_width : (g + 1) * lane_width],
                    text_values[:, g * lane_width : (g + 1) * lane_width],
                    flags,
                ],
                axis=1,
            )
            for g in range(group_count)
        ]
    )
    outgoing = jnp.tile(per_group, (count // group_count, 1, 1)).reshape(count * rows, 2 * lane_width + 128)
    got = lax.all_to_all(outgoing, "tile", 0, 0, tiled=True)
    return got, got[:, 2 * lane_width] > 0.5


def shards(queries, keys, values, text_keys, text_values, text_mask):
    tokens = queries.shape[1]
    lane_width = queries.shape[2]
    head_count = lane_width // HEAD_DIM
    query_heads = queries[0].reshape(tokens, head_count, HEAD_DIM)
    group_count = HEAD_GROUPS
    tiles_all = lax.axis_size("tile") // group_count
    grid_w = min(4, tiles_all)
    grid_h = min(4, tiles_all // grid_w)
    grid_f = tiles_all // (grid_w * grid_h)
    frames_valid = grid_f * TS - TS // 4
    my_index = lax.axis_index("tile")
    tile_id = my_index // group_count
    head_group = my_index % group_count
    w_pos = tile_id % grid_w
    h_pos = tile_id // grid_w % grid_h
    f_pos = tile_id // (grid_w * grid_h)
    key_rows = tokens
    if grid_f == 1:
        key_rows = min(tokens, frames_valid * TS * TS)
    own_pair = jnp.stack([keys[0, :key_rows], values[0, :key_rows]])
    local_frame = jnp.arange(key_rows, dtype=jnp.int32) // (TS * TS)

    def keep_mask(off_frame, off_height, off_width):
        inside = (
            (f_pos + off_frame >= 0)
            & (f_pos + off_frame < grid_f)
            & (h_pos + off_height >= 0)
            & (h_pos + off_height < grid_h)
            & (w_pos + off_width >= 0)
            & (w_pos + off_width < grid_w)
        )
        return inside & ((f_pos + off_frame) * TS + local_frame < frames_valid)

    running = (
        jnp.full((head_count, tokens), MASKED, jnp.float32),
        jnp.zeros((head_count, tokens), jnp.float32),
        jnp.zeros((head_count, tokens, HEAD_DIM), jnp.float32),
    )
    text_got, text_keep = text_pieces(text_keys, text_values, text_mask, group_count, lane_width)
    width_set = {0: own_pair}
    for off_width in (-1, 1):
        width_set[off_width] = passed_along(own_pair, "tile", -off_width * group_count)
    if grid_h == 1 and grid_f == 1:
        as_row = lambda keep: keep.astype(jnp.float32)[:, None]
        query_t = jnp.transpose(queries[0])
        carry = window_attention(query_t, [(own_pair, 0, 1, as_row(keep_mask(0, 0, 0)))], finish=False)
        carry = window_attention(
            query_t, [(text_got, 0, head_count, as_row(text_keep))], carry=carry, finish=False
        )
        blocks = [(width_set[off_width], 0, 1, as_row(keep_mask(0, 0, off_width))) for off_width in (-1, 1)]
        return window_attention(query_t, blocks, carry=carry)[None]
    piece_keys = text_got[:, :lane_width]
    piece_values = text_got[:, lane_width : 2 * lane_width]
    running = fold_block(running, query_heads, piece_keys, piece_values, text_keep)
    running = fold_block(running, query_heads, own_pair[0], own_pair[1], keep_mask(0, 0, 0))
    width_offsets = sorted(width_set)
    row_stack = jnp.stack([width_set[spot] for spot in width_offsets])
    height_set = {0: row_stack}
    if grid_h > 1:
        for off_height in (-1, 1):
            height_set[off_height] = passed_along(
                shortened(row_stack), "tile", -off_height * grid_w * group_count
            ).astype(row_stack.dtype)
    height_offsets = sorted(height_set)
    slab_stack = jnp.stack([height_set[spot] for spot in height_offsets])

    def fold_slab(state_now, slab_pairs, off_frame):
        for h_slot, off_height in enumerate(height_offsets):
            for w_slot, off_width in enumerate(width_offsets):
                if off_frame == 0 and off_height == 0 and (off_width == 0):
                    continue
                state_now = fold_block(
                    state_now,
                    query_heads,
                    slab_pairs[h_slot, w_slot, 0],
                    slab_pairs[h_slot, w_slot, 1],
                    keep_mask(off_frame, off_height, off_width),
                )
        return state_now

    running = fold_slab(running, slab_stack, 0)
    if grid_f > 1:
        for off_frame in (-1, 1):
            got_slab = passed_along(
                shortened(slab_stack), "tile", -off_frame * grid_h * grid_w * group_count
            ).astype(slab_stack.dtype)
            running = fold_slab(running, got_slab, off_frame)
    row_top, row_total, summed = running
    result = summed / row_total[:, :, None]
    result = jnp.transpose(result, (1, 0, 2)).reshape(tokens, lane_width)
    return result.astype(jnp.bfloat16)[None]


def solution(mesh):
    return jax.shard_map(
        shards,
        mesh=mesh,
        in_specs=(
            P(("req", "tile"), None, None),
            P(("req", "tile"), None, None),
            P(("req", "tile"), None, None),
            P(("req", "tile"), None),
            P(("req", "tile"), None),
            P(("req", "tile")),
        ),
        out_specs=P(("req", "tile"), None, None),
        check_vma=False,
    )
```

```python
import functools
import math

import jax
import jax.numpy as jnp
from jax import lax
from jax.experimental import pallas as pl
from jax.experimental.pallas import tpu as pltpu
from jax.sharding import PartitionSpec as P

TS = 8
HEAD_DIM = 128
HEAD_GROUPS = 4


MASKED = -1e30
EXP2_SCALE = math.log2(math.e) / math.sqrt(HEAD_DIM)


def passed_along(value, axis, steps):
    count = lax.axis_size(axis)
    first, last = (max(0, -steps), min(count, count - steps))
    return lax.ppermute(value, axis, [(source, source + steps) for source in range(first, last)])


def shortened(value):
    return jax.tree.map(lambda a: a.astype(jnp.bfloat16) if a.dtype == jnp.float32 else a, value)


def fold_block(running, query_heads, key_block, value_block, key_keep):
    row_top, row_total, summed = running
    head_count = query_heads.shape[1]
    key_heads = key_block.reshape(key_block.shape[0], head_count, HEAD_DIM)
    value_heads = value_block.reshape(value_block.shape[0], head_count, HEAD_DIM)
    scores = jnp.einsum("qhd,khd->hqk", query_heads, key_heads, preferred_element_type=jnp.float32)
    scores = scores * (1.0 / math.sqrt(HEAD_DIM))
    scores = jnp.where(key_keep[None, None, :], scores, MASKED)
    new_top = jnp.maximum(row_top, jnp.max(scores, axis=-1))
    scale_down = jnp.exp(row_top - new_top)
    exp_terms = jnp.where(key_keep[None, None, :], jnp.exp(scores - new_top[:, :, None]), 0.0)
    row_total = row_total * scale_down + jnp.sum(exp_terms, axis=-1)
    weights = exp_terms.astype(jnp.bfloat16)
    summed = summed * scale_down[:, :, None] + jnp.einsum(
        "hqk,khd->hqd", weights, value_heads, preferred_element_type=jnp.float32
    )
    return (new_top, row_total, summed)


def window_kernel(blocks, carry_in, finish, q_ref, *refs):
    block_count = len(blocks)
    source_refs = refs[:block_count]
    keep_refs = refs[block_count : 2 * block_count]
    rest = refs[2 * block_count :]
    lane_width, tokens = q_ref.shape
    head_count = lane_width // HEAD_DIM
    keeps = [
        jnp.broadcast_to(keep_refs[b][...], (keep_refs[b].shape[0], tokens)) > 0.5 for b in range(block_count)
    ]
    for h in range(head_count):
        lanes = slice(h * HEAD_DIM, (h + 1) * HEAD_DIM)
        query_t = q_ref[lanes, :]
        scores, value_tiles = [], []
        for b, (pair_form, key_at, value_at) in enumerate(blocks):
            if pair_form:
                key_tile = source_refs[b][key_at, :, lanes]
                value_tile = source_refs[b][value_at, :, lanes]
            else:
                key_tile = source_refs[b][:, (key_at + h) * HEAD_DIM : (key_at + h + 1) * HEAD_DIM]
                value_tile = source_refs[b][:, (value_at + h) * HEAD_DIM : (value_at + h + 1) * HEAD_DIM]
            s = jnp.dot(key_tile, query_t, preferred_element_type=jnp.float32)
            scores.append(jnp.where(keeps[b], s, MASKED))
            value_tiles.append(value_tile)
        top = scores[0].max(axis=0, keepdims=True)
        for s in scores[1:]:
            top = jnp.maximum(top, s.max(axis=0, keepdims=True))
        if carry_in:
            top_in = rest[0][h : h + 1, :]
            top = jnp.maximum(top, top_in)
            scale_down = jnp.exp2((top_in - top) * EXP2_SCALE)
            total = rest[0][head_count + h : head_count + h + 1, :] * scale_down
            summed = rest[1][lanes, :] * scale_down
        else:
            total = jnp.zeros_like(top)
            summed = None
        for b in range(block_count):
            terms = jnp.exp2((scores[b] - top) * EXP2_SCALE)
            total = total + terms.sum(axis=0, keepdims=True)
            part = lax.dot_general(
                value_tiles[b],
                terms.astype(jnp.bfloat16),
                (((0,), (0,)), ((), ())),
                preferred_element_type=jnp.float32,
            )
            summed = part if summed is None else summed + part
        outs = rest[2:] if carry_in else rest
        if finish:
            outs[0][:, lanes] = jnp.transpose(summed / total).astype(outs[0].dtype)
        else:
            outs[0][h : h + 1, :] = top
            outs[0][head_count + h : head_count + h + 1, :] = total
            outs[1][lanes, :] = summed


def window_attention(query_t, blocks, carry=None, finish=True):
    lane_width, tokens = query_t.shape
    head_count = lane_width // HEAD_DIM
    layout, sources, keeps = [], [], []
    key_total = 0
    for source, key_at, value_at, keep in blocks:
        key_total += keep.shape[0]
        layout.append((source.ndim == 3, key_at, value_at))
        sources.append(source)
        keeps.append(keep)
    stat_rows = -(-2 * head_count // 8) * 8
    stat_shape = jax.ShapeDtypeStruct((stat_rows, tokens), jnp.float32)
    if finish:
        out_shape = jax.ShapeDtypeStruct((tokens, lane_width), jnp.bfloat16)
        out_specs = pl.BlockSpec(memory_space=pltpu.VMEM)
    else:
        out_shape = (stat_shape, jax.ShapeDtypeStruct((lane_width, tokens), jnp.float32))
        out_specs = tuple(pl.BlockSpec(memory_space=pltpu.VMEM) for _ in range(2))
    carry_args = () if carry is None else tuple(carry)
    operand_count = 1 + 2 * len(blocks) + len(carry_args)
    flops = 4 * tokens * key_total * lane_width
    moved = 2 * (2 * tokens * lane_width + 2 * key_total * lane_width) + 4 * 2 * tokens * (lane_width + 8)
    return pl.pallas_call(
        functools.partial(window_kernel, tuple(layout), carry is not None, finish),
        out_shape=out_shape,
        in_specs=[pl.BlockSpec(memory_space=pltpu.VMEM)] * operand_count,
        out_specs=out_specs,
        cost_estimate=pl.CostEstimate(
            flops=flops, transcendentals=tokens * key_total * head_count, bytes_accessed=moved
        ),
    )(query_t, *sources, *keeps, *carry_args)


def text_pieces(text_keys, text_values, text_mask, group_count, lane_width):
    count = lax.axis_size("tile")
    rows = text_keys.shape[0]
    flags = jnp.broadcast_to(text_mask.astype(jnp.bfloat16)[:, None], (rows, 128))
    per_group = jnp.stack(
        [
            jnp.concatenate(
                [
                    text_keys[:, g * lane_width : (g + 1) * lane_width],
                    text_values[:, g * lane_width : (g + 1) * lane_width],
                    flags,
                ],
                axis=1,
            )
            for g in range(group_count)
        ]
    )
    outgoing = jnp.tile(per_group, (count // group_count, 1, 1)).reshape(count * rows, 2 * lane_width + 128)
    got = lax.all_to_all(outgoing, "tile", 0, 0, tiled=True)
    return got, got[:, 2 * lane_width] > 0.5


def shards(queries, keys, values, text_keys, text_values, text_mask):
    tokens = queries.shape[1]
    lane_width = queries.shape[2]
    head_count = lane_width // HEAD_DIM
    query_heads = queries[0].reshape(tokens, head_count, HEAD_DIM)
    group_count = HEAD_GROUPS
    tiles_all = lax.axis_size("tile") // group_count
    grid_w = min(4, tiles_all)
    grid_h = min(4, tiles_all // grid_w)
    grid_f = tiles_all // (grid_w * grid_h)
    frames_valid = grid_f * TS - TS // 4
    my_index = lax.axis_index("tile")
    tile_id = my_index // group_count
    head_group = my_index % group_count
    w_pos = tile_id % grid_w
    h_pos = tile_id // grid_w % grid_h
    f_pos = tile_id // (grid_w * grid_h)
    key_rows = tokens
    if grid_f == 1:
        key_rows = min(tokens, frames_valid * TS * TS)
    own_pair = jnp.stack([keys[0, :key_rows], values[0, :key_rows]])
    local_frame = jnp.arange(key_rows, dtype=jnp.int32) // (TS * TS)

    def keep_mask(off_frame, off_height, off_width):
        inside = (
            (f_pos + off_frame >= 0)
            & (f_pos + off_frame < grid_f)
            & (h_pos + off_height >= 0)
            & (h_pos + off_height < grid_h)
            & (w_pos + off_width >= 0)
            & (w_pos + off_width < grid_w)
        )
        return inside & ((f_pos + off_frame) * TS + local_frame < frames_valid)

    running = (
        jnp.full((head_count, tokens), MASKED, jnp.float32),
        jnp.zeros((head_count, tokens), jnp.float32),
        jnp.zeros((head_count, tokens, HEAD_DIM), jnp.float32),
    )
    text_got, text_keep = text_pieces(text_keys, text_values, text_mask, group_count, lane_width)
    width_set = {0: own_pair}
    for off_width in (-1, 1):
        width_set[off_width] = passed_along(own_pair, "tile", -off_width * group_count)
    if grid_h == 1 and grid_f == 1:
        as_row = lambda keep: keep.astype(jnp.float32)[:, None]
        query_t = jnp.transpose(queries[0])
        carry = window_attention(query_t, [(own_pair, 0, 1, as_row(keep_mask(0, 0, 0)))], finish=False)
        carry = window_attention(
            query_t, [(text_got, 0, head_count, as_row(text_keep))], carry=carry, finish=False
        )
        blocks = [(width_set[off_width], 0, 1, as_row(keep_mask(0, 0, off_width))) for off_width in (-1, 1)]
        return window_attention(query_t, blocks, carry=carry)[None]
    piece_keys = text_got[:, :lane_width]
    piece_values = text_got[:, lane_width : 2 * lane_width]
    running = fold_block(running, query_heads, piece_keys, piece_values, text_keep)
    running = fold_block(running, query_heads, own_pair[0], own_pair[1], keep_mask(0, 0, 0))
    width_offsets = sorted(width_set)
    row_stack = jnp.stack([width_set[spot] for spot in width_offsets])
    height_set = {0: row_stack}
    if grid_h > 1:
        for off_height in (-1, 1):
            height_set[off_height] = passed_along(
                shortened(row_stack), "tile", -off_height * grid_w * group_count
            ).astype(row_stack.dtype)
    height_offsets = sorted(height_set)
    slab_stack = jnp.stack([height_set[spot] for spot in height_offsets])

    def fold_slab(state_now, slab_pairs, off_frame):
        for h_slot, off_height in enumerate(height_offsets):
            for w_slot, off_width in enumerate(width_offsets):
                if off_frame == 0 and off_height == 0 and (off_width == 0):
                    continue
                state_now = fold_block(
                    state_now,
                    query_heads,
                    slab_pairs[h_slot, w_slot, 0],
                    slab_pairs[h_slot, w_slot, 1],
                    keep_mask(off_frame, off_height, off_width),
                )
        return state_now

    running = fold_slab(running, slab_stack, 0)
    if grid_f > 1:
        for off_frame in (-1, 1):
            got_slab = passed_along(
                shortened(slab_stack), "tile", -off_frame * grid_h * grid_w * group_count
            ).astype(slab_stack.dtype)
            running = fold_slab(running, got_slab, off_frame)
    row_top, row_total, summed = running
    result = summed / row_total[:, :, None]
    result = jnp.transpose(result, (1, 0, 2)).reshape(tokens, lane_width)
    return result.astype(jnp.bfloat16)[None]


def solution(mesh):
    return jax.shard_map(
        shards,
        mesh=mesh,
        in_specs=(
            P(("req", "tile"), None, None),
            P(("req", "tile"), None, None),
            P(("req", "tile"), None, None),
            P(("req", "tile"), None),
            P(("req", "tile"), None),
            P(("req", "tile")),
        ),
        out_specs=P(("req", "tile"), None, None),
        check_vma=False,
    )
```

```python
import functools
import math

import jax
import jax.numpy as jnp
from jax import lax
from jax.experimental import pallas as pl
from jax.experimental.pallas import tpu as pltpu
from jax.sharding import PartitionSpec as P

TS = 8
HEAD_DIM = 128
HEAD_GROUPS = 4


MASKED = -1e30
EXP2_SCALE = math.log2(math.e) / math.sqrt(HEAD_DIM)


def passed_along(value, axis, steps):
    count = lax.axis_size(axis)
    first, last = (max(0, -steps), min(count, count - steps))
    return lax.ppermute(value, axis, [(source, source + steps) for source in range(first, last)])


def shortened(value):
    return jax.tree.map(lambda a: a.astype(jnp.bfloat16) if a.dtype == jnp.float32 else a, value)


def fold_block(running, query_heads, key_block, value_block, key_keep):
    row_top, row_total, summed = running
    head_count = query_heads.shape[1]
    key_heads = key_block.reshape(key_block.shape[0], head_count, HEAD_DIM)
    value_heads = value_block.reshape(value_block.shape[0], head_count, HEAD_DIM)
    scores = jnp.einsum("qhd,khd->hqk", query_heads, key_heads, preferred_element_type=jnp.float32)
    scores = scores * (1.0 / math.sqrt(HEAD_DIM))
    scores = jnp.where(key_keep[None, None, :], scores, MASKED)
    new_top = jnp.maximum(row_top, jnp.max(scores, axis=-1))
    scale_down = jnp.exp(row_top - new_top)
    exp_terms = jnp.where(key_keep[None, None, :], jnp.exp(scores - new_top[:, :, None]), 0.0)
    row_total = row_total * scale_down + jnp.sum(exp_terms, axis=-1)
    weights = exp_terms.astype(jnp.bfloat16)
    summed = summed * scale_down[:, :, None] + jnp.einsum(
        "hqk,khd->hqd", weights, value_heads, preferred_element_type=jnp.float32
    )
    return (new_top, row_total, summed)


def window_kernel(blocks, carry_in, finish, q_any, *refs):
    block_count = len(blocks)
    source_anys = refs[:block_count]
    keep_refs = refs[block_count : 2 * block_count]
    rest = refs[2 * block_count :]
    carry_anys = rest[:2] if carry_in else ()
    rest = rest[2:] if carry_in else rest
    out_count = 1 if finish else 2
    outs = rest[:out_count]
    rest = rest[out_count:]
    q_ref = rest[0]
    source_refs = rest[1 : 1 + block_count]
    carry_refs = rest[1 + block_count : 1 + block_count + len(carry_anys)]
    sems = rest[-1]
    copies = [pltpu.make_async_copy(q_any, q_ref, sems.at[0])]
    copies += [pltpu.make_async_copy(source_anys[b], source_refs[b], sems.at[1 + b]) for b in range(block_count)]
    copies += [
        pltpu.make_async_copy(carry_anys[i], carry_refs[i], sems.at[1 + block_count + i])
        for i in range(len(carry_anys))
    ]
    for copy in copies:
        copy.start()
    lane_width, tokens = q_ref.shape
    head_count = lane_width // HEAD_DIM
    keeps = [
        jnp.broadcast_to(keep_refs[b][...], (keep_refs[b].shape[0], tokens)) > 0.5 for b in range(block_count)
    ]
    for h in range(head_count):
        lanes = slice(h * HEAD_DIM, (h + 1) * HEAD_DIM)
        if h == 0:
            copies[0].wait()
        query_t = q_ref[lanes, :]
        scores, value_tiles = [], []
        for b, (pair_form, key_at, value_at) in enumerate(blocks):
            if h == 0:
                copies[1 + b].wait()
            if pair_form:
                key_tile = source_refs[b][key_at, :, lanes]
                value_tile = source_refs[b][value_at, :, lanes]
            else:
                key_tile = source_refs[b][:, (key_at + h) * HEAD_DIM : (key_at + h + 1) * HEAD_DIM]
                value_tile = source_refs[b][:, (value_at + h) * HEAD_DIM : (value_at + h + 1) * HEAD_DIM]
            s = jnp.dot(key_tile, query_t, preferred_element_type=jnp.float32)
            scores.append(jnp.where(keeps[b], s, MASKED))
            value_tiles.append(value_tile)
        top = scores[0].max(axis=0, keepdims=True)
        for s in scores[1:]:
            top = jnp.maximum(top, s.max(axis=0, keepdims=True))
        if carry_in:
            if h == 0:
                for copy in copies[1 + block_count :]:
                    copy.wait()
            top_in = carry_refs[0][h : h + 1, :]
            top = jnp.maximum(top, top_in)
            scale_down = jnp.exp2((top_in - top) * EXP2_SCALE)
            total = carry_refs[0][head_count + h : head_count + h + 1, :] * scale_down
            summed = carry_refs[1][lanes, :] * scale_down
        else:
            total = jnp.zeros_like(top)
            summed = None
        for b in range(block_count):
            terms = jnp.exp2((scores[b] - top) * EXP2_SCALE)
            total = total + terms.sum(axis=0, keepdims=True)
            part = lax.dot_general(
                value_tiles[b],
                terms.astype(jnp.bfloat16),
                (((0,), (0,)), ((), ())),
                preferred_element_type=jnp.float32,
            )
            summed = part if summed is None else summed + part
        if finish:
            outs[0][:, lanes] = jnp.transpose(summed / total).astype(outs[0].dtype)
        else:
            outs[0][h : h + 1, :] = top
            outs[0][head_count + h : head_count + h + 1, :] = total
            outs[1][lanes, :] = summed


def window_attention(query_t, blocks, carry=None, finish=True):
    lane_width, tokens = query_t.shape
    head_count = lane_width // HEAD_DIM
    layout, sources, keeps = [], [], []
    key_total = 0
    for source, key_at, value_at, keep in blocks:
        key_total += keep.shape[0]
        layout.append((source.ndim == 3, key_at, value_at))
        sources.append(source)
        keeps.append(keep)
    stat_rows = -(-2 * head_count // 8) * 8
    stat_shape = jax.ShapeDtypeStruct((stat_rows, tokens), jnp.float32)
    if finish:
        out_shape = jax.ShapeDtypeStruct((tokens, lane_width), jnp.bfloat16)
        out_specs = pl.BlockSpec(memory_space=pltpu.VMEM)
    else:
        out_shape = (stat_shape, jax.ShapeDtypeStruct((lane_width, tokens), jnp.float32))
        out_specs = tuple(pl.BlockSpec(memory_space=pltpu.VMEM) for _ in range(2))
    carry_args = () if carry is None else tuple(carry)
    any_spec = pl.BlockSpec(memory_space=pl.ANY)
    vmem_spec = pl.BlockSpec(memory_space=pltpu.VMEM)
    in_specs = [any_spec] * (1 + len(sources)) + [vmem_spec] * len(keeps) + [any_spec] * len(carry_args)
    scratch = [pltpu.VMEM(query_t.shape, query_t.dtype)]
    scratch += [pltpu.VMEM(s.shape, s.dtype) for s in sources]
    scratch += [pltpu.VMEM(c.shape, c.dtype) for c in carry_args]
    scratch += [pltpu.SemaphoreType.DMA((1 + len(sources) + len(carry_args),))]
    flops = 4 * tokens * key_total * lane_width
    moved = 2 * (2 * tokens * lane_width + 2 * key_total * lane_width) + 4 * 2 * tokens * (lane_width + 8)
    return pl.pallas_call(
        functools.partial(window_kernel, tuple(layout), carry is not None, finish),
        out_shape=out_shape,
        in_specs=in_specs,
        out_specs=out_specs,
        scratch_shapes=scratch,
        cost_estimate=pl.CostEstimate(
            flops=flops, transcendentals=tokens * key_total * head_count, bytes_accessed=moved
        ),
    )(query_t, *sources, *keeps, *carry_args)


def text_pieces(text_keys, text_values, text_mask, group_count, lane_width):
    count = lax.axis_size("tile")
    rows = text_keys.shape[0]
    flags = jnp.broadcast_to(text_mask.astype(jnp.bfloat16)[:, None], (rows, 128))
    per_group = jnp.stack(
        [
            jnp.concatenate(
                [
                    text_keys[:, g * lane_width : (g + 1) * lane_width],
                    text_values[:, g * lane_width : (g + 1) * lane_width],
                    flags,
                ],
                axis=1,
            )
            for g in range(group_count)
        ]
    )
    outgoing = jnp.tile(per_group, (count // group_count, 1, 1)).reshape(count * rows, 2 * lane_width + 128)
    got = lax.all_to_all(outgoing, "tile", 0, 0, tiled=True)
    return got, got[:, 2 * lane_width] > 0.5


def shards(queries, keys, values, text_keys, text_values, text_mask):
    tokens = queries.shape[1]
    lane_width = queries.shape[2]
    head_count = lane_width // HEAD_DIM
    query_heads = queries[0].reshape(tokens, head_count, HEAD_DIM)
    group_count = HEAD_GROUPS
    tiles_all = lax.axis_size("tile") // group_count
    grid_w = min(4, tiles_all)
    grid_h = min(4, tiles_all // grid_w)
    grid_f = tiles_all // (grid_w * grid_h)
    frames_valid = grid_f * TS - TS // 4
    my_index = lax.axis_index("tile")
    tile_id = my_index // group_count
    head_group = my_index % group_count
    w_pos = tile_id % grid_w
    h_pos = tile_id // grid_w % grid_h
    f_pos = tile_id // (grid_w * grid_h)
    key_rows = tokens
    if grid_f == 1:
        key_rows = min(tokens, frames_valid * TS * TS)
    own_pair = jnp.stack([keys[0, :key_rows], values[0, :key_rows]])
    local_frame = jnp.arange(key_rows, dtype=jnp.int32) // (TS * TS)

    def keep_mask(off_frame, off_height, off_width):
        inside = (
            (f_pos + off_frame >= 0)
            & (f_pos + off_frame < grid_f)
            & (h_pos + off_height >= 0)
            & (h_pos + off_height < grid_h)
            & (w_pos + off_width >= 0)
            & (w_pos + off_width < grid_w)
        )
        return inside & ((f_pos + off_frame) * TS + local_frame < frames_valid)

    running = (
        jnp.full((head_count, tokens), MASKED, jnp.float32),
        jnp.zeros((head_count, tokens), jnp.float32),
        jnp.zeros((head_count, tokens, HEAD_DIM), jnp.float32),
    )
    text_got, text_keep = text_pieces(text_keys, text_values, text_mask, group_count, lane_width)
    width_set = {0: own_pair}
    for off_width in (-1, 1):
        width_set[off_width] = passed_along(own_pair, "tile", -off_width * group_count)
    if grid_h == 1 and grid_f == 1:
        as_row = lambda keep: keep.astype(jnp.float32)[:, None]
        query_t = jnp.transpose(queries[0])
        carry = window_attention(query_t, [(own_pair, 0, 1, as_row(keep_mask(0, 0, 0)))], finish=False)
        carry = window_attention(
            query_t, [(text_got, 0, head_count, as_row(text_keep))], carry=carry, finish=False
        )
        blocks = [(width_set[off_width], 0, 1, as_row(keep_mask(0, 0, off_width))) for off_width in (-1, 1)]
        return window_attention(query_t, blocks, carry=carry)[None]
    piece_keys = text_got[:, :lane_width]
    piece_values = text_got[:, lane_width : 2 * lane_width]
    running = fold_block(running, query_heads, piece_keys, piece_values, text_keep)
    running = fold_block(running, query_heads, own_pair[0], own_pair[1], keep_mask(0, 0, 0))
    width_offsets = sorted(width_set)
    row_stack = jnp.stack([width_set[spot] for spot in width_offsets])
    height_set = {0: row_stack}
    if grid_h > 1:
        for off_height in (-1, 1):
            height_set[off_height] = passed_along(
                shortened(row_stack), "tile", -off_height * grid_w * group_count
            ).astype(row_stack.dtype)
    height_offsets = sorted(height_set)
    slab_stack = jnp.stack([height_set[spot] for spot in height_offsets])

    def fold_slab(state_now, slab_pairs, off_frame):
        for h_slot, off_height in enumerate(height_offsets):
            for w_slot, off_width in enumerate(width_offsets):
                if off_frame == 0 and off_height == 0 and (off_width == 0):
                    continue
                state_now = fold_block(
                    state_now,
                    query_heads,
                    slab_pairs[h_slot, w_slot, 0],
                    slab_pairs[h_slot, w_slot, 1],
                    keep_mask(off_frame, off_height, off_width),
                )
        return state_now

    running = fold_slab(running, slab_stack, 0)
    if grid_f > 1:
        for off_frame in (-1, 1):
            got_slab = passed_along(
                shortened(slab_stack), "tile", -off_frame * grid_h * grid_w * group_count
            ).astype(slab_stack.dtype)
            running = fold_slab(running, got_slab, off_frame)
    row_top, row_total, summed = running
    result = summed / row_total[:, :, None]
    result = jnp.transpose(result, (1, 0, 2)).reshape(tokens, lane_width)
    return result.astype(jnp.bfloat16)[None]


def solution(mesh):
    return jax.shard_map(
        shards,
        mesh=mesh,
        in_specs=(
            P(("req", "tile"), None, None),
            P(("req", "tile"), None, None),
            P(("req", "tile"), None, None),
            P(("req", "tile"), None),
            P(("req", "tile"), None),
            P(("req", "tile")),
        ),
        out_specs=P(("req", "tile"), None, None),
        check_vma=False,
    )
```

```python
import functools
import math

import jax
import jax.numpy as jnp
from jax import lax
from jax.experimental import pallas as pl
from jax.experimental.pallas import tpu as pltpu
from jax.sharding import PartitionSpec as P

TS = 8
HEAD_DIM = 128
HEAD_GROUPS = 4


MASKED = -1e30
EXP2_SCALE = math.log2(math.e) / math.sqrt(HEAD_DIM)


def passed_along(value, axis, steps):
    count = lax.axis_size(axis)
    first, last = (max(0, -steps), min(count, count - steps))
    return lax.ppermute(value, axis, [(source, source + steps) for source in range(first, last)])


def shortened(value):
    return jax.tree.map(lambda a: a.astype(jnp.bfloat16) if a.dtype == jnp.float32 else a, value)


def fold_block(running, query_heads, key_block, value_block, key_keep):
    row_top, row_total, summed = running
    head_count = query_heads.shape[1]
    key_heads = key_block.reshape(key_block.shape[0], head_count, HEAD_DIM)
    value_heads = value_block.reshape(value_block.shape[0], head_count, HEAD_DIM)
    scores = jnp.einsum("qhd,khd->hqk", query_heads, key_heads, preferred_element_type=jnp.float32)
    scores = scores * (1.0 / math.sqrt(HEAD_DIM))
    scores = jnp.where(key_keep[None, None, :], scores, MASKED)
    new_top = jnp.maximum(row_top, jnp.max(scores, axis=-1))
    scale_down = jnp.exp(row_top - new_top)
    exp_terms = jnp.where(key_keep[None, None, :], jnp.exp(scores - new_top[:, :, None]), 0.0)
    row_total = row_total * scale_down + jnp.sum(exp_terms, axis=-1)
    weights = exp_terms.astype(jnp.bfloat16)
    summed = summed * scale_down[:, :, None] + jnp.einsum(
        "hqk,khd->hqd", weights, value_heads, preferred_element_type=jnp.float32
    )
    return (new_top, row_total, summed)


def window_kernel(blocks, carry_in, finish, q_ref, *refs):
    block_count = len(blocks)
    source_refs = refs[:block_count]
    keep_refs = refs[block_count : 2 * block_count]
    rest = refs[2 * block_count :]
    lane_width, tokens = q_ref.shape
    head_count = lane_width // HEAD_DIM
    keeps = [
        jnp.broadcast_to(keep_refs[b][...], (keep_refs[b].shape[0], tokens)) > 0.5 for b in range(block_count)
    ]
    for h in range(head_count):
        lanes = slice(h * HEAD_DIM, (h + 1) * HEAD_DIM)
        query_t = q_ref[lanes, :]
        scores, value_tiles = [], []
        for b, (pair_form, key_at, value_at) in enumerate(blocks):
            if pair_form:
                key_tile = source_refs[b][key_at, :, lanes]
                value_tile = source_refs[b][value_at, :, lanes]
            else:
                key_tile = source_refs[b][:, (key_at + h) * HEAD_DIM : (key_at + h + 1) * HEAD_DIM]
                value_tile = source_refs[b][:, (value_at + h) * HEAD_DIM : (value_at + h + 1) * HEAD_DIM]
            s = jnp.dot(key_tile, query_t, preferred_element_type=jnp.float32)
            scores.append(jnp.where(keeps[b], s, MASKED))
            value_tiles.append(value_tile)
        top = scores[0].max(axis=0, keepdims=True)
        for s in scores[1:]:
            top = jnp.maximum(top, s.max(axis=0, keepdims=True))
        if carry_in:
            top_in = rest[0][h : h + 1, :]
            top = jnp.maximum(top, top_in)
            scale_down = jnp.exp2((top_in - top) * EXP2_SCALE)
            total = rest[0][head_count + h : head_count + h + 1, :] * scale_down
            summed = rest[1][lanes, :] * scale_down
        else:
            total = jnp.zeros_like(top)
            summed = None
        for b in range(block_count):
            terms = jnp.exp2((scores[b] - top) * EXP2_SCALE)
            total = total + terms.sum(axis=0, keepdims=True)
            part = lax.dot_general(
                value_tiles[b],
                terms.astype(jnp.bfloat16),
                (((0,), (0,)), ((), ())),
                preferred_element_type=jnp.float32,
            )
            summed = part if summed is None else summed + part
        outs = rest[2:] if carry_in else rest
        if finish:
            outs[0][:, lanes] = jnp.transpose(summed / total).astype(outs[0].dtype)
        else:
            outs[0][h : h + 1, :] = top
            outs[0][head_count + h : head_count + h + 1, :] = total
            outs[1][lanes, :] = summed


def window_attention(query_t, blocks, carry=None, finish=True):
    lane_width, tokens = query_t.shape
    head_count = lane_width // HEAD_DIM
    layout, sources, keeps = [], [], []
    key_total = 0
    for source, key_at, value_at, keep in blocks:
        key_total += keep.shape[0]
        layout.append((source.ndim == 3, key_at, value_at))
        sources.append(source)
        keeps.append(keep)
    stat_rows = -(-2 * head_count // 8) * 8
    stat_shape = jax.ShapeDtypeStruct((stat_rows, tokens), jnp.float32)
    if finish:
        out_shape = jax.ShapeDtypeStruct((tokens, lane_width), jnp.bfloat16)
        out_specs = pl.BlockSpec(memory_space=pltpu.VMEM)
    else:
        out_shape = (stat_shape, jax.ShapeDtypeStruct((lane_width, tokens), jnp.float32))
        out_specs = tuple(pl.BlockSpec(memory_space=pltpu.VMEM) for _ in range(2))
    carry_args = () if carry is None else tuple(carry)
    operand_count = 1 + 2 * len(blocks) + len(carry_args)
    flops = 4 * tokens * key_total * lane_width
    moved = 2 * (2 * tokens * lane_width + 2 * key_total * lane_width) + 4 * 2 * tokens * (lane_width + 8)
    return pl.pallas_call(
        functools.partial(window_kernel, tuple(layout), carry is not None, finish),
        out_shape=out_shape,
        in_specs=[pl.BlockSpec(memory_space=pltpu.VMEM)] * operand_count,
        out_specs=out_specs,
        cost_estimate=pl.CostEstimate(
            flops=flops, transcendentals=tokens * key_total * head_count, bytes_accessed=moved
        ),
    )(query_t, *[pltpu.with_memory_space_constraint(s, pltpu.VMEM) for s in sources], *keeps, *carry_args)


def text_pieces(text_keys, text_values, text_mask, group_count, lane_width):
    count = lax.axis_size("tile")
    rows = text_keys.shape[0]
    flags = jnp.broadcast_to(text_mask.astype(jnp.bfloat16)[:, None], (rows, 128))
    per_group = jnp.stack(
        [
            jnp.concatenate(
                [
                    text_keys[:, g * lane_width : (g + 1) * lane_width],
                    text_values[:, g * lane_width : (g + 1) * lane_width],
                    flags,
                ],
                axis=1,
            )
            for g in range(group_count)
        ]
    )
    outgoing = jnp.tile(per_group, (count // group_count, 1, 1)).reshape(count * rows, 2 * lane_width + 128)
    got = lax.all_to_all(outgoing, "tile", 0, 0, tiled=True)
    return got, got[:, 2 * lane_width] > 0.5


def shards(queries, keys, values, text_keys, text_values, text_mask):
    tokens = queries.shape[1]
    lane_width = queries.shape[2]
    head_count = lane_width // HEAD_DIM
    query_heads = queries[0].reshape(tokens, head_count, HEAD_DIM)
    group_count = HEAD_GROUPS
    tiles_all = lax.axis_size("tile") // group_count
    grid_w = min(4, tiles_all)
    grid_h = min(4, tiles_all // grid_w)
    grid_f = tiles_all // (grid_w * grid_h)
    frames_valid = grid_f * TS - TS // 4
    my_index = lax.axis_index("tile")
    tile_id = my_index // group_count
    head_group = my_index % group_count
    w_pos = tile_id % grid_w
    h_pos = tile_id // grid_w % grid_h
    f_pos = tile_id // (grid_w * grid_h)
    key_rows = tokens
    if grid_f == 1:
        key_rows = min(tokens, frames_valid * TS * TS)
    own_pair = jnp.stack([keys[0, :key_rows], values[0, :key_rows]])
    local_frame = jnp.arange(key_rows, dtype=jnp.int32) // (TS * TS)

    def keep_mask(off_frame, off_height, off_width):
        inside = (
            (f_pos + off_frame >= 0)
            & (f_pos + off_frame < grid_f)
            & (h_pos + off_height >= 0)
            & (h_pos + off_height < grid_h)
            & (w_pos + off_width >= 0)
            & (w_pos + off_width < grid_w)
        )
        return inside & ((f_pos + off_frame) * TS + local_frame < frames_valid)

    running = (
        jnp.full((head_count, tokens), MASKED, jnp.float32),
        jnp.zeros((head_count, tokens), jnp.float32),
        jnp.zeros((head_count, tokens, HEAD_DIM), jnp.float32),
    )
    text_got, text_keep = text_pieces(text_keys, text_values, text_mask, group_count, lane_width)
    width_set = {0: own_pair}
    for off_width in (-1, 1):
        width_set[off_width] = passed_along(own_pair, "tile", -off_width * group_count)
    if grid_h == 1 and grid_f == 1:
        as_row = lambda keep: keep.astype(jnp.float32)[:, None]
        query_t = jnp.transpose(queries[0])
        carry = window_attention(query_t, [(own_pair, 0, 1, as_row(keep_mask(0, 0, 0)))], finish=False)
        carry = window_attention(
            query_t, [(text_got, 0, head_count, as_row(text_keep))], carry=carry, finish=False
        )
        blocks = [(width_set[off_width], 0, 1, as_row(keep_mask(0, 0, off_width))) for off_width in (-1, 1)]
        return window_attention(query_t, blocks, carry=carry)[None]
    piece_keys = text_got[:, :lane_width]
    piece_values = text_got[:, lane_width : 2 * lane_width]
    running = fold_block(running, query_heads, piece_keys, piece_values, text_keep)
    running = fold_block(running, query_heads, own_pair[0], own_pair[1], keep_mask(0, 0, 0))
    width_offsets = sorted(width_set)
    row_stack = jnp.stack([width_set[spot] for spot in width_offsets])
    height_set = {0: row_stack}
    if grid_h > 1:
        for off_height in (-1, 1):
            height_set[off_height] = passed_along(
                shortened(row_stack), "tile", -off_height * grid_w * group_count
            ).astype(row_stack.dtype)
    height_offsets = sorted(height_set)
    slab_stack = jnp.stack([height_set[spot] for spot in height_offsets])

    def fold_slab(state_now, slab_pairs, off_frame):
        for h_slot, off_height in enumerate(height_offsets):
            for w_slot, off_width in enumerate(width_offsets):
                if off_frame == 0 and off_height == 0 and (off_width == 0):
                    continue
                state_now = fold_block(
                    state_now,
                    query_heads,
                    slab_pairs[h_slot, w_slot, 0],
                    slab_pairs[h_slot, w_slot, 1],
                    keep_mask(off_frame, off_height, off_width),
                )
        return state_now

    running = fold_slab(running, slab_stack, 0)
    if grid_f > 1:
        for off_frame in (-1, 1):
            got_slab = passed_along(
                shortened(slab_stack), "tile", -off_frame * grid_h * grid_w * group_count
            ).astype(slab_stack.dtype)
            running = fold_slab(running, got_slab, off_frame)
    row_top, row_total, summed = running
    result = summed / row_total[:, :, None]
    result = jnp.transpose(result, (1, 0, 2)).reshape(tokens, lane_width)
    return result.astype(jnp.bfloat16)[None]


def solution(mesh):
    return jax.shard_map(
        shards,
        mesh=mesh,
        in_specs=(
            P(("req", "tile"), None, None),
            P(("req", "tile"), None, None),
            P(("req", "tile"), None, None),
            P(("req", "tile"), None),
            P(("req", "tile"), None),
            P(("req", "tile")),
        ),
        out_specs=P(("req", "tile"), None, None),
        check_vma=False,
    )
```

```python
import functools
import math

import jax
import jax.numpy as jnp
from jax import lax
from jax.experimental import pallas as pl
from jax.experimental.pallas import tpu as pltpu
from jax.sharding import PartitionSpec as P

TS = 8
HEAD_DIM = 128
HEAD_GROUPS = 4


MASKED = -1e30
EXP2_SCALE = math.log2(math.e) / math.sqrt(HEAD_DIM)


def passed_along(value, axis, steps):
    count = lax.axis_size(axis)
    first, last = (max(0, -steps), min(count, count - steps))
    return lax.ppermute(value, axis, [(source, source + steps) for source in range(first, last)])


def shortened(value):
    return jax.tree.map(lambda a: a.astype(jnp.bfloat16) if a.dtype == jnp.float32 else a, value)


def fold_block(running, query_heads, key_block, value_block, key_keep):
    row_top, row_total, summed = running
    head_count = query_heads.shape[1]
    key_heads = key_block.reshape(key_block.shape[0], head_count, HEAD_DIM)
    value_heads = value_block.reshape(value_block.shape[0], head_count, HEAD_DIM)
    scores = jnp.einsum("qhd,khd->hqk", query_heads, key_heads, preferred_element_type=jnp.float32)
    scores = scores * (1.0 / math.sqrt(HEAD_DIM))
    scores = jnp.where(key_keep[None, None, :], scores, MASKED)
    new_top = jnp.maximum(row_top, jnp.max(scores, axis=-1))
    scale_down = jnp.exp(row_top - new_top)
    exp_terms = jnp.where(key_keep[None, None, :], jnp.exp(scores - new_top[:, :, None]), 0.0)
    row_total = row_total * scale_down + jnp.sum(exp_terms, axis=-1)
    weights = exp_terms.astype(jnp.bfloat16)
    summed = summed * scale_down[:, :, None] + jnp.einsum(
        "hqk,khd->hqd", weights, value_heads, preferred_element_type=jnp.float32
    )
    return (new_top, row_total, summed)


def window_kernel(blocks, carry_in, finish, q_ref, *refs):
    block_count = len(blocks)
    source_refs = refs[:block_count]
    keep_refs = refs[block_count : 2 * block_count]
    rest = refs[2 * block_count :]
    lane_width, tokens = q_ref.shape
    head_count = lane_width // HEAD_DIM
    keeps = [
        jnp.broadcast_to(keep_refs[b][...], (keep_refs[b].shape[0], tokens)) > 0.5 for b in range(block_count)
    ]
    for h in range(head_count):
        lanes = slice(h * HEAD_DIM, (h + 1) * HEAD_DIM)
        query_t = q_ref[lanes, :]
        scores, value_tiles = [], []
        for b, (pair_form, key_at, value_at) in enumerate(blocks):
            if pair_form:
                key_tile = source_refs[b][key_at, :, lanes]
                value_tile = source_refs[b][value_at, :, lanes]
            else:
                key_tile = source_refs[b][:, (key_at + h) * HEAD_DIM : (key_at + h + 1) * HEAD_DIM]
                value_tile = source_refs[b][:, (value_at + h) * HEAD_DIM : (value_at + h + 1) * HEAD_DIM]
            s = jnp.dot(key_tile, query_t, preferred_element_type=jnp.float32)
            scores.append(jnp.where(keeps[b], s, MASKED))
            value_tiles.append(value_tile)
        top = scores[0].max(axis=0, keepdims=True)
        for s in scores[1:]:
            top = jnp.maximum(top, s.max(axis=0, keepdims=True))
        if carry_in:
            top_in = rest[0][h : h + 1, :]
            top = jnp.maximum(top, top_in)
            scale_down = jnp.exp2((top_in - top) * EXP2_SCALE)
            total = rest[0][head_count + h : head_count + h + 1, :] * scale_down
            summed = rest[1][lanes, :] * scale_down
        else:
            total = jnp.zeros_like(top)
            summed = None
        for b in range(block_count):
            terms = jnp.exp2((scores[b] - top) * EXP2_SCALE)
            total = total + terms.sum(axis=0, keepdims=True)
            part = lax.dot_general(
                value_tiles[b],
                terms.astype(jnp.bfloat16),
                (((0,), (0,)), ((), ())),
                preferred_element_type=jnp.float32,
            )
            summed = part if summed is None else summed + part
        outs = rest[2:] if carry_in else rest
        if finish:
            outs[0][:, lanes] = jnp.transpose(summed / total).astype(outs[0].dtype)
        else:
            outs[0][h : h + 1, :] = top
            outs[0][head_count + h : head_count + h + 1, :] = total
            outs[1][lanes, :] = summed


def window_attention(query_t, blocks, carry=None, finish=True):
    lane_width, tokens = query_t.shape
    head_count = lane_width // HEAD_DIM
    layout, sources, keeps = [], [], []
    key_total = 0
    for source, key_at, value_at, keep in blocks:
        key_total += keep.shape[0]
        layout.append((source.ndim == 3, key_at, value_at))
        sources.append(source)
        keeps.append(keep)
    stat_rows = -(-2 * head_count // 8) * 8
    stat_shape = jax.ShapeDtypeStruct((stat_rows, tokens), jnp.float32)
    if finish:
        out_shape = jax.ShapeDtypeStruct((tokens, lane_width), jnp.bfloat16)
        out_specs = pl.BlockSpec(memory_space=pltpu.VMEM)
    else:
        out_shape = (stat_shape, jax.ShapeDtypeStruct((lane_width, tokens), jnp.float32))
        out_specs = tuple(pl.BlockSpec(memory_space=pltpu.VMEM) for _ in range(2))
    carry_args = () if carry is None else tuple(carry)
    operand_count = 1 + 2 * len(blocks) + len(carry_args)
    flops = 4 * tokens * key_total * lane_width
    moved = 2 * (2 * tokens * lane_width + 2 * key_total * lane_width) + 4 * 2 * tokens * (lane_width + 8)
    return pl.pallas_call(
        functools.partial(window_kernel, tuple(layout), carry is not None, finish),
        out_shape=out_shape,
        in_specs=[pl.BlockSpec(memory_space=pltpu.VMEM)] * operand_count,
        out_specs=out_specs,
        cost_estimate=pl.CostEstimate(
            flops=flops, transcendentals=tokens * key_total * head_count, bytes_accessed=moved
        ),
    )(*[pltpu.with_memory_space_constraint(a, pltpu.VMEM) for a in (query_t, *sources, *keeps)], *carry_args)


def text_pieces(text_keys, text_values, text_mask, group_count, lane_width):
    count = lax.axis_size("tile")
    rows = text_keys.shape[0]
    flags = jnp.broadcast_to(text_mask.astype(jnp.bfloat16)[:, None], (rows, 128))
    per_group = jnp.stack(
        [
            jnp.concatenate(
                [
                    text_keys[:, g * lane_width : (g + 1) * lane_width],
                    text_values[:, g * lane_width : (g + 1) * lane_width],
                    flags,
                ],
                axis=1,
            )
            for g in range(group_count)
        ]
    )
    outgoing = jnp.tile(per_group, (count // group_count, 1, 1)).reshape(count * rows, 2 * lane_width + 128)
    got = lax.all_to_all(outgoing, "tile", 0, 0, tiled=True)
    return got, got[:, 2 * lane_width] > 0.5


def shards(queries, keys, values, text_keys, text_values, text_mask):
    tokens = queries.shape[1]
    lane_width = queries.shape[2]
    head_count = lane_width // HEAD_DIM
    query_heads = queries[0].reshape(tokens, head_count, HEAD_DIM)
    group_count = HEAD_GROUPS
    tiles_all = lax.axis_size("tile") // group_count
    grid_w = min(4, tiles_all)
    grid_h = min(4, tiles_all // grid_w)
    grid_f = tiles_all // (grid_w * grid_h)
    frames_valid = grid_f * TS - TS // 4
    my_index = lax.axis_index("tile")
    tile_id = my_index // group_count
    head_group = my_index % group_count
    w_pos = tile_id % grid_w
    h_pos = tile_id // grid_w % grid_h
    f_pos = tile_id // (grid_w * grid_h)
    key_rows = tokens
    if grid_f == 1:
        key_rows = min(tokens, frames_valid * TS * TS)
    own_pair = jnp.stack([keys[0, :key_rows], values[0, :key_rows]])
    local_frame = jnp.arange(key_rows, dtype=jnp.int32) // (TS * TS)

    def keep_mask(off_frame, off_height, off_width):
        inside = (
            (f_pos + off_frame >= 0)
            & (f_pos + off_frame < grid_f)
            & (h_pos + off_height >= 0)
            & (h_pos + off_height < grid_h)
            & (w_pos + off_width >= 0)
            & (w_pos + off_width < grid_w)
        )
        return inside & ((f_pos + off_frame) * TS + local_frame < frames_valid)

    running = (
        jnp.full((head_count, tokens), MASKED, jnp.float32),
        jnp.zeros((head_count, tokens), jnp.float32),
        jnp.zeros((head_count, tokens, HEAD_DIM), jnp.float32),
    )
    text_got, text_keep = text_pieces(text_keys, text_values, text_mask, group_count, lane_width)
    width_set = {0: own_pair}
    for off_width in (-1, 1):
        width_set[off_width] = passed_along(own_pair, "tile", -off_width * group_count)
    if grid_h == 1 and grid_f == 1:
        as_row = lambda keep: keep.astype(jnp.float32)[:, None]
        query_t = jnp.transpose(queries[0])
        carry = window_attention(query_t, [(own_pair, 0, 1, as_row(keep_mask(0, 0, 0)))], finish=False)
        carry = window_attention(
            query_t, [(text_got, 0, head_count, as_row(text_keep))], carry=carry, finish=False
        )
        blocks = [(width_set[off_width], 0, 1, as_row(keep_mask(0, 0, off_width))) for off_width in (-1, 1)]
        return window_attention(query_t, blocks, carry=carry)[None]
    piece_keys = text_got[:, :lane_width]
    piece_values = text_got[:, lane_width : 2 * lane_width]
    running = fold_block(running, query_heads, piece_keys, piece_values, text_keep)
    running = fold_block(running, query_heads, own_pair[0], own_pair[1], keep_mask(0, 0, 0))
    width_offsets = sorted(width_set)
    row_stack = jnp.stack([width_set[spot] for spot in width_offsets])
    height_set = {0: row_stack}
    if grid_h > 1:
        for off_height in (-1, 1):
            height_set[off_height] = passed_along(
                shortened(row_stack), "tile", -off_height * grid_w * group_count
            ).astype(row_stack.dtype)
    height_offsets = sorted(height_set)
    slab_stack = jnp.stack([height_set[spot] for spot in height_offsets])

    def fold_slab(state_now, slab_pairs, off_frame):
        for h_slot, off_height in enumerate(height_offsets):
            for w_slot, off_width in enumerate(width_offsets):
                if off_frame == 0 and off_height == 0 and (off_width == 0):
                    continue
                state_now = fold_block(
                    state_now,
                    query_heads,
                    slab_pairs[h_slot, w_slot, 0],
                    slab_pairs[h_slot, w_slot, 1],
                    keep_mask(off_frame, off_height, off_width),
                )
        return state_now

    running = fold_slab(running, slab_stack, 0)
    if grid_f > 1:
        for off_frame in (-1, 1):
            got_slab = passed_along(
                shortened(slab_stack), "tile", -off_frame * grid_h * grid_w * group_count
            ).astype(slab_stack.dtype)
            running = fold_slab(running, got_slab, off_frame)
    row_top, row_total, summed = running
    result = summed / row_total[:, :, None]
    result = jnp.transpose(result, (1, 0, 2)).reshape(tokens, lane_width)
    return result.astype(jnp.bfloat16)[None]


def solution(mesh):
    return jax.shard_map(
        shards,
        mesh=mesh,
        in_specs=(
            P(("req", "tile"), None, None),
            P(("req", "tile"), None, None),
            P(("req", "tile"), None, None),
            P(("req", "tile"), None),
            P(("req", "tile"), None),
            P(("req", "tile")),
        ),
        out_specs=P(("req", "tile"), None, None),
        check_vma=False,
    )
```

```python
import functools
import math

import jax
import jax.numpy as jnp
from jax import lax
from jax.experimental import pallas as pl
from jax.experimental.pallas import tpu as pltpu
from jax.sharding import PartitionSpec as P

TS = 8
HEAD_DIM = 128
HEAD_GROUPS = 4


MASKED = -1e30
EXP2_SCALE = math.log2(math.e) / math.sqrt(HEAD_DIM)


def passed_along(value, axis, steps):
    count = lax.axis_size(axis)
    first, last = (max(0, -steps), min(count, count - steps))
    return lax.ppermute(value, axis, [(source, source + steps) for source in range(first, last)])


def shortened(value):
    return jax.tree.map(lambda a: a.astype(jnp.bfloat16) if a.dtype == jnp.float32 else a, value)


def fold_block(running, query_heads, key_block, value_block, key_keep):
    row_top, row_total, summed = running
    head_count = query_heads.shape[1]
    key_heads = key_block.reshape(key_block.shape[0], head_count, HEAD_DIM)
    value_heads = value_block.reshape(value_block.shape[0], head_count, HEAD_DIM)
    scores = jnp.einsum("qhd,khd->hqk", query_heads, key_heads, preferred_element_type=jnp.float32)
    scores = scores * (1.0 / math.sqrt(HEAD_DIM))
    scores = jnp.where(key_keep[None, None, :], scores, MASKED)
    new_top = jnp.maximum(row_top, jnp.max(scores, axis=-1))
    scale_down = jnp.exp(row_top - new_top)
    exp_terms = jnp.where(key_keep[None, None, :], jnp.exp(scores - new_top[:, :, None]), 0.0)
    row_total = row_total * scale_down + jnp.sum(exp_terms, axis=-1)
    weights = exp_terms.astype(jnp.bfloat16)
    summed = summed * scale_down[:, :, None] + jnp.einsum(
        "hqk,khd->hqd", weights, value_heads, preferred_element_type=jnp.float32
    )
    return (new_top, row_total, summed)


def window_kernel(blocks, carry_in, finish, q_ref, *refs):
    block_count = len(blocks)
    source_refs = refs[:block_count]
    keep_refs = refs[block_count : 2 * block_count]
    rest = refs[2 * block_count :]
    lane_width, tokens = q_ref.shape
    head_count = lane_width // HEAD_DIM
    keeps = [
        jnp.broadcast_to(keep_refs[b][...], (keep_refs[b].shape[0], tokens)) > 0.5 for b in range(block_count)
    ]
    for h in range(head_count):
        lanes = slice(h * HEAD_DIM, (h + 1) * HEAD_DIM)
        query_t = q_ref[lanes, :]
        scores, value_tiles = [], []
        for b, (pair_form, key_at, value_at) in enumerate(blocks):
            if pair_form:
                key_tile = source_refs[b][key_at, :, lanes]
                value_tile = source_refs[b][value_at, :, lanes]
            else:
                key_tile = source_refs[b][:, (key_at + h) * HEAD_DIM : (key_at + h + 1) * HEAD_DIM]
                value_tile = source_refs[b][:, (value_at + h) * HEAD_DIM : (value_at + h + 1) * HEAD_DIM]
            s = jnp.dot(key_tile, query_t, preferred_element_type=jnp.float32)
            scores.append(jnp.where(keeps[b], s, MASKED))
            value_tiles.append(value_tile)
        top = scores[0].max(axis=0, keepdims=True)
        for s in scores[1:]:
            top = jnp.maximum(top, s.max(axis=0, keepdims=True))
        if carry_in:
            top_in = rest[0][h : h + 1, :]
            top = jnp.maximum(top, top_in)
            scale_down = jnp.exp2((top_in - top) * EXP2_SCALE)
            total = rest[0][head_count + h : head_count + h + 1, :] * scale_down
            summed = rest[1][lanes, :] * scale_down
        else:
            total = jnp.zeros_like(top)
            summed = None
        for b in range(block_count):
            terms = jnp.exp2((scores[b] - top) * EXP2_SCALE)
            total = total + terms.sum(axis=0, keepdims=True)
            part = lax.dot_general(
                value_tiles[b],
                terms.astype(jnp.bfloat16),
                (((0,), (0,)), ((), ())),
                preferred_element_type=jnp.float32,
            )
            summed = part if summed is None else summed + part
        outs = rest[2:] if carry_in else rest
        if finish:
            outs[0][:, lanes] = jnp.transpose(summed / total).astype(outs[0].dtype)
        else:
            outs[0][h : h + 1, :] = top
            outs[0][head_count + h : head_count + h + 1, :] = total
            outs[1][lanes, :] = summed


def window_attention(query_t, blocks, carry=None, finish=True):
    lane_width, tokens = query_t.shape
    head_count = lane_width // HEAD_DIM
    layout, sources, keeps = [], [], []
    key_total = 0
    for source, key_at, value_at, keep in blocks:
        key_total += keep.shape[0]
        layout.append((source.ndim == 3, key_at, value_at))
        sources.append(source)
        keeps.append(keep)
    stat_rows = -(-2 * head_count // 8) * 8
    stat_shape = jax.ShapeDtypeStruct((stat_rows, tokens), jnp.float32)
    if finish:
        out_shape = jax.ShapeDtypeStruct((tokens, lane_width), jnp.bfloat16)
        out_specs = pl.BlockSpec(memory_space=pltpu.VMEM)
    else:
        out_shape = (
            pltpu.VMEM(stat_shape.shape, stat_shape.dtype),
            pltpu.VMEM((lane_width, tokens), jnp.float32),
        )
        out_specs = tuple(pl.BlockSpec(memory_space=pltpu.VMEM) for _ in range(2))
    carry_args = () if carry is None else tuple(carry)
    operand_count = 1 + 2 * len(blocks) + len(carry_args)
    flops = 4 * tokens * key_total * lane_width
    moved = 2 * (2 * tokens * lane_width + 2 * key_total * lane_width) + 4 * 2 * tokens * (lane_width + 8)
    return pl.pallas_call(
        functools.partial(window_kernel, tuple(layout), carry is not None, finish),
        out_shape=out_shape,
        in_specs=[pl.BlockSpec(memory_space=pltpu.VMEM)] * operand_count,
        out_specs=out_specs,
        cost_estimate=pl.CostEstimate(
            flops=flops, transcendentals=tokens * key_total * head_count, bytes_accessed=moved
        ),
        compiler_params=pltpu.CompilerParams(vmem_limit_bytes=16 * 1024 * 1024),
    )(*[pltpu.with_memory_space_constraint(a, pltpu.VMEM) for a in (query_t, *sources, *keeps, *carry_args)])


def text_pieces(text_keys, text_values, text_mask, group_count, lane_width):
    count = lax.axis_size("tile")
    rows = text_keys.shape[0]
    flags = jnp.broadcast_to(text_mask.astype(jnp.bfloat16)[:, None], (rows, 128))
    per_group = jnp.stack(
        [
            jnp.concatenate(
                [
                    text_keys[:, g * lane_width : (g + 1) * lane_width],
                    text_values[:, g * lane_width : (g + 1) * lane_width],
                    flags,
                ],
                axis=1,
            )
            for g in range(group_count)
        ]
    )
    outgoing = jnp.tile(per_group, (count // group_count, 1, 1)).reshape(count * rows, 2 * lane_width + 128)
    got = lax.all_to_all(outgoing, "tile", 0, 0, tiled=True)
    return got, got[:, 2 * lane_width] > 0.5


def shards(queries, keys, values, text_keys, text_values, text_mask):
    tokens = queries.shape[1]
    lane_width = queries.shape[2]
    head_count = lane_width // HEAD_DIM
    query_heads = queries[0].reshape(tokens, head_count, HEAD_DIM)
    group_count = HEAD_GROUPS
    tiles_all = lax.axis_size("tile") // group_count
    grid_w = min(4, tiles_all)
    grid_h = min(4, tiles_all // grid_w)
    grid_f = tiles_all // (grid_w * grid_h)
    frames_valid = grid_f * TS - TS // 4
    my_index = lax.axis_index("tile")
    tile_id = my_index // group_count
    head_group = my_index % group_count
    w_pos = tile_id % grid_w
    h_pos = tile_id // grid_w % grid_h
    f_pos = tile_id // (grid_w * grid_h)
    key_rows = tokens
    if grid_f == 1:
        key_rows = min(tokens, frames_valid * TS * TS)
    own_pair = jnp.stack([keys[0, :key_rows], values[0, :key_rows]])
    local_frame = jnp.arange(key_rows, dtype=jnp.int32) // (TS * TS)

    def keep_mask(off_frame, off_height, off_width):
        inside = (
            (f_pos + off_frame >= 0)
            & (f_pos + off_frame < grid_f)
            & (h_pos + off_height >= 0)
            & (h_pos + off_height < grid_h)
            & (w_pos + off_width >= 0)
            & (w_pos + off_width < grid_w)
        )
        return inside & ((f_pos + off_frame) * TS + local_frame < frames_valid)

    running = (
        jnp.full((head_count, tokens), MASKED, jnp.float32),
        jnp.zeros((head_count, tokens), jnp.float32),
        jnp.zeros((head_count, tokens, HEAD_DIM), jnp.float32),
    )
    text_got, text_keep = text_pieces(text_keys, text_values, text_mask, group_count, lane_width)
    width_set = {0: own_pair}
    for off_width in (-1, 1):
        width_set[off_width] = passed_along(own_pair, "tile", -off_width * group_count)
    if grid_h == 1 and grid_f == 1:
        as_row = lambda keep: keep.astype(jnp.float32)[:, None]
        query_t = jnp.transpose(queries[0])
        carry = window_attention(query_t, [(own_pair, 0, 1, as_row(keep_mask(0, 0, 0)))], finish=False)
        carry = window_attention(
            query_t, [(text_got, 0, head_count, as_row(text_keep))], carry=carry, finish=False
        )
        blocks = [(width_set[off_width], 0, 1, as_row(keep_mask(0, 0, off_width))) for off_width in (-1, 1)]
        return window_attention(query_t, blocks, carry=carry)[None]
    piece_keys = text_got[:, :lane_width]
    piece_values = text_got[:, lane_width : 2 * lane_width]
    running = fold_block(running, query_heads, piece_keys, piece_values, text_keep)
    running = fold_block(running, query_heads, own_pair[0], own_pair[1], keep_mask(0, 0, 0))
    width_offsets = sorted(width_set)
    row_stack = jnp.stack([width_set[spot] for spot in width_offsets])
    height_set = {0: row_stack}
    if grid_h > 1:
        for off_height in (-1, 1):
            height_set[off_height] = passed_along(
                shortened(row_stack), "tile", -off_height * grid_w * group_count
            ).astype(row_stack.dtype)
    height_offsets = sorted(height_set)
    slab_stack = jnp.stack([height_set[spot] for spot in height_offsets])

    def fold_slab(state_now, slab_pairs, off_frame):
        for h_slot, off_height in enumerate(height_offsets):
            for w_slot, off_width in enumerate(width_offsets):
                if off_frame == 0 and off_height == 0 and (off_width == 0):
                    continue
                state_now = fold_block(
                    state_now,
                    query_heads,
                    slab_pairs[h_slot, w_slot, 0],
                    slab_pairs[h_slot, w_slot, 1],
                    keep_mask(off_frame, off_height, off_width),
                )
        return state_now

    running = fold_slab(running, slab_stack, 0)
    if grid_f > 1:
        for off_frame in (-1, 1):
            got_slab = passed_along(
                shortened(slab_stack), "tile", -off_frame * grid_h * grid_w * group_count
            ).astype(slab_stack.dtype)
            running = fold_slab(running, got_slab, off_frame)
    row_top, row_total, summed = running
    result = summed / row_total[:, :, None]
    result = jnp.transpose(result, (1, 0, 2)).reshape(tokens, lane_width)
    return result.astype(jnp.bfloat16)[None]


def solution(mesh):
    return jax.shard_map(
        shards,
        mesh=mesh,
        in_specs=(
            P(("req", "tile"), None, None),
            P(("req", "tile"), None, None),
            P(("req", "tile"), None, None),
            P(("req", "tile"), None),
            P(("req", "tile"), None),
            P(("req", "tile")),
        ),
        out_specs=P(("req", "tile"), None, None),
        check_vma=False,
    )
```

```python
import functools
import math

import jax
import jax.numpy as jnp
from jax import lax
from jax.experimental import pallas as pl
from jax.experimental.pallas import tpu as pltpu
from jax.sharding import PartitionSpec as P

TS = 8
HEAD_DIM = 128
HEAD_GROUPS = 4


MASKED = -1e30
EXP2_SCALE = math.log2(math.e) / math.sqrt(HEAD_DIM)


def passed_along(value, axis, steps):
    count = lax.axis_size(axis)
    first, last = (max(0, -steps), min(count, count - steps))
    return lax.ppermute(value, axis, [(source, source + steps) for source in range(first, last)])


def shortened(value):
    return jax.tree.map(lambda a: a.astype(jnp.bfloat16) if a.dtype == jnp.float32 else a, value)


def fold_block(running, query_heads, key_block, value_block, key_keep):
    row_top, row_total, summed = running
    head_count = query_heads.shape[1]
    key_heads = key_block.reshape(key_block.shape[0], head_count, HEAD_DIM)
    value_heads = value_block.reshape(value_block.shape[0], head_count, HEAD_DIM)
    scores = jnp.einsum("qhd,khd->hqk", query_heads, key_heads, preferred_element_type=jnp.float32)
    scores = scores * (1.0 / math.sqrt(HEAD_DIM))
    scores = jnp.where(key_keep[None, None, :], scores, MASKED)
    new_top = jnp.maximum(row_top, jnp.max(scores, axis=-1))
    scale_down = jnp.exp(row_top - new_top)
    exp_terms = jnp.where(key_keep[None, None, :], jnp.exp(scores - new_top[:, :, None]), 0.0)
    row_total = row_total * scale_down + jnp.sum(exp_terms, axis=-1)
    weights = exp_terms.astype(jnp.bfloat16)
    summed = summed * scale_down[:, :, None] + jnp.einsum(
        "hqk,khd->hqd", weights, value_heads, preferred_element_type=jnp.float32
    )
    return (new_top, row_total, summed)


def window_kernel(blocks, carry_in, finish, q_ref, *refs):
    block_count = len(blocks)
    source_refs = refs[:block_count]
    keep_refs = refs[block_count : 2 * block_count]
    rest = refs[2 * block_count :]
    lane_width, tokens = q_ref.shape
    head_count = lane_width // HEAD_DIM
    keeps = [
        jnp.broadcast_to(keep_refs[b][...], (keep_refs[b].shape[0], tokens)) > 0.5 for b in range(block_count)
    ]
    for h in range(head_count):
        lanes = slice(h * HEAD_DIM, (h + 1) * HEAD_DIM)
        query_t = q_ref[lanes, :]
        scores, value_tiles = [], []
        for b, (pair_form, key_at, value_at) in enumerate(blocks):
            if pair_form:
                key_tile = source_refs[b][key_at, :, lanes]
                value_tile = source_refs[b][value_at, :, lanes]
            else:
                key_tile = source_refs[b][:, (key_at + h) * HEAD_DIM : (key_at + h + 1) * HEAD_DIM]
                value_tile = source_refs[b][:, (value_at + h) * HEAD_DIM : (value_at + h + 1) * HEAD_DIM]
            s = jnp.dot(key_tile, query_t, preferred_element_type=jnp.float32)
            scores.append(jnp.where(keeps[b], s, MASKED))
            value_tiles.append(value_tile)
        top = scores[0].max(axis=0, keepdims=True)
        for s in scores[1:]:
            top = jnp.maximum(top, s.max(axis=0, keepdims=True))
        if carry_in:
            top_in = rest[0][h : h + 1, :]
            top = jnp.maximum(top, top_in)
            scale_down = jnp.exp2((top_in - top) * EXP2_SCALE)
            total = rest[0][head_count + h : head_count + h + 1, :] * scale_down
            summed = rest[1][lanes, :] * scale_down
        else:
            total = jnp.zeros_like(top)
            summed = None
        for b in range(block_count):
            terms = jnp.exp2((scores[b] - top) * EXP2_SCALE)
            total = total + terms.sum(axis=0, keepdims=True)
            part = lax.dot_general(
                value_tiles[b],
                terms.astype(jnp.bfloat16),
                (((0,), (0,)), ((), ())),
                preferred_element_type=jnp.float32,
            )
            summed = part if summed is None else summed + part
        outs = rest[2:] if carry_in else rest
        if finish:
            outs[0][:, lanes] = jnp.transpose(summed / total).astype(outs[0].dtype)
        else:
            outs[0][h : h + 1, :] = top
            outs[0][head_count + h : head_count + h + 1, :] = total
            outs[1][lanes, :] = summed


def window_attention(query_t, blocks, carry=None, finish=True):
    lane_width, tokens = query_t.shape
    head_count = lane_width // HEAD_DIM
    layout, sources, keeps = [], [], []
    key_total = 0
    for source, key_at, value_at, keep in blocks:
        key_total += keep.shape[0]
        layout.append((source.ndim == 3, key_at, value_at))
        sources.append(source)
        keeps.append(keep)
    stat_rows = -(-2 * head_count // 8) * 8
    stat_shape = jax.ShapeDtypeStruct((stat_rows, tokens), jnp.float32)
    if finish:
        out_shape = jax.ShapeDtypeStruct((tokens, lane_width), jnp.bfloat16)
        out_specs = pl.BlockSpec(memory_space=pltpu.VMEM)
    else:
        out_shape = (
            pltpu.VMEM(stat_shape.shape, stat_shape.dtype),
            pltpu.VMEM((lane_width, tokens), jnp.float32),
        )
        out_specs = tuple(pl.BlockSpec(memory_space=pltpu.VMEM) for _ in range(2))
    carry_args = () if carry is None else tuple(carry)
    operand_count = 1 + 2 * len(blocks) + len(carry_args)
    flops = 4 * tokens * key_total * lane_width
    moved = 2 * (2 * tokens * lane_width + 2 * key_total * lane_width) + 4 * 2 * tokens * (lane_width + 8)
    return pl.pallas_call(
        functools.partial(window_kernel, tuple(layout), carry is not None, finish),
        out_shape=out_shape,
        in_specs=[pl.BlockSpec(memory_space=pltpu.VMEM)] * operand_count,
        out_specs=out_specs,
        cost_estimate=pl.CostEstimate(
            flops=flops, transcendentals=tokens * key_total * head_count, bytes_accessed=moved
        ),
        compiler_params=pltpu.CompilerParams(vmem_limit_bytes=16 * 1024 * 1024),
    )(*[pltpu.with_memory_space_constraint(a, pltpu.VMEM) for a in (query_t, *sources, *keeps, *carry_args)])


def text_pieces(text_keys, text_values, text_mask, group_count, lane_width):
    count = lax.axis_size("tile")
    rows = text_keys.shape[0]
    flags = jnp.broadcast_to(text_mask.astype(jnp.bfloat16)[:, None], (rows, 128))
    per_group = jnp.stack(
        [
            jnp.concatenate(
                [
                    text_keys[:, g * lane_width : (g + 1) * lane_width],
                    text_values[:, g * lane_width : (g + 1) * lane_width],
                    flags,
                ],
                axis=1,
            )
            for g in range(group_count)
        ]
    )
    outgoing = jnp.tile(per_group, (count // group_count, 1, 1)).reshape(count * rows, 2 * lane_width + 128)
    got = lax.all_to_all(outgoing, "tile", 0, 0, tiled=True)
    return got, got[:, 2 * lane_width] > 0.5


def shards(queries, keys, values, text_keys, text_values, text_mask):
    tokens = queries.shape[1]
    lane_width = queries.shape[2]
    head_count = lane_width // HEAD_DIM
    query_heads = queries[0].reshape(tokens, head_count, HEAD_DIM)
    group_count = HEAD_GROUPS
    tiles_all = lax.axis_size("tile") // group_count
    grid_w = min(4, tiles_all)
    grid_h = min(4, tiles_all // grid_w)
    grid_f = tiles_all // (grid_w * grid_h)
    frames_valid = grid_f * TS - TS // 4
    my_index = lax.axis_index("tile")
    tile_id = my_index // group_count
    head_group = my_index % group_count
    w_pos = tile_id % grid_w
    h_pos = tile_id // grid_w % grid_h
    f_pos = tile_id // (grid_w * grid_h)
    key_rows = tokens
    if grid_f == 1:
        key_rows = min(tokens, frames_valid * TS * TS)
    own_pair = jnp.stack([keys[0, :key_rows], values[0, :key_rows]])
    local_frame = jnp.arange(key_rows, dtype=jnp.int32) // (TS * TS)

    def keep_mask(off_frame, off_height, off_width):
        inside = (
            (f_pos + off_frame >= 0)
            & (f_pos + off_frame < grid_f)
            & (h_pos + off_height >= 0)
            & (h_pos + off_height < grid_h)
            & (w_pos + off_width >= 0)
            & (w_pos + off_width < grid_w)
        )
        return inside & ((f_pos + off_frame) * TS + local_frame < frames_valid)

    running = (
        jnp.full((head_count, tokens), MASKED, jnp.float32),
        jnp.zeros((head_count, tokens), jnp.float32),
        jnp.zeros((head_count, tokens, HEAD_DIM), jnp.float32),
    )
    text_got, text_keep = text_pieces(text_keys, text_values, text_mask, group_count, lane_width)
    width_set = {0: own_pair}
    for off_width in (-1, 1):
        width_set[off_width] = passed_along(own_pair, "tile", -off_width * group_count)
    if grid_h == 1 and grid_f == 1:
        as_row = lambda keep: keep.astype(jnp.float32)[:, None]
        query_t = jnp.transpose(queries[0])
        carry = window_attention(query_t, [(own_pair, 0, 1, as_row(keep_mask(0, 0, 0)))], finish=False)
        carry = window_attention(
            query_t, [(text_got, 0, head_count, as_row(text_keep))], carry=carry, finish=False
        )
        blocks = [(width_set[-1], 0, 1, as_row(keep_mask(0, 0, -1)))]
        carry = window_attention(query_t, blocks, carry=carry, finish=False)
        blocks = [(width_set[1], 0, 1, as_row(keep_mask(0, 0, 1)))]
        return window_attention(query_t, blocks, carry=carry)[None]
    piece_keys = text_got[:, :lane_width]
    piece_values = text_got[:, lane_width : 2 * lane_width]
    running = fold_block(running, query_heads, piece_keys, piece_values, text_keep)
    running = fold_block(running, query_heads, own_pair[0], own_pair[1], keep_mask(0, 0, 0))
    width_offsets = sorted(width_set)
    row_stack = jnp.stack([width_set[spot] for spot in width_offsets])
    height_set = {0: row_stack}
    if grid_h > 1:
        for off_height in (-1, 1):
            height_set[off_height] = passed_along(
                shortened(row_stack), "tile", -off_height * grid_w * group_count
            ).astype(row_stack.dtype)
    height_offsets = sorted(height_set)
    slab_stack = jnp.stack([height_set[spot] for spot in height_offsets])

    def fold_slab(state_now, slab_pairs, off_frame):
        for h_slot, off_height in enumerate(height_offsets):
            for w_slot, off_width in enumerate(width_offsets):
                if off_frame == 0 and off_height == 0 and (off_width == 0):
                    continue
                state_now = fold_block(
                    state_now,
                    query_heads,
                    slab_pairs[h_slot, w_slot, 0],
                    slab_pairs[h_slot, w_slot, 1],
                    keep_mask(off_frame, off_height, off_width),
                )
        return state_now

    running = fold_slab(running, slab_stack, 0)
    if grid_f > 1:
        for off_frame in (-1, 1):
            got_slab = passed_along(
                shortened(slab_stack), "tile", -off_frame * grid_h * grid_w * group_count
            ).astype(slab_stack.dtype)
            running = fold_slab(running, got_slab, off_frame)
    row_top, row_total, summed = running
    result = summed / row_total[:, :, None]
    result = jnp.transpose(result, (1, 0, 2)).reshape(tokens, lane_width)
    return result.astype(jnp.bfloat16)[None]


def solution(mesh):
    return jax.shard_map(
        shards,
        mesh=mesh,
        in_specs=(
            P(("req", "tile"), None, None),
            P(("req", "tile"), None, None),
            P(("req", "tile"), None, None),
            P(("req", "tile"), None),
            P(("req", "tile"), None),
            P(("req", "tile")),
        ),
        out_specs=P(("req", "tile"), None, None),
        check_vma=False,
    )
```

```python
import functools
import math

import jax
import jax.numpy as jnp
from jax import lax
from jax.experimental import pallas as pl
from jax.experimental.pallas import tpu as pltpu
from jax.sharding import PartitionSpec as P

TS = 8
HEAD_DIM = 128
HEAD_GROUPS = 4


MASKED = -1e30
EXP2_SCALE = math.log2(math.e) / math.sqrt(HEAD_DIM)


def passed_along(value, axis, steps):
    count = lax.axis_size(axis)
    first, last = (max(0, -steps), min(count, count - steps))
    return lax.ppermute(value, axis, [(source, source + steps) for source in range(first, last)])


def shortened(value):
    return jax.tree.map(lambda a: a.astype(jnp.bfloat16) if a.dtype == jnp.float32 else a, value)


def fold_block(running, query_heads, key_block, value_block, key_keep):
    row_top, row_total, summed = running
    head_count = query_heads.shape[1]
    key_heads = key_block.reshape(key_block.shape[0], head_count, HEAD_DIM)
    value_heads = value_block.reshape(value_block.shape[0], head_count, HEAD_DIM)
    scores = jnp.einsum("qhd,khd->hqk", query_heads, key_heads, preferred_element_type=jnp.float32)
    scores = scores * (1.0 / math.sqrt(HEAD_DIM))
    scores = jnp.where(key_keep[None, None, :], scores, MASKED)
    new_top = jnp.maximum(row_top, jnp.max(scores, axis=-1))
    scale_down = jnp.exp(row_top - new_top)
    exp_terms = jnp.where(key_keep[None, None, :], jnp.exp(scores - new_top[:, :, None]), 0.0)
    row_total = row_total * scale_down + jnp.sum(exp_terms, axis=-1)
    weights = exp_terms.astype(jnp.bfloat16)
    summed = summed * scale_down[:, :, None] + jnp.einsum(
        "hqk,khd->hqd", weights, value_heads, preferred_element_type=jnp.float32
    )
    return (new_top, row_total, summed)


def window_kernel(blocks, carry_in, finish, q_ref, *refs):
    block_count = len(blocks)
    source_refs = refs[:block_count]
    keep_refs = refs[block_count : 2 * block_count]
    rest = refs[2 * block_count :]
    lane_width, tokens = q_ref.shape
    head_count = lane_width // HEAD_DIM
    keeps = [
        jnp.broadcast_to(keep_refs[b][...], (keep_refs[b].shape[0], tokens)) > 0.5 for b in range(block_count)
    ]
    for h in range(head_count):
        lanes = slice(h * HEAD_DIM, (h + 1) * HEAD_DIM)
        query_t = q_ref[lanes, :]
        scores, value_tiles = [], []
        for b, (pair_form, key_at, value_at) in enumerate(blocks):
            if pair_form:
                key_tile = source_refs[b][key_at, :, lanes]
                value_tile = source_refs[b][value_at, :, lanes]
            else:
                key_tile = source_refs[b][:, (key_at + h) * HEAD_DIM : (key_at + h + 1) * HEAD_DIM]
                value_tile = source_refs[b][:, (value_at + h) * HEAD_DIM : (value_at + h + 1) * HEAD_DIM]
            s = jnp.dot(key_tile, query_t, preferred_element_type=jnp.float32)
            scores.append(jnp.where(keeps[b], s, MASKED))
            value_tiles.append(value_tile)
        top = scores[0].max(axis=0, keepdims=True)
        for s in scores[1:]:
            top = jnp.maximum(top, s.max(axis=0, keepdims=True))
        if carry_in:
            top_in = rest[0][h : h + 1, :]
            top = jnp.maximum(top, top_in)
            scale_down = jnp.exp2((top_in - top) * EXP2_SCALE)
            total = rest[0][head_count + h : head_count + h + 1, :] * scale_down
            summed = rest[1][lanes, :] * scale_down
        else:
            total = jnp.zeros_like(top)
            summed = None
        for b in range(block_count):
            terms = jnp.exp2((scores[b] - top) * EXP2_SCALE)
            total = total + terms.sum(axis=0, keepdims=True)
            part = lax.dot_general(
                value_tiles[b],
                terms.astype(jnp.bfloat16),
                (((0,), (0,)), ((), ())),
                preferred_element_type=jnp.float32,
            )
            summed = part if summed is None else summed + part
        outs = rest[2:] if carry_in else rest
        if finish:
            outs[0][:, lanes] = jnp.transpose(summed / total).astype(outs[0].dtype)
        else:
            outs[0][h : h + 1, :] = top
            outs[0][head_count + h : head_count + h + 1, :] = total
            outs[1][lanes, :] = summed


def window_attention(query_t, blocks, carry=None, finish=True):
    lane_width, tokens = query_t.shape
    head_count = lane_width // HEAD_DIM
    layout, sources, keeps = [], [], []
    key_total = 0
    for source, key_at, value_at, keep in blocks:
        key_total += keep.shape[0]
        layout.append((source.ndim == 3, key_at, value_at))
        sources.append(source)
        keeps.append(keep)
    stat_rows = -(-2 * head_count // 8) * 8
    stat_shape = jax.ShapeDtypeStruct((stat_rows, tokens), jnp.float32)
    if finish:
        out_shape = jax.ShapeDtypeStruct((tokens, lane_width), jnp.bfloat16)
        out_specs = pl.BlockSpec(memory_space=pltpu.VMEM)
    else:
        out_shape = (
            pltpu.VMEM(stat_shape.shape, stat_shape.dtype),
            pltpu.VMEM((lane_width, tokens), jnp.float32),
        )
        out_specs = tuple(pl.BlockSpec(memory_space=pltpu.VMEM) for _ in range(2))
    carry_args = () if carry is None else tuple(carry)
    operand_count = 1 + 2 * len(blocks) + len(carry_args)
    flops = 4 * tokens * key_total * lane_width
    moved = 2 * (2 * tokens * lane_width + 2 * key_total * lane_width) + 4 * 2 * tokens * (lane_width + 8)
    return pl.pallas_call(
        functools.partial(window_kernel, tuple(layout), carry is not None, finish),
        out_shape=out_shape,
        in_specs=[pl.BlockSpec(memory_space=pltpu.VMEM)] * operand_count,
        out_specs=out_specs,
        cost_estimate=pl.CostEstimate(
            flops=flops, transcendentals=tokens * key_total * head_count, bytes_accessed=moved
        ),
        compiler_params=pltpu.CompilerParams(vmem_limit_bytes=16 * 1024 * 1024),
    )(*[pltpu.with_memory_space_constraint(a, pltpu.VMEM) for a in (query_t, *sources, *keeps, *carry_args)])


def text_pieces(text_keys, text_values, text_mask, group_count, lane_width):
    count = lax.axis_size("tile")
    rows = text_keys.shape[0]
    shape = (rows, group_count, lane_width)
    flags = jnp.broadcast_to(text_mask.astype(jnp.bfloat16)[:, None, None], (rows, group_count, 128))
    per_group = jnp.concatenate([text_keys.reshape(shape), text_values.reshape(shape), flags], axis=2)
    per_group = jnp.transpose(per_group, (1, 0, 2))
    width = 2 * lane_width + 128
    outgoing = jnp.broadcast_to(per_group[None], (count // group_count, group_count, rows, width))
    outgoing = outgoing.reshape(count * rows, width)
    got = lax.all_to_all(outgoing, "tile", 0, 0, tiled=True)
    return got, got[:, 2 * lane_width] > 0.5


def shards(queries, keys, values, text_keys, text_values, text_mask):
    tokens = queries.shape[1]
    lane_width = queries.shape[2]
    head_count = lane_width // HEAD_DIM
    query_heads = queries[0].reshape(tokens, head_count, HEAD_DIM)
    group_count = HEAD_GROUPS
    tiles_all = lax.axis_size("tile") // group_count
    grid_w = min(4, tiles_all)
    grid_h = min(4, tiles_all // grid_w)
    grid_f = tiles_all // (grid_w * grid_h)
    frames_valid = grid_f * TS - TS // 4
    my_index = lax.axis_index("tile")
    tile_id = my_index // group_count
    head_group = my_index % group_count
    w_pos = tile_id % grid_w
    h_pos = tile_id // grid_w % grid_h
    f_pos = tile_id // (grid_w * grid_h)
    key_rows = tokens
    if grid_f == 1:
        key_rows = min(tokens, frames_valid * TS * TS)
    own_pair = jnp.stack([keys[0, :key_rows], values[0, :key_rows]])
    local_frame = jnp.arange(key_rows, dtype=jnp.int32) // (TS * TS)

    def keep_mask(off_frame, off_height, off_width):
        inside = (
            (f_pos + off_frame >= 0)
            & (f_pos + off_frame < grid_f)
            & (h_pos + off_height >= 0)
            & (h_pos + off_height < grid_h)
            & (w_pos + off_width >= 0)
            & (w_pos + off_width < grid_w)
        )
        return inside & ((f_pos + off_frame) * TS + local_frame < frames_valid)

    running = (
        jnp.full((head_count, tokens), MASKED, jnp.float32),
        jnp.zeros((head_count, tokens), jnp.float32),
        jnp.zeros((head_count, tokens, HEAD_DIM), jnp.float32),
    )
    text_got, text_keep = text_pieces(text_keys, text_values, text_mask, group_count, lane_width)
    width_set = {0: own_pair}
    for off_width in (-1, 1):
        width_set[off_width] = passed_along(own_pair, "tile", -off_width * group_count)
    if grid_h == 1 and grid_f == 1:
        as_row = lambda keep: keep.astype(jnp.float32)[:, None]
        query_t = jnp.transpose(queries[0])
        carry = window_attention(query_t, [(own_pair, 0, 1, as_row(keep_mask(0, 0, 0)))], finish=False)
        carry = window_attention(
            query_t, [(text_got, 0, head_count, as_row(text_keep))], carry=carry, finish=False
        )
        blocks = [(width_set[-1], 0, 1, as_row(keep_mask(0, 0, -1)))]
        carry = window_attention(query_t, blocks, carry=carry, finish=False)
        blocks = [(width_set[1], 0, 1, as_row(keep_mask(0, 0, 1)))]
        return window_attention(query_t, blocks, carry=carry)[None]
    piece_keys = text_got[:, :lane_width]
    piece_values = text_got[:, lane_width : 2 * lane_width]
    running = fold_block(running, query_heads, piece_keys, piece_values, text_keep)
    running = fold_block(running, query_heads, own_pair[0], own_pair[1], keep_mask(0, 0, 0))
    width_offsets = sorted(width_set)
    row_stack = jnp.stack([width_set[spot] for spot in width_offsets])
    height_set = {0: row_stack}
    if grid_h > 1:
        for off_height in (-1, 1):
            height_set[off_height] = passed_along(
                shortened(row_stack), "tile", -off_height * grid_w * group_count
            ).astype(row_stack.dtype)
    height_offsets = sorted(height_set)
    slab_stack = jnp.stack([height_set[spot] for spot in height_offsets])

    def fold_slab(state_now, slab_pairs, off_frame):
        for h_slot, off_height in enumerate(height_offsets):
            for w_slot, off_width in enumerate(width_offsets):
                if off_frame == 0 and off_height == 0 and (off_width == 0):
                    continue
                state_now = fold_block(
                    state_now,
                    query_heads,
                    slab_pairs[h_slot, w_slot, 0],
                    slab_pairs[h_slot, w_slot, 1],
                    keep_mask(off_frame, off_height, off_width),
                )
        return state_now

    running = fold_slab(running, slab_stack, 0)
    if grid_f > 1:
        for off_frame in (-1, 1):
            got_slab = passed_along(
                shortened(slab_stack), "tile", -off_frame * grid_h * grid_w * group_count
            ).astype(slab_stack.dtype)
            running = fold_slab(running, got_slab, off_frame)
    row_top, row_total, summed = running
    result = summed / row_total[:, :, None]
    result = jnp.transpose(result, (1, 0, 2)).reshape(tokens, lane_width)
    return result.astype(jnp.bfloat16)[None]


def solution(mesh):
    return jax.shard_map(
        shards,
        mesh=mesh,
        in_specs=(
            P(("req", "tile"), None, None),
            P(("req", "tile"), None, None),
            P(("req", "tile"), None, None),
            P(("req", "tile"), None),
            P(("req", "tile"), None),
            P(("req", "tile")),
        ),
        out_specs=P(("req", "tile"), None, None),
        check_vma=False,
    )
```

```python
import functools
import math

import jax
import jax.numpy as jnp
from jax import lax
from jax.experimental import pallas as pl
from jax.experimental.pallas import tpu as pltpu
from jax.sharding import PartitionSpec as P

TS = 8
HEAD_DIM = 128
HEAD_GROUPS = 4


MASKED = -1e30
EXP2_SCALE = math.log2(math.e) / math.sqrt(HEAD_DIM)


def passed_along(value, axis, steps):
    count = lax.axis_size(axis)
    first, last = (max(0, -steps), min(count, count - steps))
    return lax.ppermute(value, axis, [(source, source + steps) for source in range(first, last)])


def shortened(value):
    return jax.tree.map(lambda a: a.astype(jnp.bfloat16) if a.dtype == jnp.float32 else a, value)


def fold_block(running, query_heads, key_block, value_block, key_keep):
    row_top, row_total, summed = running
    head_count = query_heads.shape[1]
    key_heads = key_block.reshape(key_block.shape[0], head_count, HEAD_DIM)
    value_heads = value_block.reshape(value_block.shape[0], head_count, HEAD_DIM)
    scores = jnp.einsum("qhd,khd->hqk", query_heads, key_heads, preferred_element_type=jnp.float32)
    scores = scores * (1.0 / math.sqrt(HEAD_DIM))
    scores = jnp.where(key_keep[None, None, :], scores, MASKED)
    new_top = jnp.maximum(row_top, jnp.max(scores, axis=-1))
    scale_down = jnp.exp(row_top - new_top)
    exp_terms = jnp.where(key_keep[None, None, :], jnp.exp(scores - new_top[:, :, None]), 0.0)
    row_total = row_total * scale_down + jnp.sum(exp_terms, axis=-1)
    weights = exp_terms.astype(jnp.bfloat16)
    summed = summed * scale_down[:, :, None] + jnp.einsum(
        "hqk,khd->hqd", weights, value_heads, preferred_element_type=jnp.float32
    )
    return (new_top, row_total, summed)


def window_kernel(blocks, carry_in, finish, q_ref, *refs):
    block_count = len(blocks)
    source_refs = refs[:block_count]
    keep_refs = refs[block_count : 2 * block_count]
    rest = refs[2 * block_count :]
    lane_width, tokens = q_ref.shape
    head_count = lane_width // HEAD_DIM
    keeps = [
        jnp.broadcast_to(keep_refs[b][...], (keep_refs[b].shape[0], tokens)) > 0.5 for b in range(block_count)
    ]
    for h in range(head_count):
        lanes = slice(h * HEAD_DIM, (h + 1) * HEAD_DIM)
        query_t = q_ref[lanes, :]
        scores, value_tiles = [], []
        for b, (pair_form, key_at, value_at) in enumerate(blocks):
            if pair_form:
                key_tile = source_refs[b][key_at, :, lanes]
                value_tile = source_refs[b][value_at, :, lanes]
            else:
                key_tile = source_refs[b][:, (key_at + h) * HEAD_DIM : (key_at + h + 1) * HEAD_DIM]
                value_tile = source_refs[b][:, (value_at + h) * HEAD_DIM : (value_at + h + 1) * HEAD_DIM]
            s = jnp.dot(key_tile, query_t, preferred_element_type=jnp.float32)
            scores.append(jnp.where(keeps[b], s, MASKED))
            value_tiles.append(value_tile)
        top = scores[0].max(axis=0, keepdims=True)
        for s in scores[1:]:
            top = jnp.maximum(top, s.max(axis=0, keepdims=True))
        if carry_in:
            top_in = rest[0][h : h + 1, :]
            top = jnp.maximum(top, top_in)
            scale_down = jnp.exp2((top_in - top) * EXP2_SCALE)
            total = rest[0][head_count + h : head_count + h + 1, :] * scale_down
            summed = rest[1][lanes, :] * scale_down
        else:
            total = jnp.zeros_like(top)
            summed = None
        for b in range(block_count):
            terms = jnp.exp2((scores[b] - top) * EXP2_SCALE)
            total = total + terms.sum(axis=0, keepdims=True)
            part = lax.dot_general(
                value_tiles[b],
                terms.astype(jnp.bfloat16),
                (((0,), (0,)), ((), ())),
                preferred_element_type=jnp.float32,
            )
            summed = part if summed is None else summed + part
        outs = rest[2:] if carry_in else rest
        if finish:
            outs[0][:, lanes] = jnp.transpose(summed / total).astype(outs[0].dtype)
        else:
            outs[0][h : h + 1, :] = top
            outs[0][head_count + h : head_count + h + 1, :] = total
            outs[1][lanes, :] = summed


def window_attention(query_t, blocks, carry=None, finish=True):
    lane_width, tokens = query_t.shape
    head_count = lane_width // HEAD_DIM
    layout, sources, keeps = [], [], []
    key_total = 0
    for source, key_at, value_at, keep in blocks:
        key_total += keep.shape[0]
        layout.append((source.ndim == 3, key_at, value_at))
        sources.append(source)
        keeps.append(keep)
    stat_rows = -(-2 * head_count // 8) * 8
    stat_shape = jax.ShapeDtypeStruct((stat_rows, tokens), jnp.float32)
    if finish:
        out_shape = jax.ShapeDtypeStruct((tokens, lane_width), jnp.bfloat16)
        out_specs = pl.BlockSpec(memory_space=pltpu.VMEM)
    else:
        out_shape = (
            pltpu.VMEM(stat_shape.shape, stat_shape.dtype),
            pltpu.VMEM((lane_width, tokens), jnp.float32),
        )
        out_specs = tuple(pl.BlockSpec(memory_space=pltpu.VMEM) for _ in range(2))
    carry_args = () if carry is None else tuple(carry)
    operand_count = 1 + 2 * len(blocks) + len(carry_args)
    flops = 4 * tokens * key_total * lane_width
    moved = 2 * (2 * tokens * lane_width + 2 * key_total * lane_width) + 4 * 2 * tokens * (lane_width + 8)
    return pl.pallas_call(
        functools.partial(window_kernel, tuple(layout), carry is not None, finish),
        out_shape=out_shape,
        in_specs=[pl.BlockSpec(memory_space=pltpu.VMEM)] * operand_count,
        out_specs=out_specs,
        cost_estimate=pl.CostEstimate(
            flops=flops, transcendentals=tokens * key_total * head_count, bytes_accessed=moved
        ),
        compiler_params=pltpu.CompilerParams(vmem_limit_bytes=16 * 1024 * 1024),
    )(*[pltpu.with_memory_space_constraint(a, pltpu.VMEM) for a in (query_t, *sources, *keeps, *carry_args)])


def text_pieces(text_keys, text_values, text_mask, group_count, lane_width, after=None):
    count = lax.axis_size("tile")
    rows = text_keys.shape[0]
    shape = (rows, group_count, lane_width)
    flags = jnp.broadcast_to(text_mask.astype(jnp.bfloat16)[:, None, None], (rows, group_count, 128))
    per_group = jnp.concatenate([text_keys.reshape(shape), text_values.reshape(shape), flags], axis=2)
    per_group = jnp.transpose(per_group, (1, 0, 2))
    width = 2 * lane_width + 128
    outgoing = jnp.broadcast_to(per_group[None], (count // group_count, group_count, rows, width))
    outgoing = outgoing.reshape(count * rows, width)
    if after is not None:
        outgoing = lax.optimization_barrier((outgoing, after))[0]
    got = lax.all_to_all(outgoing, "tile", 0, 0, tiled=True)
    return got, got[:, 2 * lane_width] > 0.5


def shards(queries, keys, values, text_keys, text_values, text_mask):
    tokens = queries.shape[1]
    lane_width = queries.shape[2]
    head_count = lane_width // HEAD_DIM
    query_heads = queries[0].reshape(tokens, head_count, HEAD_DIM)
    group_count = HEAD_GROUPS
    tiles_all = lax.axis_size("tile") // group_count
    grid_w = min(4, tiles_all)
    grid_h = min(4, tiles_all // grid_w)
    grid_f = tiles_all // (grid_w * grid_h)
    frames_valid = grid_f * TS - TS // 4
    my_index = lax.axis_index("tile")
    tile_id = my_index // group_count
    head_group = my_index % group_count
    w_pos = tile_id % grid_w
    h_pos = tile_id // grid_w % grid_h
    f_pos = tile_id // (grid_w * grid_h)
    key_rows = tokens
    if grid_f == 1:
        key_rows = min(tokens, frames_valid * TS * TS)
    own_pair = jnp.stack([keys[0, :key_rows], values[0, :key_rows]])
    local_frame = jnp.arange(key_rows, dtype=jnp.int32) // (TS * TS)

    def keep_mask(off_frame, off_height, off_width):
        inside = (
            (f_pos + off_frame >= 0)
            & (f_pos + off_frame < grid_f)
            & (h_pos + off_height >= 0)
            & (h_pos + off_height < grid_h)
            & (w_pos + off_width >= 0)
            & (w_pos + off_width < grid_w)
        )
        return inside & ((f_pos + off_frame) * TS + local_frame < frames_valid)

    running = (
        jnp.full((head_count, tokens), MASKED, jnp.float32),
        jnp.zeros((head_count, tokens), jnp.float32),
        jnp.zeros((head_count, tokens, HEAD_DIM), jnp.float32),
    )
    text_got, text_keep = text_pieces(text_keys, text_values, text_mask, group_count, lane_width, own_pair)
    width_set = {0: own_pair}
    for off_width in (-1, 1):
        width_set[off_width] = passed_along(own_pair, "tile", -off_width * group_count)
    if grid_h == 1 and grid_f == 1:
        as_row = lambda keep: keep.astype(jnp.float32)[:, None]
        query_t = jnp.transpose(queries[0])
        carry = window_attention(query_t, [(own_pair, 0, 1, as_row(keep_mask(0, 0, 0)))], finish=False)
        carry = window_attention(
            query_t, [(text_got, 0, head_count, as_row(text_keep))], carry=carry, finish=False
        )
        blocks = [(width_set[-1], 0, 1, as_row(keep_mask(0, 0, -1)))]
        carry = window_attention(query_t, blocks, carry=carry, finish=False)
        blocks = [(width_set[1], 0, 1, as_row(keep_mask(0, 0, 1)))]
        return window_attention(query_t, blocks, carry=carry)[None]
    piece_keys = text_got[:, :lane_width]
    piece_values = text_got[:, lane_width : 2 * lane_width]
    running = fold_block(running, query_heads, piece_keys, piece_values, text_keep)
    running = fold_block(running, query_heads, own_pair[0], own_pair[1], keep_mask(0, 0, 0))
    width_offsets = sorted(width_set)
    row_stack = jnp.stack([width_set[spot] for spot in width_offsets])
    height_set = {0: row_stack}
    if grid_h > 1:
        for off_height in (-1, 1):
            height_set[off_height] = passed_along(
                shortened(row_stack), "tile", -off_height * grid_w * group_count
            ).astype(row_stack.dtype)
    height_offsets = sorted(height_set)
    slab_stack = jnp.stack([height_set[spot] for spot in height_offsets])

    def fold_slab(state_now, slab_pairs, off_frame):
        for h_slot, off_height in enumerate(height_offsets):
            for w_slot, off_width in enumerate(width_offsets):
                if off_frame == 0 and off_height == 0 and (off_width == 0):
                    continue
                state_now = fold_block(
                    state_now,
                    query_heads,
                    slab_pairs[h_slot, w_slot, 0],
                    slab_pairs[h_slot, w_slot, 1],
                    keep_mask(off_frame, off_height, off_width),
                )
        return state_now

    running = fold_slab(running, slab_stack, 0)
    if grid_f > 1:
        for off_frame in (-1, 1):
            got_slab = passed_along(
                shortened(slab_stack), "tile", -off_frame * grid_h * grid_w * group_count
            ).astype(slab_stack.dtype)
            running = fold_slab(running, got_slab, off_frame)
    row_top, row_total, summed = running
    result = summed / row_total[:, :, None]
    result = jnp.transpose(result, (1, 0, 2)).reshape(tokens, lane_width)
    return result.astype(jnp.bfloat16)[None]


def solution(mesh):
    return jax.shard_map(
        shards,
        mesh=mesh,
        in_specs=(
            P(("req", "tile"), None, None),
            P(("req", "tile"), None, None),
            P(("req", "tile"), None, None),
            P(("req", "tile"), None),
            P(("req", "tile"), None),
            P(("req", "tile")),
        ),
        out_specs=P(("req", "tile"), None, None),
        check_vma=False,
    )
```

```python
import functools
import math

import jax
import jax.numpy as jnp
from jax import lax
from jax.experimental import pallas as pl
from jax.experimental.pallas import tpu as pltpu
from jax.sharding import PartitionSpec as P

TS = 8
HEAD_DIM = 128
HEAD_GROUPS = 4


MASKED = -1e30
EXP2_SCALE = math.log2(math.e) / math.sqrt(HEAD_DIM)


def passed_along(value, axis, steps):
    count = lax.axis_size(axis)
    first, last = (max(0, -steps), min(count, count - steps))
    return lax.ppermute(value, axis, [(source, source + steps) for source in range(first, last)])


def shortened(value):
    return jax.tree.map(lambda a: a.astype(jnp.bfloat16) if a.dtype == jnp.float32 else a, value)


def fold_block(running, query_heads, key_block, value_block, key_keep):
    row_top, row_total, summed = running
    head_count = query_heads.shape[1]
    key_heads = key_block.reshape(key_block.shape[0], head_count, HEAD_DIM)
    value_heads = value_block.reshape(value_block.shape[0], head_count, HEAD_DIM)
    scores = jnp.einsum("qhd,khd->hqk", query_heads, key_heads, preferred_element_type=jnp.float32)
    scores = scores * (1.0 / math.sqrt(HEAD_DIM))
    scores = jnp.where(key_keep[None, None, :], scores, MASKED)
    new_top = jnp.maximum(row_top, jnp.max(scores, axis=-1))
    scale_down = jnp.exp(row_top - new_top)
    exp_terms = jnp.where(key_keep[None, None, :], jnp.exp(scores - new_top[:, :, None]), 0.0)
    row_total = row_total * scale_down + jnp.sum(exp_terms, axis=-1)
    weights = exp_terms.astype(jnp.bfloat16)
    summed = summed * scale_down[:, :, None] + jnp.einsum(
        "hqk,khd->hqd", weights, value_heads, preferred_element_type=jnp.float32
    )
    return (new_top, row_total, summed)


def window_kernel(blocks, carry_in, finish, q_ref, *refs):
    block_count = len(blocks)
    source_refs = refs[:block_count]
    keep_refs = refs[block_count : 2 * block_count]
    rest = refs[2 * block_count :]
    lane_width, tokens = q_ref.shape
    head_count = lane_width // HEAD_DIM
    keeps = [
        jnp.broadcast_to(keep_refs[b][...], (keep_refs[b].shape[0], tokens)) > 0.5 for b in range(block_count)
    ]
    for h in range(head_count):
        lanes = slice(h * HEAD_DIM, (h + 1) * HEAD_DIM)
        query_t = q_ref[lanes, :]
        scores, value_tiles = [], []
        for b, (pair_form, key_at, value_at) in enumerate(blocks):
            if pair_form:
                key_tile = source_refs[b][key_at, :, lanes]
                value_tile = source_refs[b][value_at, :, lanes]
            else:
                key_tile = source_refs[b][:, (key_at + h) * HEAD_DIM : (key_at + h + 1) * HEAD_DIM]
                value_tile = source_refs[b][:, (value_at + h) * HEAD_DIM : (value_at + h + 1) * HEAD_DIM]
            s = jnp.dot(key_tile, query_t, preferred_element_type=jnp.float32)
            scores.append(jnp.where(keeps[b], s, MASKED))
            value_tiles.append(value_tile)
        top = scores[0].max(axis=0, keepdims=True)
        for s in scores[1:]:
            top = jnp.maximum(top, s.max(axis=0, keepdims=True))
        if carry_in:
            top_in = rest[0][h : h + 1, :]
            top = jnp.maximum(top, top_in)
            scale_down = jnp.exp2((top_in - top) * EXP2_SCALE)
            total = rest[0][head_count + h : head_count + h + 1, :] * scale_down
            summed = rest[1][lanes, :] * scale_down
        else:
            total = jnp.zeros_like(top)
            summed = None
        for b in range(block_count):
            terms = jnp.exp2((scores[b] - top) * EXP2_SCALE)
            total = total + terms.sum(axis=0, keepdims=True)
            part = lax.dot_general(
                value_tiles[b],
                terms.astype(jnp.bfloat16),
                (((0,), (0,)), ((), ())),
                preferred_element_type=jnp.float32,
            )
            summed = part if summed is None else summed + part
        outs = rest[2:] if carry_in else rest
        if finish:
            outs[0][:, lanes] = jnp.transpose(summed / total).astype(outs[0].dtype)
        else:
            outs[0][h : h + 1, :] = top
            outs[0][head_count + h : head_count + h + 1, :] = total
            outs[1][lanes, :] = summed


def window_attention(query_t, blocks, carry=None, finish=True):
    lane_width, tokens = query_t.shape
    head_count = lane_width // HEAD_DIM
    layout, sources, keeps = [], [], []
    key_total = 0
    for source, key_at, value_at, keep in blocks:
        key_total += keep.shape[0]
        layout.append((source.ndim == 3, key_at, value_at))
        sources.append(source)
        keeps.append(keep)
    stat_rows = -(-2 * head_count // 8) * 8
    stat_shape = jax.ShapeDtypeStruct((stat_rows, tokens), jnp.float32)
    if finish:
        out_shape = jax.ShapeDtypeStruct((tokens, lane_width), jnp.bfloat16)
        out_specs = pl.BlockSpec(memory_space=pltpu.VMEM)
    else:
        out_shape = (
            pltpu.VMEM(stat_shape.shape, stat_shape.dtype),
            pltpu.VMEM((lane_width, tokens), jnp.float32),
        )
        out_specs = tuple(pl.BlockSpec(memory_space=pltpu.VMEM) for _ in range(2))
    carry_args = () if carry is None else tuple(carry)
    operand_count = 1 + 2 * len(blocks) + len(carry_args)
    flops = 4 * tokens * key_total * lane_width
    moved = 2 * (2 * tokens * lane_width + 2 * key_total * lane_width) + 4 * 2 * tokens * (lane_width + 8)
    return pl.pallas_call(
        functools.partial(window_kernel, tuple(layout), carry is not None, finish),
        out_shape=out_shape,
        in_specs=[pl.BlockSpec(memory_space=pltpu.VMEM)] * operand_count,
        out_specs=out_specs,
        cost_estimate=pl.CostEstimate(
            flops=flops, transcendentals=tokens * key_total * head_count, bytes_accessed=moved
        ),
        compiler_params=pltpu.CompilerParams(vmem_limit_bytes=16 * 1024 * 1024),
    )(*[pltpu.with_memory_space_constraint(a, pltpu.VMEM) for a in (query_t, *sources, *keeps, *carry_args)])


def text_pieces(text_keys, text_values, text_mask, group_count, lane_width):
    count = lax.axis_size("tile")
    rows = text_keys.shape[0]
    flags = jnp.broadcast_to(text_mask.astype(jnp.bfloat16)[:, None], (rows, 128))
    per_group = jnp.stack(
        [
            jnp.concatenate(
                [
                    text_keys[:, g * lane_width : (g + 1) * lane_width],
                    text_values[:, g * lane_width : (g + 1) * lane_width],
                    flags,
                ],
                axis=1,
            )
            for g in range(group_count)
        ]
    )
    outgoing = jnp.tile(per_group, (count // group_count, 1, 1)).reshape(count * rows, 2 * lane_width + 128)
    got = lax.all_to_all(outgoing, "tile", 0, 0, tiled=True)
    return got, got[:, 2 * lane_width] > 0.5


def shards(queries, keys, values, text_keys, text_values, text_mask):
    tokens = queries.shape[1]
    lane_width = queries.shape[2]
    head_count = lane_width // HEAD_DIM
    query_heads = queries[0].reshape(tokens, head_count, HEAD_DIM)
    group_count = HEAD_GROUPS
    tiles_all = lax.axis_size("tile") // group_count
    grid_w = min(4, tiles_all)
    grid_h = min(4, tiles_all // grid_w)
    grid_f = tiles_all // (grid_w * grid_h)
    frames_valid = grid_f * TS - TS // 4
    my_index = lax.axis_index("tile")
    tile_id = my_index // group_count
    head_group = my_index % group_count
    w_pos = tile_id % grid_w
    h_pos = tile_id // grid_w % grid_h
    f_pos = tile_id // (grid_w * grid_h)
    key_rows = tokens
    if grid_f == 1:
        key_rows = min(tokens, frames_valid * TS * TS)
    own_pair = jnp.stack([keys[0, :key_rows], values[0, :key_rows]])
    local_frame = jnp.arange(key_rows, dtype=jnp.int32) // (TS * TS)

    def keep_mask(off_frame, off_height, off_width):
        inside = (
            (f_pos + off_frame >= 0)
            & (f_pos + off_frame < grid_f)
            & (h_pos + off_height >= 0)
            & (h_pos + off_height < grid_h)
            & (w_pos + off_width >= 0)
            & (w_pos + off_width < grid_w)
        )
        return inside & ((f_pos + off_frame) * TS + local_frame < frames_valid)

    running = (
        jnp.full((head_count, tokens), MASKED, jnp.float32),
        jnp.zeros((head_count, tokens), jnp.float32),
        jnp.zeros((head_count, tokens, HEAD_DIM), jnp.float32),
    )
    text_got, text_keep = text_pieces(text_keys, text_values, text_mask, group_count, lane_width)
    if grid_h == 1 and grid_f == 1:
        pieces = 2 if key_rows % 32 == 0 else 1
        step = key_rows // pieces
        spans = [(p * step, (p + 1) * step) for p in range(pieces)]
        own_parts = [jnp.stack([keys[0, a:b], values[0, a:b]]) for a, b in spans]
        as_row = lambda keep: keep.astype(jnp.float32)[:, None]

        def part_blocks(parts, off_width):
            keep = keep_mask(0, 0, off_width)
            return [(part, 0, 1, as_row(keep[a:b])) for part, (a, b) in zip(parts, spans)]

        got_parts = {
            off_width: [passed_along(part, "tile", -off_width * group_count) for part in own_parts]
            for off_width in (-1, 1)
        }
        query_t = jnp.transpose(queries[0])
        carry = window_attention(query_t, part_blocks(own_parts, 0), finish=False)
        carry = window_attention(
            query_t, [(text_got, 0, head_count, as_row(text_keep))], carry=carry, finish=False
        )
        carry = window_attention(query_t, part_blocks(got_parts[-1], -1), carry=carry, finish=False)
        return window_attention(query_t, part_blocks(got_parts[1], 1), carry=carry)[None]
    width_set = {0: own_pair}
    for off_width in (-1, 1):
        width_set[off_width] = passed_along(own_pair, "tile", -off_width * group_count)
    piece_keys = text_got[:, :lane_width]
    piece_values = text_got[:, lane_width : 2 * lane_width]
    running = fold_block(running, query_heads, piece_keys, piece_values, text_keep)
    running = fold_block(running, query_heads, own_pair[0], own_pair[1], keep_mask(0, 0, 0))
    width_offsets = sorted(width_set)
    row_stack = jnp.stack([width_set[spot] for spot in width_offsets])
    height_set = {0: row_stack}
    if grid_h > 1:
        for off_height in (-1, 1):
            height_set[off_height] = passed_along(
                shortened(row_stack), "tile", -off_height * grid_w * group_count
            ).astype(row_stack.dtype)
    height_offsets = sorted(height_set)
    slab_stack = jnp.stack([height_set[spot] for spot in height_offsets])

    def fold_slab(state_now, slab_pairs, off_frame):
        for h_slot, off_height in enumerate(height_offsets):
            for w_slot, off_width in enumerate(width_offsets):
                if off_frame == 0 and off_height == 0 and (off_width == 0):
                    continue
                state_now = fold_block(
                    state_now,
                    query_heads,
                    slab_pairs[h_slot, w_slot, 0],
                    slab_pairs[h_slot, w_slot, 1],
                    keep_mask(off_frame, off_height, off_width),
                )
        return state_now

    running = fold_slab(running, slab_stack, 0)
    if grid_f > 1:
        for off_frame in (-1, 1):
            got_slab = passed_along(
                shortened(slab_stack), "tile", -off_frame * grid_h * grid_w * group_count
            ).astype(slab_stack.dtype)
            running = fold_slab(running, got_slab, off_frame)
    row_top, row_total, summed = running
    result = summed / row_total[:, :, None]
    result = jnp.transpose(result, (1, 0, 2)).reshape(tokens, lane_width)
    return result.astype(jnp.bfloat16)[None]


def solution(mesh):
    return jax.shard_map(
        shards,
        mesh=mesh,
        in_specs=(
            P(("req", "tile"), None, None),
            P(("req", "tile"), None, None),
            P(("req", "tile"), None, None),
            P(("req", "tile"), None),
            P(("req", "tile"), None),
            P(("req", "tile")),
        ),
        out_specs=P(("req", "tile"), None, None),
        check_vma=False,
    )
```

```python
import functools
import math

import jax
import jax.numpy as jnp
from jax import lax
from jax.experimental import pallas as pl
from jax.experimental.pallas import tpu as pltpu
from jax.sharding import PartitionSpec as P

TS = 8
HEAD_DIM = 128
HEAD_GROUPS = 4


MASKED = -1e30
EXP2_SCALE = math.log2(math.e) / math.sqrt(HEAD_DIM)


def passed_along(value, axis, steps):
    count = lax.axis_size(axis)
    first, last = (max(0, -steps), min(count, count - steps))
    return lax.ppermute(value, axis, [(source, source + steps) for source in range(first, last)])


def shortened(value):
    return jax.tree.map(lambda a: a.astype(jnp.bfloat16) if a.dtype == jnp.float32 else a, value)


def fold_block(running, query_heads, key_block, value_block, key_keep):
    row_top, row_total, summed = running
    head_count = query_heads.shape[1]
    key_heads = key_block.reshape(key_block.shape[0], head_count, HEAD_DIM)
    value_heads = value_block.reshape(value_block.shape[0], head_count, HEAD_DIM)
    scores = jnp.einsum("qhd,khd->hqk", query_heads, key_heads, preferred_element_type=jnp.float32)
    scores = scores * (1.0 / math.sqrt(HEAD_DIM))
    scores = jnp.where(key_keep[None, None, :], scores, MASKED)
    new_top = jnp.maximum(row_top, jnp.max(scores, axis=-1))
    scale_down = jnp.exp(row_top - new_top)
    exp_terms = jnp.where(key_keep[None, None, :], jnp.exp(scores - new_top[:, :, None]), 0.0)
    row_total = row_total * scale_down + jnp.sum(exp_terms, axis=-1)
    weights = exp_terms.astype(jnp.bfloat16)
    summed = summed * scale_down[:, :, None] + jnp.einsum(
        "hqk,khd->hqd", weights, value_heads, preferred_element_type=jnp.float32
    )
    return (new_top, row_total, summed)


def window_kernel(blocks, carry_in, finish, q_ref, *refs):
    block_count = len(blocks)
    source_refs = refs[:block_count]
    keep_refs = refs[block_count : 2 * block_count]
    rest = refs[2 * block_count :]
    lane_width, tokens = q_ref.shape
    head_count = lane_width // HEAD_DIM
    keeps = [
        jnp.broadcast_to(keep_refs[b][...], (keep_refs[b].shape[0], tokens)) > 0.5 for b in range(block_count)
    ]
    for h in range(head_count):
        lanes = slice(h * HEAD_DIM, (h + 1) * HEAD_DIM)
        query_t = q_ref[lanes, :]
        scores, value_tiles = [], []
        for b, (pair_form, key_at, value_at) in enumerate(blocks):
            if pair_form:
                key_tile = source_refs[b][key_at, :, lanes]
                value_tile = source_refs[b][value_at, :, lanes]
            else:
                key_tile = source_refs[b][:, (key_at + h) * HEAD_DIM : (key_at + h + 1) * HEAD_DIM]
                value_tile = source_refs[b][:, (value_at + h) * HEAD_DIM : (value_at + h + 1) * HEAD_DIM]
            s = jnp.dot(key_tile, query_t, preferred_element_type=jnp.float32)
            scores.append(jnp.where(keeps[b], s, MASKED))
            value_tiles.append(value_tile)
        top = scores[0].max(axis=0, keepdims=True)
        for s in scores[1:]:
            top = jnp.maximum(top, s.max(axis=0, keepdims=True))
        if carry_in:
            top_in = rest[0][h : h + 1, :]
            top = jnp.maximum(top, top_in)
            scale_down = jnp.exp2((top_in - top) * EXP2_SCALE)
            total = rest[0][head_count + h : head_count + h + 1, :] * scale_down
            summed = rest[1][lanes, :] * scale_down
        else:
            total = jnp.zeros_like(top)
            summed = None
        for b in range(block_count):
            terms = jnp.exp2((scores[b] - top) * EXP2_SCALE)
            total = total + terms.sum(axis=0, keepdims=True)
            part = lax.dot_general(
                value_tiles[b],
                terms.astype(jnp.bfloat16),
                (((0,), (0,)), ((), ())),
                preferred_element_type=jnp.float32,
            )
            summed = part if summed is None else summed + part
        outs = rest[2:] if carry_in else rest
        if finish:
            outs[0][:, lanes] = jnp.transpose(summed / total).astype(outs[0].dtype)
        else:
            outs[0][h : h + 1, :] = top
            outs[0][head_count + h : head_count + h + 1, :] = total
            outs[1][lanes, :] = summed


def window_attention(query_t, blocks, carry=None, finish=True):
    lane_width, tokens = query_t.shape
    head_count = lane_width // HEAD_DIM
    layout, sources, keeps = [], [], []
    key_total = 0
    for source, key_at, value_at, keep in blocks:
        key_total += keep.shape[0]
        layout.append((source.ndim == 3, key_at, value_at))
        sources.append(source)
        keeps.append(keep)
    stat_rows = -(-2 * head_count // 8) * 8
    stat_shape = jax.ShapeDtypeStruct((stat_rows, tokens), jnp.float32)
    if finish:
        out_shape = jax.ShapeDtypeStruct((tokens, lane_width), jnp.bfloat16)
        out_specs = pl.BlockSpec(memory_space=pltpu.VMEM)
    else:
        out_shape = (
            pltpu.VMEM(stat_shape.shape, stat_shape.dtype),
            pltpu.VMEM((lane_width, tokens), jnp.float32),
        )
        out_specs = tuple(pl.BlockSpec(memory_space=pltpu.VMEM) for _ in range(2))
    carry_args = () if carry is None else tuple(carry)
    operand_count = 1 + 2 * len(blocks) + len(carry_args)
    flops = 4 * tokens * key_total * lane_width
    moved = 2 * (2 * tokens * lane_width + 2 * key_total * lane_width) + 4 * 2 * tokens * (lane_width + 8)
    return pl.pallas_call(
        functools.partial(window_kernel, tuple(layout), carry is not None, finish),
        out_shape=out_shape,
        in_specs=[pl.BlockSpec(memory_space=pltpu.VMEM)] * operand_count,
        out_specs=out_specs,
        cost_estimate=pl.CostEstimate(
            flops=flops, transcendentals=tokens * key_total * head_count, bytes_accessed=moved
        ),
        compiler_params=pltpu.CompilerParams(vmem_limit_bytes=16 * 1024 * 1024),
    )(*[pltpu.with_memory_space_constraint(a, pltpu.VMEM) for a in (query_t, *sources, *keeps, *carry_args)])


def payload_kernel(group_count, lane_width, mask_ref, key_ref, value_ref, out_ref):
    rows = key_ref.shape[0]
    row_at = lax.broadcasted_iota(jnp.int32, (rows, 128), 0)
    flags = jnp.zeros((rows, 128), jnp.float32)
    for r in range(rows):
        flags = jnp.where(row_at == r, mask_ref[r].astype(jnp.float32), flags)
    flags = flags.astype(out_ref.dtype)
    for j in range(out_ref.shape[0]):
        g = j % group_count
        out_ref[j, :, :lane_width] = key_ref[:, g * lane_width : (g + 1) * lane_width]
        out_ref[j, :, lane_width : 2 * lane_width] = value_ref[:, g * lane_width : (g + 1) * lane_width]
        out_ref[j, :, 2 * lane_width :] = flags


def text_pieces(text_keys, text_values, text_mask, group_count, lane_width):
    count = lax.axis_size("tile")
    rows = text_keys.shape[0]
    width = 2 * lane_width + 128
    outgoing = pl.pallas_call(
        functools.partial(payload_kernel, group_count, lane_width),
        out_shape=jax.ShapeDtypeStruct((count, rows, width), jnp.bfloat16),
        in_specs=[
            pl.BlockSpec(memory_space=pltpu.SMEM),
            pl.BlockSpec(memory_space=pltpu.VMEM),
            pl.BlockSpec(memory_space=pltpu.VMEM),
        ],
        out_specs=pl.BlockSpec(memory_space=pltpu.VMEM),
    )(text_mask, text_keys, text_values).reshape(count * rows, width)
    got = lax.all_to_all(outgoing, "tile", 0, 0, tiled=True)
    return got, got[:, 2 * lane_width] > 0.5


def shards(queries, keys, values, text_keys, text_values, text_mask):
    tokens = queries.shape[1]
    lane_width = queries.shape[2]
    head_count = lane_width // HEAD_DIM
    query_heads = queries[0].reshape(tokens, head_count, HEAD_DIM)
    group_count = HEAD_GROUPS
    tiles_all = lax.axis_size("tile") // group_count
    grid_w = min(4, tiles_all)
    grid_h = min(4, tiles_all // grid_w)
    grid_f = tiles_all // (grid_w * grid_h)
    frames_valid = grid_f * TS - TS // 4
    my_index = lax.axis_index("tile")
    tile_id = my_index // group_count
    head_group = my_index % group_count
    w_pos = tile_id % grid_w
    h_pos = tile_id // grid_w % grid_h
    f_pos = tile_id // (grid_w * grid_h)
    key_rows = tokens
    if grid_f == 1:
        key_rows = min(tokens, frames_valid * TS * TS)
    own_pair = jnp.stack([keys[0, :key_rows], values[0, :key_rows]])
    local_frame = jnp.arange(key_rows, dtype=jnp.int32) // (TS * TS)

    def keep_mask(off_frame, off_height, off_width):
        inside = (
            (f_pos + off_frame >= 0)
            & (f_pos + off_frame < grid_f)
            & (h_pos + off_height >= 0)
            & (h_pos + off_height < grid_h)
            & (w_pos + off_width >= 0)
            & (w_pos + off_width < grid_w)
        )
        return inside & ((f_pos + off_frame) * TS + local_frame < frames_valid)

    running = (
        jnp.full((head_count, tokens), MASKED, jnp.float32),
        jnp.zeros((head_count, tokens), jnp.float32),
        jnp.zeros((head_count, tokens, HEAD_DIM), jnp.float32),
    )
    text_got, text_keep = text_pieces(text_keys, text_values, text_mask, group_count, lane_width)
    width_set = {0: own_pair}
    for off_width in (-1, 1):
        width_set[off_width] = passed_along(own_pair, "tile", -off_width * group_count)
    if grid_h == 1 and grid_f == 1:
        as_row = lambda keep: keep.astype(jnp.float32)[:, None]
        query_t = jnp.transpose(queries[0])
        carry = window_attention(query_t, [(own_pair, 0, 1, as_row(keep_mask(0, 0, 0)))], finish=False)
        carry = window_attention(
            query_t, [(text_got, 0, head_count, as_row(text_keep))], carry=carry, finish=False
        )
        blocks = [(width_set[-1], 0, 1, as_row(keep_mask(0, 0, -1)))]
        carry = window_attention(query_t, blocks, carry=carry, finish=False)
        blocks = [(width_set[1], 0, 1, as_row(keep_mask(0, 0, 1)))]
        return window_attention(query_t, blocks, carry=carry)[None]
    piece_keys = text_got[:, :lane_width]
    piece_values = text_got[:, lane_width : 2 * lane_width]
    running = fold_block(running, query_heads, piece_keys, piece_values, text_keep)
    running = fold_block(running, query_heads, own_pair[0], own_pair[1], keep_mask(0, 0, 0))
    width_offsets = sorted(width_set)
    row_stack = jnp.stack([width_set[spot] for spot in width_offsets])
    height_set = {0: row_stack}
    if grid_h > 1:
        for off_height in (-1, 1):
            height_set[off_height] = passed_along(
                shortened(row_stack), "tile", -off_height * grid_w * group_count
            ).astype(row_stack.dtype)
    height_offsets = sorted(height_set)
    slab_stack = jnp.stack([height_set[spot] for spot in height_offsets])

    def fold_slab(state_now, slab_pairs, off_frame):
        for h_slot, off_height in enumerate(height_offsets):
            for w_slot, off_width in enumerate(width_offsets):
                if off_frame == 0 and off_height == 0 and (off_width == 0):
                    continue
                state_now = fold_block(
                    state_now,
                    query_heads,
                    slab_pairs[h_slot, w_slot, 0],
                    slab_pairs[h_slot, w_slot, 1],
                    keep_mask(off_frame, off_height, off_width),
                )
        return state_now

    running = fold_slab(running, slab_stack, 0)
    if grid_f > 1:
        for off_frame in (-1, 1):
            got_slab = passed_along(
                shortened(slab_stack), "tile", -off_frame * grid_h * grid_w * group_count
            ).astype(slab_stack.dtype)
            running = fold_slab(running, got_slab, off_frame)
    row_top, row_total, summed = running
    result = summed / row_total[:, :, None]
    result = jnp.transpose(result, (1, 0, 2)).reshape(tokens, lane_width)
    return result.astype(jnp.bfloat16)[None]


def solution(mesh):
    return jax.shard_map(
        shards,
        mesh=mesh,
        in_specs=(
            P(("req", "tile"), None, None),
            P(("req", "tile"), None, None),
            P(("req", "tile"), None, None),
            P(("req", "tile"), None),
            P(("req", "tile"), None),
            P(("req", "tile")),
        ),
        out_specs=P(("req", "tile"), None, None),
        check_vma=False,
    )
```

```python
import functools
import math

import jax
import jax.numpy as jnp
from jax import lax
from jax.experimental import pallas as pl
from jax.experimental.pallas import tpu as pltpu
from jax.sharding import PartitionSpec as P

TS = 8
HEAD_DIM = 128
HEAD_GROUPS = 4


MASKED = -1e30
EXP2_SCALE = math.log2(math.e) / math.sqrt(HEAD_DIM)


def passed_along(value, axis, steps):
    count = lax.axis_size(axis)
    first, last = (max(0, -steps), min(count, count - steps))
    return lax.ppermute(value, axis, [(source, source + steps) for source in range(first, last)])


def shortened(value):
    return jax.tree.map(lambda a: a.astype(jnp.bfloat16) if a.dtype == jnp.float32 else a, value)


def fold_block(running, query_heads, key_block, value_block, key_keep):
    row_top, row_total, summed = running
    head_count = query_heads.shape[1]
    key_heads = key_block.reshape(key_block.shape[0], head_count, HEAD_DIM)
    value_heads = value_block.reshape(value_block.shape[0], head_count, HEAD_DIM)
    scores = jnp.einsum("qhd,khd->hqk", query_heads, key_heads, preferred_element_type=jnp.float32)
    scores = scores * (1.0 / math.sqrt(HEAD_DIM))
    scores = jnp.where(key_keep[None, None, :], scores, MASKED)
    new_top = jnp.maximum(row_top, jnp.max(scores, axis=-1))
    scale_down = jnp.exp(row_top - new_top)
    exp_terms = jnp.where(key_keep[None, None, :], jnp.exp(scores - new_top[:, :, None]), 0.0)
    row_total = row_total * scale_down + jnp.sum(exp_terms, axis=-1)
    weights = exp_terms.astype(jnp.bfloat16)
    summed = summed * scale_down[:, :, None] + jnp.einsum(
        "hqk,khd->hqd", weights, value_heads, preferred_element_type=jnp.float32
    )
    return (new_top, row_total, summed)


def window_kernel(blocks, carry_in, finish, q_ref, *refs):
    block_count = len(blocks)
    source_refs = refs[:block_count]
    keep_refs = refs[block_count : 2 * block_count]
    rest = refs[2 * block_count :]
    lane_width, tokens = q_ref.shape
    head_count = lane_width // HEAD_DIM
    keeps = [
        jnp.broadcast_to(keep_refs[b][...], (keep_refs[b].shape[0], tokens)) > 0.5 for b in range(block_count)
    ]
    for h in range(head_count):
        lanes = slice(h * HEAD_DIM, (h + 1) * HEAD_DIM)
        query_t = q_ref[lanes, :]
        scores, value_tiles = [], []
        for b, (pair_form, key_at, value_at) in enumerate(blocks):
            if pair_form:
                key_tile = source_refs[b][key_at, :, lanes]
                value_tile = source_refs[b][value_at, :, lanes]
            else:
                key_tile = source_refs[b][:, (key_at + h) * HEAD_DIM : (key_at + h + 1) * HEAD_DIM]
                value_tile = source_refs[b][:, (value_at + h) * HEAD_DIM : (value_at + h + 1) * HEAD_DIM]
            s = jnp.dot(key_tile, query_t, preferred_element_type=jnp.float32)
            scores.append(jnp.where(keeps[b], s, MASKED))
            value_tiles.append(value_tile)
        top = scores[0].max(axis=0, keepdims=True)
        for s in scores[1:]:
            top = jnp.maximum(top, s.max(axis=0, keepdims=True))
        if carry_in:
            top_in = rest[0][h : h + 1, :]
            top = jnp.maximum(top, top_in)
            scale_down = jnp.exp2((top_in - top) * EXP2_SCALE)
            total = rest[0][head_count + h : head_count + h + 1, :] * scale_down
            summed = rest[1][lanes, :] * scale_down
        else:
            total = jnp.zeros_like(top)
            summed = None
        for b in range(block_count):
            terms = jnp.exp2((scores[b] - top) * EXP2_SCALE)
            total = total + terms.sum(axis=0, keepdims=True)
            part = lax.dot_general(
                value_tiles[b],
                terms.astype(jnp.bfloat16),
                (((0,), (0,)), ((), ())),
                preferred_element_type=jnp.float32,
            )
            summed = part if summed is None else summed + part
        outs = rest[2:] if carry_in else rest
        if finish:
            outs[0][:, lanes] = jnp.transpose(summed / total).astype(outs[0].dtype)
        else:
            outs[0][h : h + 1, :] = top
            outs[0][head_count + h : head_count + h + 1, :] = total
            outs[1][lanes, :] = summed


def window_attention(query_t, blocks, carry=None, finish=True):
    lane_width, tokens = query_t.shape
    head_count = lane_width // HEAD_DIM
    layout, sources, keeps = [], [], []
    key_total = 0
    for source, key_at, value_at, keep in blocks:
        key_total += keep.shape[0]
        layout.append((source.ndim == 3, key_at, value_at))
        sources.append(source)
        keeps.append(keep)
    stat_rows = -(-2 * head_count // 8) * 8
    stat_shape = jax.ShapeDtypeStruct((stat_rows, tokens), jnp.float32)
    if finish:
        out_shape = jax.ShapeDtypeStruct((tokens, lane_width), jnp.bfloat16)
        out_specs = pl.BlockSpec(memory_space=pltpu.VMEM)
    else:
        out_shape = (
            pltpu.VMEM(stat_shape.shape, stat_shape.dtype),
            pltpu.VMEM((lane_width, tokens), jnp.float32),
        )
        out_specs = tuple(pl.BlockSpec(memory_space=pltpu.VMEM) for _ in range(2))
    carry_args = () if carry is None else tuple(carry)
    operand_count = 1 + 2 * len(blocks) + len(carry_args)
    flops = 4 * tokens * key_total * lane_width
    moved = 2 * (2 * tokens * lane_width + 2 * key_total * lane_width) + 4 * 2 * tokens * (lane_width + 8)
    return pl.pallas_call(
        functools.partial(window_kernel, tuple(layout), carry is not None, finish),
        out_shape=out_shape,
        in_specs=[pl.BlockSpec(memory_space=pltpu.VMEM)] * operand_count,
        out_specs=out_specs,
        cost_estimate=pl.CostEstimate(
            flops=flops, transcendentals=tokens * key_total * head_count, bytes_accessed=moved
        ),
        compiler_params=pltpu.CompilerParams(vmem_limit_bytes=16 * 1024 * 1024),
    )(*[pltpu.with_memory_space_constraint(a, pltpu.VMEM) for a in (query_t, *sources, *keeps, *carry_args)])


def payload_kernel(group_count, lane_width, mask_ref, key_ref, value_ref, *refs):
    if len(refs) == 4:
        own_keys, own_values, out_ref, pair_ref = refs
        pair_ref[0] = own_keys[: pair_ref.shape[1], :]
        pair_ref[1] = own_values[: pair_ref.shape[1], :]
    else:
        (out_ref,) = refs
    rows = key_ref.shape[0]
    row_at = lax.broadcasted_iota(jnp.int32, (rows, 128), 0)
    flags = jnp.zeros((rows, 128), jnp.float32)
    for r in range(rows):
        flags = jnp.where(row_at == r, mask_ref[r].astype(jnp.float32), flags)
    flags = flags.astype(out_ref.dtype)
    for j in range(out_ref.shape[0]):
        g = j % group_count
        out_ref[j, :, :lane_width] = key_ref[:, g * lane_width : (g + 1) * lane_width]
        out_ref[j, :, lane_width : 2 * lane_width] = value_ref[:, g * lane_width : (g + 1) * lane_width]
        out_ref[j, :, 2 * lane_width :] = flags


def text_pieces(text_keys, text_values, text_mask, group_count, lane_width, own=None):
    count = lax.axis_size("tile")
    rows = text_keys.shape[0]
    width = 2 * lane_width + 128
    vmem = pl.BlockSpec(memory_space=pltpu.VMEM)
    out_shape = jax.ShapeDtypeStruct((count, rows, width), jnp.bfloat16)
    extra = ()
    if own is not None:
        own_keys, own_values, key_rows = own
        extra = (own_keys, own_values)
        out_shape = (out_shape, jax.ShapeDtypeStruct((2, key_rows, own_keys.shape[1]), own_keys.dtype))
    made = pl.pallas_call(
        functools.partial(payload_kernel, group_count, lane_width),
        out_shape=out_shape,
        in_specs=[pl.BlockSpec(memory_space=pltpu.SMEM)] + [vmem] * (2 + len(extra)),
        out_specs=vmem if own is None else (vmem, vmem),
    )(text_mask, text_keys, text_values, *extra)
    own_pair = None
    if own is not None:
        made, own_pair = made
    outgoing = made.reshape(count * rows, width)
    got = lax.all_to_all(outgoing, "tile", 0, 0, tiled=True)
    if own is not None:
        return got, got[:, 2 * lane_width] > 0.5, own_pair
    return got, got[:, 2 * lane_width] > 0.5


def shards(queries, keys, values, text_keys, text_values, text_mask):
    tokens = queries.shape[1]
    lane_width = queries.shape[2]
    head_count = lane_width // HEAD_DIM
    query_heads = queries[0].reshape(tokens, head_count, HEAD_DIM)
    group_count = HEAD_GROUPS
    tiles_all = lax.axis_size("tile") // group_count
    grid_w = min(4, tiles_all)
    grid_h = min(4, tiles_all // grid_w)
    grid_f = tiles_all // (grid_w * grid_h)
    frames_valid = grid_f * TS - TS // 4
    my_index = lax.axis_index("tile")
    tile_id = my_index // group_count
    head_group = my_index % group_count
    w_pos = tile_id % grid_w
    h_pos = tile_id // grid_w % grid_h
    f_pos = tile_id // (grid_w * grid_h)
    key_rows = tokens
    if grid_f == 1:
        key_rows = min(tokens, frames_valid * TS * TS)
    own_pair = jnp.stack([keys[0, :key_rows], values[0, :key_rows]])
    local_frame = jnp.arange(key_rows, dtype=jnp.int32) // (TS * TS)

    def keep_mask(off_frame, off_height, off_width):
        inside = (
            (f_pos + off_frame >= 0)
            & (f_pos + off_frame < grid_f)
            & (h_pos + off_height >= 0)
            & (h_pos + off_height < grid_h)
            & (w_pos + off_width >= 0)
            & (w_pos + off_width < grid_w)
        )
        return inside & ((f_pos + off_frame) * TS + local_frame < frames_valid)

    running = (
        jnp.full((head_count, tokens), MASKED, jnp.float32),
        jnp.zeros((head_count, tokens), jnp.float32),
        jnp.zeros((head_count, tokens, HEAD_DIM), jnp.float32),
    )
    if grid_h == 1 and grid_f == 1:
        text_got, text_keep, own_pair = text_pieces(
            text_keys, text_values, text_mask, group_count, lane_width, (keys[0], values[0], key_rows)
        )
    else:
        text_got, text_keep = text_pieces(text_keys, text_values, text_mask, group_count, lane_width)
    width_set = {0: own_pair}
    for off_width in (-1, 1):
        width_set[off_width] = passed_along(own_pair, "tile", -off_width * group_count)
    if grid_h == 1 and grid_f == 1:
        as_row = lambda keep: keep.astype(jnp.float32)[:, None]
        query_t = jnp.transpose(queries[0])
        carry = window_attention(query_t, [(own_pair, 0, 1, as_row(keep_mask(0, 0, 0)))], finish=False)
        carry = window_attention(
            query_t, [(text_got, 0, head_count, as_row(text_keep))], carry=carry, finish=False
        )
        blocks = [(width_set[-1], 0, 1, as_row(keep_mask(0, 0, -1)))]
        carry = window_attention(query_t, blocks, carry=carry, finish=False)
        blocks = [(width_set[1], 0, 1, as_row(keep_mask(0, 0, 1)))]
        return window_attention(query_t, blocks, carry=carry)[None]
    piece_keys = text_got[:, :lane_width]
    piece_values = text_got[:, lane_width : 2 * lane_width]
    running = fold_block(running, query_heads, piece_keys, piece_values, text_keep)
    running = fold_block(running, query_heads, own_pair[0], own_pair[1], keep_mask(0, 0, 0))
    width_offsets = sorted(width_set)
    row_stack = jnp.stack([width_set[spot] for spot in width_offsets])
    height_set = {0: row_stack}
    if grid_h > 1:
        for off_height in (-1, 1):
            height_set[off_height] = passed_along(
                shortened(row_stack), "tile", -off_height * grid_w * group_count
            ).astype(row_stack.dtype)
    height_offsets = sorted(height_set)
    slab_stack = jnp.stack([height_set[spot] for spot in height_offsets])

    def fold_slab(state_now, slab_pairs, off_frame):
        for h_slot, off_height in enumerate(height_offsets):
            for w_slot, off_width in enumerate(width_offsets):
                if off_frame == 0 and off_height == 0 and (off_width == 0):
                    continue
                state_now = fold_block(
                    state_now,
                    query_heads,
                    slab_pairs[h_slot, w_slot, 0],
                    slab_pairs[h_slot, w_slot, 1],
                    keep_mask(off_frame, off_height, off_width),
                )
        return state_now

    running = fold_slab(running, slab_stack, 0)
    if grid_f > 1:
        for off_frame in (-1, 1):
            got_slab = passed_along(
                shortened(slab_stack), "tile", -off_frame * grid_h * grid_w * group_count
            ).astype(slab_stack.dtype)
            running = fold_slab(running, got_slab, off_frame)
    row_top, row_total, summed = running
    result = summed / row_total[:, :, None]
    result = jnp.transpose(result, (1, 0, 2)).reshape(tokens, lane_width)
    return result.astype(jnp.bfloat16)[None]


def solution(mesh):
    return jax.shard_map(
        shards,
        mesh=mesh,
        in_specs=(
            P(("req", "tile"), None, None),
            P(("req", "tile"), None, None),
            P(("req", "tile"), None, None),
            P(("req", "tile"), None),
            P(("req", "tile"), None),
            P(("req", "tile")),
        ),
        out_specs=P(("req", "tile"), None, None),
        check_vma=False,
    )
```

```python
import functools
import math

import jax
import jax.numpy as jnp
from jax import lax
from jax.experimental import pallas as pl
from jax.experimental.pallas import tpu as pltpu
from jax.sharding import PartitionSpec as P

TS = 8
HEAD_DIM = 128
HEAD_GROUPS = 4


MASKED = -1e30
EXP2_SCALE = math.log2(math.e) / math.sqrt(HEAD_DIM)


def passed_along(value, axis, steps):
    count = lax.axis_size(axis)
    first, last = (max(0, -steps), min(count, count - steps))
    return lax.ppermute(value, axis, [(source, source + steps) for source in range(first, last)])


def shortened(value):
    return jax.tree.map(lambda a: a.astype(jnp.bfloat16) if a.dtype == jnp.float32 else a, value)


def fold_block(running, query_heads, key_block, value_block, key_keep):
    row_top, row_total, summed = running
    head_count = query_heads.shape[1]
    key_heads = key_block.reshape(key_block.shape[0], head_count, HEAD_DIM)
    value_heads = value_block.reshape(value_block.shape[0], head_count, HEAD_DIM)
    scores = jnp.einsum("qhd,khd->hqk", query_heads, key_heads, preferred_element_type=jnp.float32)
    scores = scores * (1.0 / math.sqrt(HEAD_DIM))
    scores = jnp.where(key_keep[None, None, :], scores, MASKED)
    new_top = jnp.maximum(row_top, jnp.max(scores, axis=-1))
    scale_down = jnp.exp(row_top - new_top)
    exp_terms = jnp.where(key_keep[None, None, :], jnp.exp(scores - new_top[:, :, None]), 0.0)
    row_total = row_total * scale_down + jnp.sum(exp_terms, axis=-1)
    weights = exp_terms.astype(jnp.bfloat16)
    summed = summed * scale_down[:, :, None] + jnp.einsum(
        "hqk,khd->hqd", weights, value_heads, preferred_element_type=jnp.float32
    )
    return (new_top, row_total, summed)


def window_kernel(blocks, carry_in, finish, q_ref, *refs):
    block_count = len(blocks)
    source_refs = refs[:block_count]
    keep_refs = refs[block_count : 2 * block_count]
    rest = refs[2 * block_count :]
    lane_width, tokens = q_ref.shape
    head_count = lane_width // HEAD_DIM
    keeps = [
        jnp.broadcast_to(keep_refs[b][...], (keep_refs[b].shape[0], tokens)) > 0.5 for b in range(block_count)
    ]
    for h in range(head_count):
        lanes = slice(h * HEAD_DIM, (h + 1) * HEAD_DIM)
        query_t = q_ref[lanes, :]
        scores, value_tiles = [], []
        for b, (pair_form, key_at, value_at) in enumerate(blocks):
            if pair_form:
                key_tile = source_refs[b][key_at, :, lanes]
                value_tile = source_refs[b][value_at, :, lanes]
            else:
                key_tile = source_refs[b][:, (key_at + h) * HEAD_DIM : (key_at + h + 1) * HEAD_DIM]
                value_tile = source_refs[b][:, (value_at + h) * HEAD_DIM : (value_at + h + 1) * HEAD_DIM]
            s = jnp.dot(key_tile, query_t, preferred_element_type=jnp.float32)
            scores.append(jnp.where(keeps[b], s, MASKED))
            value_tiles.append(value_tile)
        top = scores[0].max(axis=0, keepdims=True)
        for s in scores[1:]:
            top = jnp.maximum(top, s.max(axis=0, keepdims=True))
        if carry_in:
            top_in = rest[0][h : h + 1, :]
            top = jnp.maximum(top, top_in)
            scale_down = jnp.exp2((top_in - top) * EXP2_SCALE)
            total = rest[0][head_count + h : head_count + h + 1, :] * scale_down
            summed = rest[1][lanes, :] * scale_down
        else:
            total = jnp.zeros_like(top)
            summed = None
        for b in range(block_count):
            terms = jnp.exp2((scores[b] - top) * EXP2_SCALE)
            total = total + terms.sum(axis=0, keepdims=True)
            part = lax.dot_general(
                value_tiles[b],
                terms.astype(jnp.bfloat16),
                (((0,), (0,)), ((), ())),
                preferred_element_type=jnp.float32,
            )
            summed = part if summed is None else summed + part
        outs = rest[2:] if carry_in else rest
        if finish:
            staged, sems = rest[-2], rest[-1]
            staged[:, lanes] = jnp.transpose(summed / total).astype(staged.dtype)
            copy = pltpu.make_async_copy(staged.at[:, lanes], outs[0].at[:, lanes], sems.at[h])
            copy.start()
            if h == head_count - 1:
                for k in range(head_count):
                    done = slice(k * HEAD_DIM, (k + 1) * HEAD_DIM)
                    pltpu.make_async_copy(staged.at[:, done], outs[0].at[:, done], sems.at[k]).wait()
        else:
            outs[0][h : h + 1, :] = top
            outs[0][head_count + h : head_count + h + 1, :] = total
            outs[1][lanes, :] = summed


def window_attention(query_t, blocks, carry=None, finish=True):
    lane_width, tokens = query_t.shape
    head_count = lane_width // HEAD_DIM
    layout, sources, keeps = [], [], []
    key_total = 0
    for source, key_at, value_at, keep in blocks:
        key_total += keep.shape[0]
        layout.append((source.ndim == 3, key_at, value_at))
        sources.append(source)
        keeps.append(keep)
    stat_rows = -(-2 * head_count // 8) * 8
    stat_shape = jax.ShapeDtypeStruct((stat_rows, tokens), jnp.float32)
    scratch = []
    if finish:
        out_shape = jax.ShapeDtypeStruct((tokens, lane_width), jnp.bfloat16)
        out_specs = pl.BlockSpec(memory_space=pl.ANY)
        scratch = [pltpu.VMEM((tokens, lane_width), jnp.bfloat16), pltpu.SemaphoreType.DMA((head_count,))]
    else:
        out_shape = (
            pltpu.VMEM(stat_shape.shape, stat_shape.dtype),
            pltpu.VMEM((lane_width, tokens), jnp.float32),
        )
        out_specs = tuple(pl.BlockSpec(memory_space=pltpu.VMEM) for _ in range(2))
    carry_args = () if carry is None else tuple(carry)
    operand_count = 1 + 2 * len(blocks) + len(carry_args)
    flops = 4 * tokens * key_total * lane_width
    moved = 2 * (2 * tokens * lane_width + 2 * key_total * lane_width) + 4 * 2 * tokens * (lane_width + 8)
    return pl.pallas_call(
        functools.partial(window_kernel, tuple(layout), carry is not None, finish),
        out_shape=out_shape,
        in_specs=[pl.BlockSpec(memory_space=pltpu.VMEM)] * operand_count,
        out_specs=out_specs,
        scratch_shapes=scratch,
        cost_estimate=pl.CostEstimate(
            flops=flops, transcendentals=tokens * key_total * head_count, bytes_accessed=moved
        ),
        compiler_params=pltpu.CompilerParams(vmem_limit_bytes=16 * 1024 * 1024),
    )(*[pltpu.with_memory_space_constraint(a, pltpu.VMEM) for a in (query_t, *sources, *keeps, *carry_args)])


def payload_kernel(group_count, lane_width, mask_ref, key_ref, value_ref, out_ref):
    rows = key_ref.shape[0]
    row_at = lax.broadcasted_iota(jnp.int32, (rows, 128), 0)
    flags = jnp.zeros((rows, 128), jnp.float32)
    for r in range(rows):
        flags = jnp.where(row_at == r, mask_ref[r].astype(jnp.float32), flags)
    flags = flags.astype(out_ref.dtype)
    for j in range(out_ref.shape[0]):
        g = j % group_count
        out_ref[j, :, :lane_width] = key_ref[:, g * lane_width : (g + 1) * lane_width]
        out_ref[j, :, lane_width : 2 * lane_width] = value_ref[:, g * lane_width : (g + 1) * lane_width]
        out_ref[j, :, 2 * lane_width :] = flags


def text_pieces(text_keys, text_values, text_mask, group_count, lane_width):
    count = lax.axis_size("tile")
    rows = text_keys.shape[0]
    width = 2 * lane_width + 128
    outgoing = pl.pallas_call(
        functools.partial(payload_kernel, group_count, lane_width),
        out_shape=jax.ShapeDtypeStruct((count, rows, width), jnp.bfloat16),
        in_specs=[
            pl.BlockSpec(memory_space=pltpu.SMEM),
            pl.BlockSpec(memory_space=pltpu.VMEM),
            pl.BlockSpec(memory_space=pltpu.VMEM),
        ],
        out_specs=pl.BlockSpec(memory_space=pltpu.VMEM),
    )(text_mask, text_keys, text_values).reshape(count * rows, width)
    got = lax.all_to_all(outgoing, "tile", 0, 0, tiled=True)
    return got, got[:, 2 * lane_width] > 0.5


def shards(queries, keys, values, text_keys, text_values, text_mask):
    tokens = queries.shape[1]
    lane_width = queries.shape[2]
    head_count = lane_width // HEAD_DIM
    query_heads = queries[0].reshape(tokens, head_count, HEAD_DIM)
    group_count = HEAD_GROUPS
    tiles_all = lax.axis_size("tile") // group_count
    grid_w = min(4, tiles_all)
    grid_h = min(4, tiles_all // grid_w)
    grid_f = tiles_all // (grid_w * grid_h)
    frames_valid = grid_f * TS - TS // 4
    my_index = lax.axis_index("tile")
    tile_id = my_index // group_count
    head_group = my_index % group_count
    w_pos = tile_id % grid_w
    h_pos = tile_id // grid_w % grid_h
    f_pos = tile_id // (grid_w * grid_h)
    key_rows = tokens
    if grid_f == 1:
        key_rows = min(tokens, frames_valid * TS * TS)
    own_pair = jnp.stack([keys[0, :key_rows], values[0, :key_rows]])
    local_frame = jnp.arange(key_rows, dtype=jnp.int32) // (TS * TS)

    def keep_mask(off_frame, off_height, off_width):
        inside = (
            (f_pos + off_frame >= 0)
            & (f_pos + off_frame < grid_f)
            & (h_pos + off_height >= 0)
            & (h_pos + off_height < grid_h)
            & (w_pos + off_width >= 0)
            & (w_pos + off_width < grid_w)
        )
        return inside & ((f_pos + off_frame) * TS + local_frame < frames_valid)

    running = (
        jnp.full((head_count, tokens), MASKED, jnp.float32),
        jnp.zeros((head_count, tokens), jnp.float32),
        jnp.zeros((head_count, tokens, HEAD_DIM), jnp.float32),
    )
    text_got, text_keep = text_pieces(text_keys, text_values, text_mask, group_count, lane_width)
    width_set = {0: own_pair}
    for off_width in (-1, 1):
        width_set[off_width] = passed_along(own_pair, "tile", -off_width * group_count)
    if grid_h == 1 and grid_f == 1:
        as_row = lambda keep: keep.astype(jnp.float32)[:, None]
        query_t = jnp.transpose(queries[0])
        carry = window_attention(query_t, [(own_pair, 0, 1, as_row(keep_mask(0, 0, 0)))], finish=False)
        carry = window_attention(
            query_t, [(text_got, 0, head_count, as_row(text_keep))], carry=carry, finish=False
        )
        blocks = [(width_set[-1], 0, 1, as_row(keep_mask(0, 0, -1)))]
        carry = window_attention(query_t, blocks, carry=carry, finish=False)
        blocks = [(width_set[1], 0, 1, as_row(keep_mask(0, 0, 1)))]
        return window_attention(query_t, blocks, carry=carry)[None]
    piece_keys = text_got[:, :lane_width]
    piece_values = text_got[:, lane_width : 2 * lane_width]
    running = fold_block(running, query_heads, piece_keys, piece_values, text_keep)
    running = fold_block(running, query_heads, own_pair[0], own_pair[1], keep_mask(0, 0, 0))
    width_offsets = sorted(width_set)
    row_stack = jnp.stack([width_set[spot] for spot in width_offsets])
    height_set = {0: row_stack}
    if grid_h > 1:
        for off_height in (-1, 1):
            height_set[off_height] = passed_along(
                shortened(row_stack), "tile", -off_height * grid_w * group_count
            ).astype(row_stack.dtype)
    height_offsets = sorted(height_set)
    slab_stack = jnp.stack([height_set[spot] for spot in height_offsets])

    def fold_slab(state_now, slab_pairs, off_frame):
        for h_slot, off_height in enumerate(height_offsets):
            for w_slot, off_width in enumerate(width_offsets):
                if off_frame == 0 and off_height == 0 and (off_width == 0):
                    continue
                state_now = fold_block(
                    state_now,
                    query_heads,
                    slab_pairs[h_slot, w_slot, 0],
                    slab_pairs[h_slot, w_slot, 1],
                    keep_mask(off_frame, off_height, off_width),
                )
        return state_now

    running = fold_slab(running, slab_stack, 0)
    if grid_f > 1:
        for off_frame in (-1, 1):
            got_slab = passed_along(
                shortened(slab_stack), "tile", -off_frame * grid_h * grid_w * group_count
            ).astype(slab_stack.dtype)
            running = fold_slab(running, got_slab, off_frame)
    row_top, row_total, summed = running
    result = summed / row_total[:, :, None]
    result = jnp.transpose(result, (1, 0, 2)).reshape(tokens, lane_width)
    return result.astype(jnp.bfloat16)[None]


def solution(mesh):
    return jax.shard_map(
        shards,
        mesh=mesh,
        in_specs=(
            P(("req", "tile"), None, None),
            P(("req", "tile"), None, None),
            P(("req", "tile"), None, None),
            P(("req", "tile"), None),
            P(("req", "tile"), None),
            P(("req", "tile")),
        ),
        out_specs=P(("req", "tile"), None, None),
        check_vma=False,
    )
```

```python
import functools
import math

import jax
import jax.numpy as jnp
from jax import lax
from jax.experimental import pallas as pl
from jax.experimental.pallas import tpu as pltpu
from jax.sharding import PartitionSpec as P

TS = 8
HEAD_DIM = 128
HEAD_GROUPS = 4


MASKED = -1e30
EXP2_SCALE = math.log2(math.e) / math.sqrt(HEAD_DIM)


def passed_along(value, axis, steps):
    count = lax.axis_size(axis)
    first, last = (max(0, -steps), min(count, count - steps))
    return lax.ppermute(value, axis, [(source, source + steps) for source in range(first, last)])


def shortened(value):
    return jax.tree.map(lambda a: a.astype(jnp.bfloat16) if a.dtype == jnp.float32 else a, value)


def fold_block(running, query_heads, key_block, value_block, key_keep):
    row_top, row_total, summed = running
    head_count = query_heads.shape[1]
    key_heads = key_block.reshape(key_block.shape[0], head_count, HEAD_DIM)
    value_heads = value_block.reshape(value_block.shape[0], head_count, HEAD_DIM)
    scores = jnp.einsum("qhd,khd->hqk", query_heads, key_heads, preferred_element_type=jnp.float32)
    scores = scores * (1.0 / math.sqrt(HEAD_DIM))
    scores = jnp.where(key_keep[None, None, :], scores, MASKED)
    new_top = jnp.maximum(row_top, jnp.max(scores, axis=-1))
    scale_down = jnp.exp(row_top - new_top)
    exp_terms = jnp.where(key_keep[None, None, :], jnp.exp(scores - new_top[:, :, None]), 0.0)
    row_total = row_total * scale_down + jnp.sum(exp_terms, axis=-1)
    weights = exp_terms.astype(jnp.bfloat16)
    summed = summed * scale_down[:, :, None] + jnp.einsum(
        "hqk,khd->hqd", weights, value_heads, preferred_element_type=jnp.float32
    )
    return (new_top, row_total, summed)


def window_kernel(blocks, carry_in, finish, q_ref, *refs):
    block_count = len(blocks)
    source_refs = refs[:block_count]
    keep_refs = refs[block_count : 2 * block_count]
    rest = refs[2 * block_count :]
    lane_width, tokens = q_ref.shape
    head_count = lane_width // HEAD_DIM
    keeps = [
        jnp.broadcast_to(keep_refs[b][...], (keep_refs[b].shape[0], tokens)) > 0.5 for b in range(block_count)
    ]
    for h in range(head_count):
        lanes = slice(h * HEAD_DIM, (h + 1) * HEAD_DIM)
        query_t = q_ref[lanes, :]
        scores, value_tiles = [], []
        for b, (pair_form, key_at, value_at) in enumerate(blocks):
            if pair_form:
                key_tile = source_refs[b][key_at, :, lanes]
                value_tile = source_refs[b][value_at, :, lanes]
            else:
                key_tile = source_refs[b][:, (key_at + h) * HEAD_DIM : (key_at + h + 1) * HEAD_DIM]
                value_tile = source_refs[b][:, (value_at + h) * HEAD_DIM : (value_at + h + 1) * HEAD_DIM]
            s = jnp.dot(key_tile, query_t, preferred_element_type=jnp.float32)
            scores.append(jnp.where(keeps[b], s, MASKED))
            value_tiles.append(value_tile)
        top = scores[0].max(axis=0, keepdims=True)
        for s in scores[1:]:
            top = jnp.maximum(top, s.max(axis=0, keepdims=True))
        if carry_in:
            top_in = rest[0][h : h + 1, :]
            top = jnp.maximum(top, top_in)
            scale_down = jnp.exp2((top_in - top) * EXP2_SCALE)
            total = rest[0][head_count + h : head_count + h + 1, :] * scale_down
            summed = rest[1][lanes, :] * scale_down
        else:
            total = jnp.zeros_like(top)
            summed = None
        for b in range(block_count):
            terms = jnp.exp2((scores[b] - top) * EXP2_SCALE)
            total = total + terms.sum(axis=0, keepdims=True)
            part = lax.dot_general(
                value_tiles[b],
                terms.astype(jnp.bfloat16),
                (((0,), (0,)), ((), ())),
                preferred_element_type=jnp.float32,
            )
            summed = part if summed is None else summed + part
        outs = rest[2:] if carry_in else rest
        if finish:
            outs[0][:, lanes] = jnp.transpose(summed / total).astype(outs[0].dtype)
        else:
            outs[0][h : h + 1, :] = top
            outs[0][head_count + h : head_count + h + 1, :] = total
            outs[1][lanes, :] = summed


def window_attention(query_t, blocks, carry=None, finish=True):
    lane_width, tokens = query_t.shape
    head_count = lane_width // HEAD_DIM
    layout, sources, keeps = [], [], []
    key_total = 0
    for source, key_at, value_at, keep in blocks:
        key_total += keep.shape[0]
        layout.append((source.ndim == 3, key_at, value_at))
        sources.append(source)
        keeps.append(keep)
    stat_rows = -(-2 * head_count // 8) * 8
    stat_shape = jax.ShapeDtypeStruct((stat_rows, tokens), jnp.float32)
    if finish:
        out_shape = jax.ShapeDtypeStruct((tokens, lane_width), jnp.bfloat16)
        out_specs = pl.BlockSpec(memory_space=pltpu.VMEM)
    else:
        out_shape = (
            pltpu.VMEM(stat_shape.shape, stat_shape.dtype),
            pltpu.VMEM((lane_width, tokens), jnp.float32),
        )
        out_specs = tuple(pl.BlockSpec(memory_space=pltpu.VMEM) for _ in range(2))
    carry_args = () if carry is None else tuple(carry)
    operand_count = 1 + 2 * len(blocks) + len(carry_args)
    flops = 4 * tokens * key_total * lane_width
    moved = 2 * (2 * tokens * lane_width + 2 * key_total * lane_width) + 4 * 2 * tokens * (lane_width + 8)
    return pl.pallas_call(
        functools.partial(window_kernel, tuple(layout), carry is not None, finish),
        out_shape=out_shape,
        in_specs=[pl.BlockSpec(memory_space=pltpu.VMEM)] * operand_count,
        out_specs=out_specs,
        cost_estimate=pl.CostEstimate(
            flops=flops, transcendentals=tokens * key_total * head_count, bytes_accessed=moved
        ),
        compiler_params=pltpu.CompilerParams(vmem_limit_bytes=16 * 1024 * 1024),
    )(*[pltpu.with_memory_space_constraint(a, pltpu.VMEM) for a in (query_t, *sources, *keeps, *carry_args)])


def payload_kernel(group_count, lane_width, mask_ref, key_ref, value_ref, out_ref):
    rows = key_ref.shape[0]
    row_at = lax.broadcasted_iota(jnp.int32, (rows, 128), 0)
    flags = jnp.zeros((rows, 128), jnp.float32)
    for r in range(rows):
        flags = jnp.where(row_at == r, mask_ref[r].astype(jnp.float32), flags)
    flags = flags.astype(out_ref.dtype)
    for j in range(out_ref.shape[0]):
        g = j % group_count
        out_ref[j, :, :lane_width] = key_ref[:, g * lane_width : (g + 1) * lane_width]
        out_ref[j, :, lane_width : 2 * lane_width] = value_ref[:, g * lane_width : (g + 1) * lane_width]
        out_ref[j, :, 2 * lane_width :] = flags


def text_pieces(text_keys, text_values, text_mask, group_count, lane_width):
    count = lax.axis_size("tile")
    rows = text_keys.shape[0]
    width = 2 * lane_width + 128
    outgoing = pl.pallas_call(
        functools.partial(payload_kernel, group_count, lane_width),
        out_shape=pltpu.VMEM((count, rows, width), jnp.bfloat16),
        in_specs=[
            pl.BlockSpec(memory_space=pltpu.SMEM),
            pl.BlockSpec(memory_space=pltpu.VMEM),
            pl.BlockSpec(memory_space=pltpu.VMEM),
        ],
        out_specs=pl.BlockSpec(memory_space=pltpu.VMEM),
    )(text_mask, text_keys, text_values).reshape(count * rows, width)
    got = lax.all_to_all(outgoing, "tile", 0, 0, tiled=True)
    return got, got[:, 2 * lane_width] > 0.5


def shards(queries, keys, values, text_keys, text_values, text_mask):
    tokens = queries.shape[1]
    lane_width = queries.shape[2]
    head_count = lane_width // HEAD_DIM
    query_heads = queries[0].reshape(tokens, head_count, HEAD_DIM)
    group_count = HEAD_GROUPS
    tiles_all = lax.axis_size("tile") // group_count
    grid_w = min(4, tiles_all)
    grid_h = min(4, tiles_all // grid_w)
    grid_f = tiles_all // (grid_w * grid_h)
    frames_valid = grid_f * TS - TS // 4
    my_index = lax.axis_index("tile")
    tile_id = my_index // group_count
    head_group = my_index % group_count
    w_pos = tile_id % grid_w
    h_pos = tile_id // grid_w % grid_h
    f_pos = tile_id // (grid_w * grid_h)
    key_rows = tokens
    if grid_f == 1:
        key_rows = min(tokens, frames_valid * TS * TS)
    own_pair = jnp.stack([keys[0, :key_rows], values[0, :key_rows]])
    local_frame = jnp.arange(key_rows, dtype=jnp.int32) // (TS * TS)

    def keep_mask(off_frame, off_height, off_width):
        inside = (
            (f_pos + off_frame >= 0)
            & (f_pos + off_frame < grid_f)
            & (h_pos + off_height >= 0)
            & (h_pos + off_height < grid_h)
            & (w_pos + off_width >= 0)
            & (w_pos + off_width < grid_w)
        )
        return inside & ((f_pos + off_frame) * TS + local_frame < frames_valid)

    running = (
        jnp.full((head_count, tokens), MASKED, jnp.float32),
        jnp.zeros((head_count, tokens), jnp.float32),
        jnp.zeros((head_count, tokens, HEAD_DIM), jnp.float32),
    )
    text_got, text_keep = text_pieces(text_keys, text_values, text_mask, group_count, lane_width)
    width_set = {0: own_pair}
    for off_width in (-1, 1):
        width_set[off_width] = passed_along(own_pair, "tile", -off_width * group_count)
    if grid_h == 1 and grid_f == 1:
        as_row = lambda keep: keep.astype(jnp.float32)[:, None]
        query_t = jnp.transpose(queries[0])
        carry = window_attention(query_t, [(own_pair, 0, 1, as_row(keep_mask(0, 0, 0)))], finish=False)
        carry = window_attention(
            query_t, [(text_got, 0, head_count, as_row(text_keep))], carry=carry, finish=False
        )
        blocks = [(width_set[-1], 0, 1, as_row(keep_mask(0, 0, -1)))]
        carry = window_attention(query_t, blocks, carry=carry, finish=False)
        blocks = [(width_set[1], 0, 1, as_row(keep_mask(0, 0, 1)))]
        return window_attention(query_t, blocks, carry=carry)[None]
    piece_keys = text_got[:, :lane_width]
    piece_values = text_got[:, lane_width : 2 * lane_width]
    running = fold_block(running, query_heads, piece_keys, piece_values, text_keep)
    running = fold_block(running, query_heads, own_pair[0], own_pair[1], keep_mask(0, 0, 0))
    width_offsets = sorted(width_set)
    row_stack = jnp.stack([width_set[spot] for spot in width_offsets])
    height_set = {0: row_stack}
    if grid_h > 1:
        for off_height in (-1, 1):
            height_set[off_height] = passed_along(
                shortened(row_stack), "tile", -off_height * grid_w * group_count
            ).astype(row_stack.dtype)
    height_offsets = sorted(height_set)
    slab_stack = jnp.stack([height_set[spot] for spot in height_offsets])

    def fold_slab(state_now, slab_pairs, off_frame):
        for h_slot, off_height in enumerate(height_offsets):
            for w_slot, off_width in enumerate(width_offsets):
                if off_frame == 0 and off_height == 0 and (off_width == 0):
                    continue
                state_now = fold_block(
                    state_now,
                    query_heads,
                    slab_pairs[h_slot, w_slot, 0],
                    slab_pairs[h_slot, w_slot, 1],
                    keep_mask(off_frame, off_height, off_width),
                )
        return state_now

    running = fold_slab(running, slab_stack, 0)
    if grid_f > 1:
        for off_frame in (-1, 1):
            got_slab = passed_along(
                shortened(slab_stack), "tile", -off_frame * grid_h * grid_w * group_count
            ).astype(slab_stack.dtype)
            running = fold_slab(running, got_slab, off_frame)
    row_top, row_total, summed = running
    result = summed / row_total[:, :, None]
    result = jnp.transpose(result, (1, 0, 2)).reshape(tokens, lane_width)
    return result.astype(jnp.bfloat16)[None]


def solution(mesh):
    return jax.shard_map(
        shards,
        mesh=mesh,
        in_specs=(
            P(("req", "tile"), None, None),
            P(("req", "tile"), None, None),
            P(("req", "tile"), None, None),
            P(("req", "tile"), None),
            P(("req", "tile"), None),
            P(("req", "tile")),
        ),
        out_specs=P(("req", "tile"), None, None),
        check_vma=False,
    )
```

```python
import functools
import math

import jax
import jax.numpy as jnp
from jax import lax
from jax.experimental import pallas as pl
from jax.experimental.pallas import tpu as pltpu
from jax.sharding import PartitionSpec as P

TS = 8
HEAD_DIM = 128
HEAD_GROUPS = 4


MASKED = -1e30
EXP2_SCALE = math.log2(math.e) / math.sqrt(HEAD_DIM)


def passed_along(value, axis, steps):
    count = lax.axis_size(axis)
    first, last = (max(0, -steps), min(count, count - steps))
    return lax.ppermute(value, axis, [(source, source + steps) for source in range(first, last)])


def shortened(value):
    return jax.tree.map(lambda a: a.astype(jnp.bfloat16) if a.dtype == jnp.float32 else a, value)


def fold_block(running, query_heads, key_block, value_block, key_keep):
    row_top, row_total, summed = running
    head_count = query_heads.shape[1]
    key_heads = key_block.reshape(key_block.shape[0], head_count, HEAD_DIM)
    value_heads = value_block.reshape(value_block.shape[0], head_count, HEAD_DIM)
    scores = jnp.einsum("qhd,khd->hqk", query_heads, key_heads, preferred_element_type=jnp.float32)
    scores = scores * (1.0 / math.sqrt(HEAD_DIM))
    scores = jnp.where(key_keep[None, None, :], scores, MASKED)
    new_top = jnp.maximum(row_top, jnp.max(scores, axis=-1))
    scale_down = jnp.exp(row_top - new_top)
    exp_terms = jnp.where(key_keep[None, None, :], jnp.exp(scores - new_top[:, :, None]), 0.0)
    row_total = row_total * scale_down + jnp.sum(exp_terms, axis=-1)
    weights = exp_terms.astype(jnp.bfloat16)
    summed = summed * scale_down[:, :, None] + jnp.einsum(
        "hqk,khd->hqd", weights, value_heads, preferred_element_type=jnp.float32
    )
    return (new_top, row_total, summed)


def window_kernel(blocks, carry_in, finish, q_ref, *refs):
    block_count = len(blocks)
    source_refs = refs[:block_count]
    keep_refs = refs[block_count : 2 * block_count]
    rest = refs[2 * block_count :]
    lane_width, tokens = q_ref.shape
    head_count = lane_width // HEAD_DIM
    keeps = [
        jnp.broadcast_to(keep_refs[b][...], (keep_refs[b].shape[0], tokens)) > 0.5 for b in range(block_count)
    ]
    for h in range(head_count):
        lanes = slice(h * HEAD_DIM, (h + 1) * HEAD_DIM)
        query_t = q_ref[lanes, :]
        scores, value_tiles = [], []
        for b, (pair_form, key_at, value_at) in enumerate(blocks):
            if pair_form:
                key_tile = source_refs[b][key_at, :, lanes]
                value_tile = source_refs[b][value_at, :, lanes]
            else:
                key_tile = source_refs[b][:, (key_at + h) * HEAD_DIM : (key_at + h + 1) * HEAD_DIM]
                value_tile = source_refs[b][:, (value_at + h) * HEAD_DIM : (value_at + h + 1) * HEAD_DIM]
            s = jnp.dot(key_tile, query_t, preferred_element_type=jnp.float32)
            scores.append(jnp.where(keeps[b], s, MASKED))
            value_tiles.append(value_tile)
        top = scores[0].max(axis=0, keepdims=True)
        for s in scores[1:]:
            top = jnp.maximum(top, s.max(axis=0, keepdims=True))
        if carry_in:
            top_in = rest[0][h : h + 1, :]
            top = jnp.maximum(top, top_in)
            scale_down = jnp.exp2((top_in - top) * EXP2_SCALE)
            total = rest[0][head_count + h : head_count + h + 1, :] * scale_down
            summed = rest[1][lanes, :] * scale_down
        else:
            total = jnp.zeros_like(top)
            summed = None
        for b in range(block_count):
            terms = jnp.exp2((scores[b] - top) * EXP2_SCALE)
            total = total + terms.sum(axis=0, keepdims=True)
            part = lax.dot_general(
                value_tiles[b],
                terms.astype(jnp.bfloat16),
                (((0,), (0,)), ((), ())),
                preferred_element_type=jnp.float32,
            )
            summed = part if summed is None else summed + part
        outs = rest[2:] if carry_in else rest
        if finish:
            outs[0][:, lanes] = jnp.transpose(summed / total).astype(outs[0].dtype)
        else:
            outs[0][h : h + 1, :] = top
            outs[0][head_count + h : head_count + h + 1, :] = total
            outs[1][lanes, :] = summed


def window_attention(query_t, blocks, carry=None, finish=True):
    lane_width, tokens = query_t.shape
    head_count = lane_width // HEAD_DIM
    layout, sources, keeps = [], [], []
    key_total = 0
    for source, key_at, value_at, keep in blocks:
        key_total += keep.shape[0]
        layout.append((source.ndim == 3, key_at, value_at))
        sources.append(source)
        keeps.append(keep)
    stat_rows = -(-2 * head_count // 8) * 8
    stat_shape = jax.ShapeDtypeStruct((stat_rows, tokens), jnp.float32)
    if finish:
        out_shape = jax.ShapeDtypeStruct((tokens, lane_width), jnp.bfloat16)
        out_specs = pl.BlockSpec(memory_space=pltpu.VMEM)
    else:
        out_shape = (
            pltpu.VMEM(stat_shape.shape, stat_shape.dtype),
            pltpu.VMEM((lane_width, tokens), jnp.float32),
        )
        out_specs = tuple(pl.BlockSpec(memory_space=pltpu.VMEM) for _ in range(2))
    carry_args = () if carry is None else tuple(carry)
    operand_count = 1 + 2 * len(blocks) + len(carry_args)
    flops = 4 * tokens * key_total * lane_width
    moved = 2 * (2 * tokens * lane_width + 2 * key_total * lane_width) + 4 * 2 * tokens * (lane_width + 8)
    return pl.pallas_call(
        functools.partial(window_kernel, tuple(layout), carry is not None, finish),
        out_shape=out_shape,
        in_specs=[pl.BlockSpec(memory_space=pltpu.VMEM)] * operand_count,
        out_specs=out_specs,
        cost_estimate=pl.CostEstimate(
            flops=flops, transcendentals=tokens * key_total * head_count, bytes_accessed=moved
        ),
        compiler_params=pltpu.CompilerParams(vmem_limit_bytes=16 * 1024 * 1024),
    )(*[pltpu.with_memory_space_constraint(a, pltpu.VMEM) for a in (query_t, *sources, *keeps, *carry_args)])


def payload_kernel(group_count, lane_width, mask_ref, key_ref, value_ref, *refs):
    if len(refs) == 4:
        own_keys, own_values, out_ref, pair_ref = refs
        pair_ref[0] = own_keys[: pair_ref.shape[1], :]
        pair_ref[1] = own_values[: pair_ref.shape[1], :]
    else:
        (out_ref,) = refs
    rows = key_ref.shape[0]
    row_at = lax.broadcasted_iota(jnp.int32, (rows, 128), 0)
    flags = jnp.zeros((rows, 128), jnp.float32)
    for r in range(rows):
        flags = jnp.where(row_at == r, mask_ref[r].astype(jnp.float32), flags)
    flags = flags.astype(out_ref.dtype)
    for j in range(out_ref.shape[0]):
        g = j % group_count
        out_ref[j, :, :lane_width] = key_ref[:, g * lane_width : (g + 1) * lane_width]
        out_ref[j, :, lane_width : 2 * lane_width] = value_ref[:, g * lane_width : (g + 1) * lane_width]
        out_ref[j, :, 2 * lane_width :] = flags


def text_pieces(text_keys, text_values, text_mask, group_count, lane_width, own=None):
    count = lax.axis_size("tile")
    rows = text_keys.shape[0]
    width = 2 * lane_width + 128
    vmem = pl.BlockSpec(memory_space=pltpu.VMEM)
    out_shape = pltpu.VMEM((count, rows, width), jnp.bfloat16)
    extra = ()
    if own is not None:
        own_keys, own_values, key_rows = own
        extra = (own_keys, own_values)
        out_shape = (out_shape, pltpu.VMEM((2, key_rows, own_keys.shape[1]), own_keys.dtype))
    made = pl.pallas_call(
        functools.partial(payload_kernel, group_count, lane_width),
        out_shape=out_shape,
        in_specs=[pl.BlockSpec(memory_space=pltpu.SMEM)] + [vmem] * (2 + len(extra)),
        out_specs=vmem if own is None else (vmem, vmem),
    )(text_mask, text_keys, text_values, *extra)
    own_pair = None
    if own is not None:
        made, own_pair = made
    outgoing = made.reshape(count * rows, width)
    got = lax.all_to_all(outgoing, "tile", 0, 0, tiled=True)
    if own is not None:
        return got, got[:, 2 * lane_width] > 0.5, own_pair
    return got, got[:, 2 * lane_width] > 0.5


def shards(queries, keys, values, text_keys, text_values, text_mask):
    tokens = queries.shape[1]
    lane_width = queries.shape[2]
    head_count = lane_width // HEAD_DIM
    query_heads = queries[0].reshape(tokens, head_count, HEAD_DIM)
    group_count = HEAD_GROUPS
    tiles_all = lax.axis_size("tile") // group_count
    grid_w = min(4, tiles_all)
    grid_h = min(4, tiles_all // grid_w)
    grid_f = tiles_all // (grid_w * grid_h)
    frames_valid = grid_f * TS - TS // 4
    my_index = lax.axis_index("tile")
    tile_id = my_index // group_count
    head_group = my_index % group_count
    w_pos = tile_id % grid_w
    h_pos = tile_id // grid_w % grid_h
    f_pos = tile_id // (grid_w * grid_h)
    key_rows = tokens
    if grid_f == 1:
        key_rows = min(tokens, frames_valid * TS * TS)
    own_pair = jnp.stack([keys[0, :key_rows], values[0, :key_rows]])
    local_frame = jnp.arange(key_rows, dtype=jnp.int32) // (TS * TS)

    def keep_mask(off_frame, off_height, off_width):
        inside = (
            (f_pos + off_frame >= 0)
            & (f_pos + off_frame < grid_f)
            & (h_pos + off_height >= 0)
            & (h_pos + off_height < grid_h)
            & (w_pos + off_width >= 0)
            & (w_pos + off_width < grid_w)
        )
        return inside & ((f_pos + off_frame) * TS + local_frame < frames_valid)

    running = (
        jnp.full((head_count, tokens), MASKED, jnp.float32),
        jnp.zeros((head_count, tokens), jnp.float32),
        jnp.zeros((head_count, tokens, HEAD_DIM), jnp.float32),
    )
    if grid_h == 1 and grid_f == 1:
        text_got, text_keep, own_pair = text_pieces(
            text_keys, text_values, text_mask, group_count, lane_width, (keys[0], values[0], key_rows)
        )
    else:
        text_got, text_keep = text_pieces(text_keys, text_values, text_mask, group_count, lane_width)
    width_set = {0: own_pair}
    for off_width in (-1, 1):
        width_set[off_width] = passed_along(own_pair, "tile", -off_width * group_count)
    if grid_h == 1 and grid_f == 1:
        as_row = lambda keep: keep.astype(jnp.float32)[:, None]
        query_t = jnp.transpose(queries[0])
        carry = window_attention(query_t, [(own_pair, 0, 1, as_row(keep_mask(0, 0, 0)))], finish=False)
        carry = window_attention(
            query_t, [(text_got, 0, head_count, as_row(text_keep))], carry=carry, finish=False
        )
        blocks = [(width_set[-1], 0, 1, as_row(keep_mask(0, 0, -1)))]
        carry = window_attention(query_t, blocks, carry=carry, finish=False)
        blocks = [(width_set[1], 0, 1, as_row(keep_mask(0, 0, 1)))]
        return window_attention(query_t, blocks, carry=carry)[None]
    piece_keys = text_got[:, :lane_width]
    piece_values = text_got[:, lane_width : 2 * lane_width]
    running = fold_block(running, query_heads, piece_keys, piece_values, text_keep)
    running = fold_block(running, query_heads, own_pair[0], own_pair[1], keep_mask(0, 0, 0))
    width_offsets = sorted(width_set)
    row_stack = jnp.stack([width_set[spot] for spot in width_offsets])
    height_set = {0: row_stack}
    if grid_h > 1:
        for off_height in (-1, 1):
            height_set[off_height] = passed_along(
                shortened(row_stack), "tile", -off_height * grid_w * group_count
            ).astype(row_stack.dtype)
    height_offsets = sorted(height_set)
    slab_stack = jnp.stack([height_set[spot] for spot in height_offsets])

    def fold_slab(state_now, slab_pairs, off_frame):
        for h_slot, off_height in enumerate(height_offsets):
            for w_slot, off_width in enumerate(width_offsets):
                if off_frame == 0 and off_height == 0 and (off_width == 0):
                    continue
                state_now = fold_block(
                    state_now,
                    query_heads,
                    slab_pairs[h_slot, w_slot, 0],
                    slab_pairs[h_slot, w_slot, 1],
                    keep_mask(off_frame, off_height, off_width),
                )
        return state_now

    running = fold_slab(running, slab_stack, 0)
    if grid_f > 1:
        for off_frame in (-1, 1):
            got_slab = passed_along(
                shortened(slab_stack), "tile", -off_frame * grid_h * grid_w * group_count
            ).astype(slab_stack.dtype)
            running = fold_slab(running, got_slab, off_frame)
    row_top, row_total, summed = running
    result = summed / row_total[:, :, None]
    result = jnp.transpose(result, (1, 0, 2)).reshape(tokens, lane_width)
    return result.astype(jnp.bfloat16)[None]


def solution(mesh):
    return jax.shard_map(
        shards,
        mesh=mesh,
        in_specs=(
            P(("req", "tile"), None, None),
            P(("req", "tile"), None, None),
            P(("req", "tile"), None, None),
            P(("req", "tile"), None),
            P(("req", "tile"), None),
            P(("req", "tile")),
        ),
        out_specs=P(("req", "tile"), None, None),
        check_vma=False,
    )
```
